32 devices in a mesh: grp: 2 (over y), chan: 4 (over z), tmpl: 4 (over x, core).
Axes of the slice: x: 2, y: 2, z: 4, core: 2. Of those that a mesh axis runs over, the one named last changes fastest.
Arguments:
- data: bfloat16 [1024, 1664], P(('grp', 'chan', 'tmpl')), parts along dimension 0, may hold values from -600 to 600
- templates: bfloat16 [256, 128, 512], P(('grp', 'chan'), 'tmpl'), parts along dimension 0, may hold values from -6 to 6
- stations: int32 [256, 128], P(('grp', 'chan'), 'tmpl'), parts along dimension 0, may hold values from 0 to 511, as said below
- offsets: int32 [256, 128], P(('grp', 'chan'), 'tmpl'), parts along dimension 0, may hold values from 0 to 128
- owner_map: int32 [8, 32], P(('grp', 'chan')), parts along dimension 0, may hold values from 0 to 31, each once within a row
Outputs:
- detection: float32 [256, 1024], P(('grp', 'chan', 'tmpl')), parts along dimension 0
The draws below stay inside these ranges and needn't reach their ends.
There are 2 independent parts, one for each index of `grp`. The reference program is written for one: setup_inputs(seed, part) draws one part's arguments, and reference() takes and returns one part's arrays. A program takes and returns all parts, laid end to end along the dimension named above; each array names one. Nothing has to cross between parts.
Inputs may be any that keep to these rules, and one draw needn't show every extreme that they name: For each template j there is a sub-array g_j such that entries t * 32 to (t + 1) * 32 - 1 of stations[j] are the channels (g_j * 4 + t) * 32 + i, i < 32, each once, in some order. Among the 32 templates of one home block (rows h * 32 to (h + 1) * 32 - 1) at most 16 share a sub-array; in every draw one sub-array is named by exactly 16 templates of every home block.
All inputs are finite; a program needn't handle non-finite values.
Results may differ from the reference program's by a relative error of at most 0.0085.
Values may be sent and summed in bfloat16 or wider, within the bound.
No kernel may reach another device: no remote copies, remote signals or barrier semaphores. Data moves between devices by JAX's collectives and lax.ppermute only.
A program may use at most 64 MiB of HBM per device.

```python
import math
import jax
import jax.numpy as jnp
from jax import lax

CH_DEV = 32
NL = 1024
NTC = 32
L = 512
OFF = 128
LP = 640
W = 1664
SUBARRAYS = 4
K = 128
CH = 512
NT = 128
TEMPLATE_LIMIT = 16
N_TMPL = 4


def draw_data(key, part):
    k_noise, k_scale, k_env = jax.random.split(key, 3)
    chan_scale = jnp.exp(jax.random.uniform(k_scale, (CH, 1), minval=0.0, maxval=math.log(10.0)))
    nblocks = (W + 127) // 128
    envelope = jnp.exp(jax.random.uniform(k_env, (nblocks,), minval=0.0, maxval=math.log(10.0)))
    envelope = jnp.repeat(envelope, 128)[:W]
    noise_trace = jax.random.normal(k_noise, (CH, W))
    values = jnp.clip(noise_trace * chan_scale * envelope[None, :], -600.0, 600.0)
    return values.astype(jnp.float32).astype(jnp.bfloat16)


def dest_blocks(key):
    sender_blocks = NT // NTC
    slot_total = sender_blocks * TEMPLATE_LIMIT
    busy_subarray = jax.random.randint(jax.random.fold_in(key, 7), (), 0, sender_blocks)

    def sender(index):
        sender_rngkey = jax.random.fold_in(key, 100 + index)
        slot_entries = jnp.arange(slot_total, dtype=jnp.int32)
        slot_target = slot_entries // TEMPLATE_LIMIT
        noise_trace = jax.random.randint(sender_rngkey, (slot_total,), 0, 2 ** 20)
        detect_score = jnp.where(slot_target == busy_subarray, 0, noise_trace + 1) * slot_total + slot_entries
        chosen = slot_target[jnp.argsort(detect_score)[:NTC]]
        mixing = jax.random.randint(jax.random.fold_in(sender_rngkey, 1), (NTC,), 0, 2 ** 20)
        mixing = mixing * NTC + jnp.arange(NTC, dtype=jnp.int32)
        return chosen[jnp.argsort(mixing)]
    return jax.vmap(sender)(jnp.arange(sender_blocks, dtype=jnp.int32))


def draw_stations(key, part):
    tmpl_count = K // CH_DEV
    dest = dest_blocks(jax.random.fold_in(key, 11)).reshape(NT)
    scores = jax.random.randint(jax.random.fold_in(key, 13), (NT, tmpl_count, CH_DEV), 0, 2 ** 20)
    scores = scores * CH_DEV + jnp.arange(CH_DEV, dtype=jnp.int32)
    inner = jnp.argsort(scores, axis=-1).astype(jnp.int32)
    block = dest[:, None] * tmpl_count + jnp.arange(tmpl_count, dtype=jnp.int32)[None, :]
    return (block[:, :, None] * CH_DEV + inner).reshape(NT, K).astype(jnp.int32)


def set_ends(drawn, rng, smallest, top_value):
    longest = drawn.shape.index(max(drawn.shape))
    spots = []
    for shift in (0, 1):
        where = [jax.random.randint(jax.random.fold_in(rng, axis), (), 0, length) for axis, length in enumerate(drawn.shape)]
        where[longest] = (where[longest] + shift) % drawn.shape[longest]
        spots.append(tuple(where))
    return drawn.at[spots[0]].set(smallest).at[spots[1]].set(top_value)


def block_scale(key, shape, cuts, low, largest):
    loudness = 1.0
    for position, blocks in cuts:
        draws = jax.random.uniform(jax.random.fold_in(jax.random.fold_in(key, 6), position), (blocks,), jnp.float32, low / len(cuts), largest / len(cuts))
        loudness = loudness * jnp.repeat(jnp.exp(draws), shape[position] // blocks).reshape((-1,) + (1,) * (len(shape) - 1 - position))
    return loudness


def scatter_about(own_key, extent, scale, reach, cuts=(), held_as=jnp.bfloat16):
    values = jax.random.normal(own_key, extent, jnp.float32) * scale
    if len(cuts) > 0:
        values = block_scale(own_key, extent, cuts, -0.22, 0.18) * values
    return jnp.clip(values, min=-reach, max=reach).astype(held_as)


def setup_inputs(seed: int = 0, part: int = 0) -> dict:
    key_of = jax.random.split(jax.random.key(seed), 6)
    part_splits = jax.random.split(jax.random.fold_in(key_of[5], part), 6)
    data = draw_data(jax.random.fold_in(jax.random.fold_in(key_of[5], part), 71), part)
    templates = scatter_about(part_splits[1], (NT, K, L), 1.0, 6.0, ((0, 4), (1, 4)))
    stations = draw_stations(jax.random.fold_in(jax.random.fold_in(key_of[5], part), 71), part)
    offsets = set_ends(jax.random.randint(part_splits[3], (NT, K), 0, OFF + 1), jax.random.fold_in(part_splits[3], 1), 0, OFF).astype(jnp.int32)
    owner_map = jax.vmap(lambda own: jax.random.permutation(own, NTC))(jax.random.split(part_splits[4], SUBARRAYS)).reshape((SUBARRAYS, NTC)).astype(jnp.int32)
    return dict(data=data, templates=templates, stations=stations, offsets=offsets, owner_map=owner_map)


eps = 1e-05

def normalize_rows(values):
    values = values.astype(jnp.float32)
    centred = values - lax.optimization_barrier(jnp.mean(values, axis=-1, keepdims=True))
    scale = lax.rsqrt(lax.optimization_barrier(jnp.mean(centred * centred, axis=-1, keepdims=True)) + eps)
    return (centred * scale).astype(jnp.bfloat16)

def place_row(row, shift):
    return lax.dynamic_update_slice(jnp.zeros((LP,), jnp.float32), row, (shift.astype(jnp.int32),))

def reference(data, templates, stations, offsets, owner_map):
    signal = normalize_rows(data).astype(jnp.float32)
    shaped = normalize_rows(templates)
    spectra = jnp.fft.rfft(signal, n=W, axis=-1)

    def single(items):
        rows, chans, shifts = items
        placed = jax.vmap(place_row)(rows.astype(jnp.float32), shifts)
        filt = jnp.fft.rfft(placed, n=W, axis=-1)
        product = jnp.conj(filt) * spectra[chans]
        grouped = lax.optimization_barrier(jnp.sum(product.reshape(N_TMPL, CH_DEV, product.shape[-1]), axis=1))
        corr = jnp.fft.irfft(grouped, n=W, axis=-1)[:, :NL]
        rounded = lax.optimization_barrier(corr.astype(jnp.bfloat16)).astype(jnp.float32)
        return lax.optimization_barrier(jnp.sum(rounded, axis=0))
    stack = lax.map(single, (shaped, stations, offsets))
    stack = stack.reshape(SUBARRAYS, NTC, NL)
    blocks = jnp.arange(SUBARRAYS, dtype=jnp.int32)[:, None]
    placed = jnp.zeros_like(stack).at[blocks, owner_map].set(stack)
    flat = placed.reshape(SUBARRAYS * NTC, NL)
    return flat * lax.rsqrt(lax.optimization_barrier(jnp.mean(flat * flat, axis=1, keepdims=True)) + eps)
```

```python
import jax
import jax.numpy as jnp
from jax import lax
from jax.sharding import PartitionSpec as P

OFF = 128
PHASES = 8


eps = 1e-05


def normalize_rows(values):
    values = values.astype(jnp.float32)
    centred = values - jnp.mean(values, axis=-1, keepdims=True)
    scale = lax.rsqrt(jnp.mean(centred * centred, axis=-1, keepdims=True) + eps)
    return (centred * scale).astype(jnp.bfloat16)


def place_moveout(rows, shifts, padded_len):
    extra = padded_len - rows.shape[-1]
    tail = jnp.zeros(rows.shape[:-1] + (extra,), rows.dtype)
    current = jnp.concatenate([rows, tail], axis=-1)
    for bit_number in range(OFF.bit_length()):
        step_len = 1 << bit_number
        lead = jnp.zeros(rows.shape[:-1] + (step_len,), rows.dtype)
        moved = jnp.concatenate([lead, current[..., : padded_len - step_len]], axis=-1)
        active = shifts >> bit_number & 1 == 1
        current = jnp.where(active[..., None], moved, current)
    return current


def polyphase_filters(placed, phases):
    count, chans, padded_len = placed.shape
    taps = padded_len // phases + 1
    span = taps * phases
    padded = jnp.pad(placed, ((0, 0), (0, 0), (phases - 1, span - padded_len)))
    shifted = jnp.stack(
        [padded[:, :, phases - 1 - e : phases - 1 - e + span] for e in range(phases)], axis=1
    )
    shifted = shifted.reshape(count, phases, chans, taps, phases)
    shifted = jnp.transpose(shifted, (0, 1, 2, 4, 3))
    return shifted.reshape(count * phases, chans * phases, taps)


def polyphase_signal(blocks, phases):
    n_blocks, chans, window = blocks.shape
    split = blocks.reshape(n_blocks, chans, window // phases, phases)
    split = jnp.transpose(split, (0, 1, 3, 2))
    return split.reshape(n_blocks, chans * phases, window // phases)


def shards(data, templates, stations, offsets, owner_map):
    n_tmpl = lax.axis_size("tmpl")
    ch_local = data.shape[0]
    window = data.shape[1]
    count = templates.shape[0]
    padded_len = templates.shape[2] + OFF
    lags = window - padded_len
    phases = PHASES
    signal = normalize_rows(data)
    blocks = lax.all_gather(signal, "chan", axis=0, tiled=False)
    n_blocks = blocks.shape[0]
    shaped = normalize_rows(templates)
    local_chan = stations % ch_local
    target = stations[:, 0] // (ch_local * n_tmpl)
    hit = local_chan[:, :, None] == jnp.arange(ch_local, dtype=jnp.int32)[None, None, :]
    ordered = jnp.einsum(
        "jki,jkl->jil", hit.astype(jnp.bfloat16), shaped, preferred_element_type=jnp.float32
    ).astype(jnp.bfloat16)
    ordered_shift = jnp.sum(jnp.where(hit, offsets[:, :, None], 0), axis=1)
    placed = place_moveout(ordered, ordered_shift, padded_len)
    filters = polyphase_filters(placed, phases)
    lhs = polyphase_signal(blocks, phases)
    corr = lax.conv_general_dilated(
        lhs,
        filters,
        (1,),
        "VALID",
        dimension_numbers=("NCH", "OIH", "NCH"),
        preferred_element_type=jnp.float32,
    )
    corr = corr[:, :, : lags // phases].reshape(n_blocks, count, phases, lags // phases)
    pick = target[None, :] == jnp.arange(n_blocks, dtype=jnp.int32)[:, None]
    chosen = jnp.sum(jnp.where(pick[:, :, None, None], corr, 0.0), axis=0)
    partial_value = jnp.transpose(chosen, (0, 2, 1)).reshape(count, lags)
    partial_value = partial_value.astype(jnp.bfloat16).astype(jnp.float32)
    inverse = (
        jnp.zeros((count,), jnp.int32).at[owner_map[0]].set(jnp.arange(count, dtype=jnp.int32))
    )
    arranged = partial_value[inverse]
    stack = lax.psum_scatter(arranged, "tmpl", scatter_dimension=0, tiled=True)
    power = jnp.mean(stack * stack, axis=1, keepdims=True)
    return stack * lax.rsqrt(power + eps)


def solution(mesh):
    in_specs = (
        P(("grp", "chan", "tmpl"), None),
        P(("grp", "chan"), "tmpl", None),
        P(("grp", "chan"), "tmpl"),
        P(("grp", "chan"), "tmpl"),
        P(("grp", "chan"), None),
    )
    out_specs = P(("grp", "chan", "tmpl"), None)
    return jax.shard_map(shards, mesh=mesh, in_specs=in_specs, out_specs=out_specs, check_vma=False)
```

```python
import functools

import jax
import jax.numpy as jnp
from jax import lax
from jax.experimental import pallas as pl
from jax.experimental.pallas import tpu as pltpu
from jax.sharding import PartitionSpec as P

OFF = 128
PHASES = 8


eps = 1e-05


def normalize_rows(values):
    values = values.astype(jnp.float32)
    centred = values - jnp.mean(values, axis=-1, keepdims=True)
    scale = lax.rsqrt(jnp.mean(centred * centred, axis=-1, keepdims=True) + eps)
    return (centred * scale).astype(jnp.bfloat16)


def place_moveout(rows, shifts, padded_len):
    extra = padded_len - rows.shape[-1]
    tail = jnp.zeros(rows.shape[:-1] + (extra,), rows.dtype)
    current = jnp.concatenate([rows, tail], axis=-1)
    for bit_number in range(OFF.bit_length()):
        step_len = 1 << bit_number
        lead = jnp.zeros(rows.shape[:-1] + (step_len,), rows.dtype)
        moved = jnp.concatenate([lead, current[..., : padded_len - step_len]], axis=-1)
        active = shifts >> bit_number & 1 == 1
        current = jnp.where(active[..., None], moved, current)
    return current


def _filter_kernel(grouped_ref, out_ref, *, steps, count, chans, phases):
    width = phases * chans
    first = pl.program_id(0) * steps
    for step in range(steps):
        lo = grouped_ref[first + step].astype(jnp.float32)
        hi = grouped_ref[first + step + 1].astype(jnp.float32)
        joined = jnp.concatenate([lo, hi], axis=-1)
        for e in range(phases):
            cut = (phases - 1 - e) * chans
            moved = pltpu.roll(joined, 2 * width - cut, 1) if cut else joined
            out_ref[step, e * count : (e + 1) * count, :] = moved[:, :width].astype(out_ref.dtype)


def polyphase_filters(placed, phases):
    count, chans, padded_len = placed.shape
    taps = padded_len // phases + 1
    front = phases - 1
    blocks = taps + 1
    padded = jnp.pad(placed, ((0, 0), (0, 0), (front, blocks * phases - padded_len - front)))
    grouped = padded.reshape(count, chans, blocks, phases)
    grouped = jnp.transpose(grouped, (2, 0, 3, 1)).reshape(blocks, count, phases * chans)
    steps = next(d for d in (9, 3, 1) if taps % d == 0)
    width = phases * chans
    kernel = functools.partial(
        _filter_kernel, steps=steps, count=count, chans=chans, phases=phases
    )
    return pl.pallas_call(
        kernel,
        grid=(taps // steps,),
        in_specs=[pl.BlockSpec((blocks, count, width), lambda q: (0, 0, 0))],
        out_specs=pl.BlockSpec((steps, phases * count, width), lambda q: (q, 0, 0)),
        out_shape=jax.ShapeDtypeStruct((taps, phases * count, width), placed.dtype),
    )(grouped)


def polyphase_signal(blocks, phases):
    n_blocks, chans, window = blocks.shape
    split = blocks.reshape(n_blocks, chans, window // phases, phases)
    split = jnp.transpose(split, (0, 3, 1, 2))
    return split.reshape(n_blocks, phases * chans, window // phases)


def shards(data, templates, stations, offsets, owner_map):
    n_tmpl = lax.axis_size("tmpl")
    ch_local = data.shape[0]
    window = data.shape[1]
    count = templates.shape[0]
    padded_len = templates.shape[2] + OFF
    lags = window - padded_len
    phases = PHASES
    signal = normalize_rows(data)
    blocks = lax.all_gather(signal, "chan", axis=0, tiled=False)
    n_blocks = blocks.shape[0]
    shaped = normalize_rows(templates)
    local_chan = stations % ch_local
    target = stations[:, 0] // (ch_local * n_tmpl)
    hit = local_chan[:, :, None] == jnp.arange(ch_local, dtype=jnp.int32)[None, None, :]
    ordered = jnp.einsum(
        "jki,jkl->jil", hit.astype(jnp.bfloat16), shaped, preferred_element_type=jnp.float32
    ).astype(jnp.bfloat16)
    ordered_shift = jnp.sum(jnp.where(hit, offsets[:, :, None], 0), axis=1)
    placed = place_moveout(ordered, ordered_shift, padded_len)
    filters = polyphase_filters(placed, phases)
    lhs = polyphase_signal(blocks, phases)
    corr = lax.conv_general_dilated(
        lhs,
        filters,
        (1,),
        "VALID",
        dimension_numbers=("NCH", "HOI", "NCH"),
        preferred_element_type=jnp.float32,
    )
    corr = corr[:, :, : lags // phases].reshape(n_blocks, phases, count, lags // phases)
    pick = target[None, :] == jnp.arange(n_blocks, dtype=jnp.int32)[:, None]
    chosen = jnp.sum(jnp.where(pick[:, None, :, None], corr, 0.0), axis=0)
    partial_value = jnp.transpose(chosen, (1, 2, 0)).reshape(count, lags)
    partial_value = partial_value.astype(jnp.bfloat16).astype(jnp.float32)
    inverse = (
        jnp.zeros((count,), jnp.int32).at[owner_map[0]].set(jnp.arange(count, dtype=jnp.int32))
    )
    arranged = partial_value[inverse]
    stack = lax.psum_scatter(arranged, "tmpl", scatter_dimension=0, tiled=True)
    power = jnp.mean(stack * stack, axis=1, keepdims=True)
    return stack * lax.rsqrt(power + eps)


def solution(mesh):
    in_specs = (
        P(("grp", "chan", "tmpl"), None),
        P(("grp", "chan"), "tmpl", None),
        P(("grp", "chan"), "tmpl"),
        P(("grp", "chan"), "tmpl"),
        P(("grp", "chan"), None),
    )
    out_specs = P(("grp", "chan", "tmpl"), None)
    return jax.shard_map(shards, mesh=mesh, in_specs=in_specs, out_specs=out_specs, check_vma=False)
```

```python
import functools

import jax
import jax.numpy as jnp
from jax import lax
from jax.experimental import pallas as pl
from jax.experimental.pallas import tpu as pltpu
from jax.sharding import PartitionSpec as P

OFF = 128
PHASES = 8


eps = 1e-05


def normalize_rows(values):
    values = values.astype(jnp.float32)
    centred = values - jnp.mean(values, axis=-1, keepdims=True)
    scale = lax.rsqrt(jnp.mean(centred * centred, axis=-1, keepdims=True) + eps)
    return (centred * scale).astype(jnp.bfloat16)


def place_moveout(rows, shifts, padded_len):
    extra = padded_len - rows.shape[-1]
    tail = jnp.zeros(rows.shape[:-1] + (extra,), rows.dtype)
    current = jnp.concatenate([rows, tail], axis=-1)
    for bit_number in range(OFF.bit_length()):
        step_len = 1 << bit_number
        lead = jnp.zeros(rows.shape[:-1] + (step_len,), rows.dtype)
        moved = jnp.concatenate([lead, current[..., : padded_len - step_len]], axis=-1)
        active = shifts >> bit_number & 1 == 1
        current = jnp.where(active[..., None], moved, current)
    return current


def _filter_kernel(grouped_ref, out_ref, *, steps, count, chans, phases):
    width = phases * chans
    first = pl.program_id(0) * steps
    for step in range(steps):
        lo = grouped_ref[first + step].astype(jnp.float32)
        hi = grouped_ref[first + step + 1].astype(jnp.float32)
        joined = jnp.concatenate([lo, hi], axis=-1)
        for e in range(phases):
            cut = (phases - 1 - e) * chans
            moved = pltpu.roll(joined, 2 * width - cut, 1) if cut else joined
            out_ref[step, e * count : (e + 1) * count, :] = moved[:, :width].astype(out_ref.dtype)


def polyphase_filters(placed, phases):
    count, chans, padded_len = placed.shape
    taps = padded_len // phases + 1
    front = phases - 1
    blocks = taps + 1
    padded = jnp.pad(placed, ((0, 0), (0, 0), (front, blocks * phases - padded_len - front)))
    grouped = padded.reshape(count, chans, blocks, phases)
    grouped = jnp.transpose(grouped, (2, 0, 3, 1)).reshape(blocks, count, phases * chans)
    steps = next(d for d in (9, 3, 1) if taps % d == 0)
    width = phases * chans
    kernel = functools.partial(
        _filter_kernel, steps=steps, count=count, chans=chans, phases=phases
    )
    return pl.pallas_call(
        kernel,
        grid=(taps // steps,),
        in_specs=[pl.BlockSpec((blocks, count, width), lambda q: (0, 0, 0))],
        out_specs=pl.BlockSpec((steps, phases * count, width), lambda q: (q, 0, 0)),
        out_shape=jax.ShapeDtypeStruct((taps, phases * count, width), placed.dtype),
    )(grouped)


def polyphase_signal(blocks, phases):
    n_blocks, chans, window = blocks.shape
    split = blocks.reshape(n_blocks, chans, window // phases, phases)
    split = jnp.transpose(split, (0, 3, 1, 2))
    return split.reshape(n_blocks, phases * chans, window // phases)


def shards(data, templates, stations, offsets, owner_map):
    n_tmpl = lax.axis_size("tmpl")
    ch_local = data.shape[0]
    window = data.shape[1]
    count = templates.shape[0]
    padded_len = templates.shape[2] + OFF
    lags = window - padded_len
    phases = PHASES
    signal = normalize_rows(data)
    n_chan = lax.axis_size("chan")
    if n_chan <= 8:
        me = lax.axis_index("chan")
        pieces = [signal]
        for shift in range(1, n_chan):
            pairs = [(c, (c + shift) % n_chan) for c in range(n_chan)]
            pieces.append(lax.ppermute(signal, "chan", pairs))
        blocks = jnp.stack(pieces)
    else:
        blocks = lax.all_gather(signal, "chan", axis=0, tiled=False)
    n_blocks = blocks.shape[0]
    shaped = normalize_rows(templates)
    local_chan = stations % ch_local
    target = stations[:, 0] // (ch_local * n_tmpl)
    if n_chan <= 8:
        target = (me - target) % n_chan
    hit = local_chan[:, :, None] == jnp.arange(ch_local, dtype=jnp.int32)[None, None, :]
    ordered = jnp.einsum(
        "jki,jkl->jil", hit.astype(jnp.bfloat16), shaped, preferred_element_type=jnp.float32
    ).astype(jnp.bfloat16)
    ordered_shift = jnp.sum(jnp.where(hit, offsets[:, :, None], 0), axis=1)
    placed = place_moveout(ordered, ordered_shift, padded_len)
    filters = polyphase_filters(placed, phases)
    lhs = polyphase_signal(blocks, phases)
    corr = lax.conv_general_dilated(
        lhs,
        filters,
        (1,),
        "VALID",
        dimension_numbers=("NCH", "HOI", "NCH"),
        preferred_element_type=jnp.float32,
    )
    corr = corr[:, :, : lags // phases].reshape(n_blocks, phases, count, lags // phases)
    pick = target[None, :] == jnp.arange(n_blocks, dtype=jnp.int32)[:, None]
    chosen = jnp.sum(jnp.where(pick[:, None, :, None], corr, 0.0), axis=0)
    partial_value = jnp.transpose(chosen, (1, 2, 0)).reshape(count, lags)
    partial_value = partial_value.astype(jnp.bfloat16)
    inverse = (
        jnp.zeros((count,), jnp.int32).at[owner_map[0]].set(jnp.arange(count, dtype=jnp.int32))
    )
    arranged = partial_value[inverse].reshape(n_tmpl, count // n_tmpl, lags)
    received = lax.all_to_all(arranged, "tmpl", 0, 0, tiled=True)
    stack = jnp.sum(received.astype(jnp.float32), axis=0)
    power = jnp.mean(stack * stack, axis=1, keepdims=True)
    return stack * lax.rsqrt(power + eps)


def solution(mesh):
    in_specs = (
        P(("grp", "chan", "tmpl"), None),
        P(("grp", "chan"), "tmpl", None),
        P(("grp", "chan"), "tmpl"),
        P(("grp", "chan"), "tmpl"),
        P(("grp", "chan"), None),
    )
    out_specs = P(("grp", "chan", "tmpl"), None)
    return jax.shard_map(shards, mesh=mesh, in_specs=in_specs, out_specs=out_specs, check_vma=False)
```

```python
import functools

import jax
import jax.numpy as jnp
from jax import lax
from jax.experimental import pallas as pl
from jax.experimental.pallas import tpu as pltpu
from jax.sharding import PartitionSpec as P

OFF = 128
PHASES = 8


eps = 1e-05


def normalize_rows(values):
    values = values.astype(jnp.float32)
    centred = values - jnp.mean(values, axis=-1, keepdims=True)
    scale = lax.rsqrt(jnp.mean(centred * centred, axis=-1, keepdims=True) + eps)
    return (centred * scale).astype(jnp.bfloat16)


def place_moveout(rows, shifts, padded_len):
    extra = padded_len - rows.shape[-1]
    tail = jnp.zeros(rows.shape[:-1] + (extra,), rows.dtype)
    current = jnp.concatenate([rows, tail], axis=-1)
    bits = OFF.bit_length()
    for low in range(0, bits, 3):
        width = min(3, bits - low)
        digit = (shifts >> low) & ((1 << width) - 1)
        padded = jnp.pad(current, [(0, 0)] * (rows.ndim - 1) + [(((1 << width) - 1) << low, 0)])
        total = padded.shape[-1]
        result = current
        for value in range(1, 1 << width):
            start = total - padded_len - (value << low)
            moved = padded[..., start : start + padded_len]
            result = jnp.where((digit == value)[..., None], moved, result)
        current = result
    return current


def _filter_kernel(grouped_ref, out_ref, *, steps, count, chans, phases):
    width = phases * chans
    first = pl.program_id(0) * steps
    for step in range(steps):
        lo = grouped_ref[first + step].astype(jnp.float32)
        hi = grouped_ref[first + step + 1].astype(jnp.float32)
        joined = jnp.concatenate([lo, hi], axis=-1)
        for e in range(phases):
            cut = (phases - 1 - e) * chans
            moved = pltpu.roll(joined, 2 * width - cut, 1) if cut else joined
            out_ref[step, e * count : (e + 1) * count, :] = moved[:, :width].astype(out_ref.dtype)


def polyphase_filters(placed, phases):
    count, chans, padded_len = placed.shape
    taps = padded_len // phases + 1
    front = phases - 1
    blocks = taps + 1
    padded = jnp.pad(placed, ((0, 0), (0, 0), (front, blocks * phases - padded_len - front)))
    grouped = jnp.transpose(padded, (0, 2, 1)).reshape(count, blocks, phases * chans)
    grouped = jnp.transpose(grouped, (1, 0, 2))
    steps = next(d for d in (9, 3, 1) if taps % d == 0)
    width = phases * chans
    kernel = functools.partial(
        _filter_kernel, steps=steps, count=count, chans=chans, phases=phases
    )
    return pl.pallas_call(
        kernel,
        grid=(taps // steps,),
        in_specs=[pl.BlockSpec((blocks, count, width), lambda q: (0, 0, 0))],
        out_specs=pl.BlockSpec((steps, phases * count, width), lambda q: (q, 0, 0)),
        out_shape=jax.ShapeDtypeStruct((taps, phases * count, width), placed.dtype),
    )(grouped)


def polyphase_signal(blocks, phases):
    n_blocks, chans, window = blocks.shape
    split = blocks.reshape(n_blocks, chans, window // phases, phases)
    split = jnp.transpose(split, (0, 3, 1, 2))
    return split.reshape(n_blocks, phases * chans, window // phases)


def shards(data, templates, stations, offsets, owner_map):
    n_tmpl = lax.axis_size("tmpl")
    ch_local = data.shape[0]
    window = data.shape[1]
    count = templates.shape[0]
    padded_len = templates.shape[2] + OFF
    lags = window - padded_len
    phases = PHASES
    signal = normalize_rows(data)
    n_chan = lax.axis_size("chan")
    if n_chan <= 8:
        me = lax.axis_index("chan")
        pieces = [signal]
        for shift in range(1, n_chan):
            pairs = [(c, (c + shift) % n_chan) for c in range(n_chan)]
            pieces.append(lax.ppermute(signal, "chan", pairs))
        blocks = jnp.stack(pieces)
    else:
        blocks = lax.all_gather(signal, "chan", axis=0, tiled=False)
    n_blocks = blocks.shape[0]
    shaped = normalize_rows(templates)
    local_chan = stations % ch_local
    target = stations[:, 0] // (ch_local * n_tmpl)
    if n_chan <= 8:
        target = (me - target) % n_chan
    hit = local_chan[:, :, None] == jnp.arange(ch_local, dtype=jnp.int32)[None, None, :]
    ordered = jnp.einsum(
        "jki,jkl->jil", hit.astype(jnp.bfloat16), shaped, preferred_element_type=jnp.float32
    ).astype(jnp.bfloat16)
    ordered_shift = jnp.sum(jnp.where(hit, offsets[:, :, None], 0), axis=1)
    placed = place_moveout(ordered, ordered_shift, padded_len)
    filters = polyphase_filters(placed, phases)
    lhs = polyphase_signal(blocks, phases)
    corr = lax.conv_general_dilated(
        lhs,
        filters,
        (1,),
        "VALID",
        dimension_numbers=("NCH", "HOI", "NCH"),
        preferred_element_type=jnp.float32,
    )
    corr = corr[:, :, : lags // phases].reshape(n_blocks, phases, count, lags // phases)
    pick = target[None, :] == jnp.arange(n_blocks, dtype=jnp.int32)[:, None]
    chosen = jnp.sum(jnp.where(pick[:, None, :, None], corr, 0.0), axis=0)
    partial_value = jnp.transpose(chosen, (1, 2, 0)).reshape(count, lags)
    partial_value = partial_value.astype(jnp.bfloat16)
    inverse = (
        jnp.zeros((count,), jnp.int32).at[owner_map[0]].set(jnp.arange(count, dtype=jnp.int32))
    )
    arranged = partial_value[inverse].reshape(n_tmpl, count // n_tmpl, lags)
    received = lax.all_to_all(arranged, "tmpl", 0, 0, tiled=True)
    stack = jnp.sum(received.astype(jnp.float32), axis=0)
    power = jnp.mean(stack * stack, axis=1, keepdims=True)
    return stack * lax.rsqrt(power + eps)


def solution(mesh):
    in_specs = (
        P(("grp", "chan", "tmpl"), None),
        P(("grp", "chan"), "tmpl", None),
        P(("grp", "chan"), "tmpl"),
        P(("grp", "chan"), "tmpl"),
        P(("grp", "chan"), None),
    )
    out_specs = P(("grp", "chan", "tmpl"), None)
    return jax.shard_map(shards, mesh=mesh, in_specs=in_specs, out_specs=out_specs, check_vma=False)
```

```python
import functools

import jax
import jax.numpy as jnp
from jax import lax
from jax.experimental import pallas as pl
from jax.experimental.pallas import tpu as pltpu
from jax.sharding import PartitionSpec as P

OFF = 128
PHASES = 8


eps = 1e-05


def normalize_rows(values):
    values = values.astype(jnp.float32)
    centred = values - jnp.mean(values, axis=-1, keepdims=True)
    scale = lax.rsqrt(jnp.mean(centred * centred, axis=-1, keepdims=True) + eps)
    return (centred * scale).astype(jnp.bfloat16)


def place_moveout(rows, shifts, padded_len):
    extra = padded_len - rows.shape[-1]
    tail = jnp.zeros(rows.shape[:-1] + (extra,), rows.dtype)
    current = jnp.concatenate([rows, tail], axis=-1)
    for bit_number in range(OFF.bit_length()):
        step_len = 1 << bit_number
        lead = jnp.zeros(rows.shape[:-1] + (step_len,), rows.dtype)
        moved = jnp.concatenate([lead, current[..., : padded_len - step_len]], axis=-1)
        active = shifts >> bit_number & 1 == 1
        current = jnp.where(active[..., None], moved, current)
    return current


def _filter_kernel(grouped_ref, out_ref, *, steps, count, chans, phases):
    width = phases * chans
    first = pl.program_id(0) * steps
    for step in range(steps):
        lo = grouped_ref[first + step].astype(jnp.float32)
        hi = grouped_ref[first + step + 1].astype(jnp.float32)
        joined = jnp.concatenate([lo, hi], axis=-1)
        for e in range(phases):
            cut = (phases - 1 - e) * chans
            moved = pltpu.roll(joined, 2 * width - cut, 1) if cut else joined
            out_ref[step, e * count : (e + 1) * count, :] = moved[:, :width].astype(out_ref.dtype)


def polyphase_filters(placed, phases):
    count, padded_len, chans = placed.shape
    taps = padded_len // phases + 1
    front = phases - 1
    blocks = taps + 1
    padded = jnp.pad(placed, ((0, 0), (front, blocks * phases - padded_len - front), (0, 0)))
    grouped = padded.reshape(count, blocks, phases * chans)
    grouped = jnp.transpose(grouped, (1, 0, 2))
    steps = next(d for d in (9, 3, 1) if taps % d == 0)
    width = phases * chans
    kernel = functools.partial(
        _filter_kernel, steps=steps, count=count, chans=chans, phases=phases
    )
    return pl.pallas_call(
        kernel,
        grid=(taps // steps,),
        in_specs=[pl.BlockSpec((blocks, count, width), lambda q: (0, 0, 0))],
        out_specs=pl.BlockSpec((steps, phases * count, width), lambda q: (q, 0, 0)),
        out_shape=jax.ShapeDtypeStruct((taps, phases * count, width), placed.dtype),
    )(grouped)


def polyphase_signal(blocks, phases):
    n_blocks, chans, window = blocks.shape
    split = blocks.reshape(n_blocks, chans, window // phases, phases)
    split = jnp.transpose(split, (0, 3, 1, 2))
    return split.reshape(n_blocks, phases * chans, window // phases)


def shards(data, templates, stations, offsets, owner_map):
    n_tmpl = lax.axis_size("tmpl")
    ch_local = data.shape[0]
    window = data.shape[1]
    count = templates.shape[0]
    padded_len = templates.shape[2] + OFF
    lags = window - padded_len
    phases = PHASES
    signal = normalize_rows(data)
    n_chan = lax.axis_size("chan")
    if n_chan <= 8:
        me = lax.axis_index("chan")
        pieces = [signal]
        for shift in range(1, n_chan):
            pairs = [(c, (c + shift) % n_chan) for c in range(n_chan)]
            pieces.append(lax.ppermute(signal, "chan", pairs))
        blocks = jnp.stack(pieces)
    else:
        blocks = lax.all_gather(signal, "chan", axis=0, tiled=False)
    n_blocks = blocks.shape[0]
    shaped = normalize_rows(templates)
    local_chan = stations % ch_local
    target = stations[:, 0] // (ch_local * n_tmpl)
    if n_chan <= 8:
        target = (me - target) % n_chan
    hit = local_chan[:, :, None] == jnp.arange(ch_local, dtype=jnp.int32)[None, None, :]
    moved = place_moveout(shaped, offsets, padded_len)
    placed = jnp.einsum(
        "jki,jkl->jli", hit.astype(jnp.bfloat16), moved, preferred_element_type=jnp.float32
    ).astype(jnp.bfloat16)
    filters = polyphase_filters(placed, phases)
    lhs = polyphase_signal(blocks, phases)
    corr = lax.conv_general_dilated(
        lhs,
        filters,
        (1,),
        "VALID",
        dimension_numbers=("NCH", "HOI", "NCH"),
        preferred_element_type=jnp.float32,
    )
    corr = corr[:, :, : lags // phases].reshape(n_blocks, phases, count, lags // phases)
    pick = target[None, :] == jnp.arange(n_blocks, dtype=jnp.int32)[:, None]
    chosen = jnp.sum(jnp.where(pick[:, None, :, None], corr, 0.0), axis=0)
    partial_value = jnp.transpose(chosen, (1, 2, 0)).reshape(count, lags)
    partial_value = partial_value.astype(jnp.bfloat16)
    inverse = (
        jnp.zeros((count,), jnp.int32).at[owner_map[0]].set(jnp.arange(count, dtype=jnp.int32))
    )
    arranged = partial_value[inverse].reshape(n_tmpl, count // n_tmpl, lags)
    received = lax.all_to_all(arranged, "tmpl", 0, 0, tiled=True)
    stack = jnp.sum(received.astype(jnp.float32), axis=0)
    power = jnp.mean(stack * stack, axis=1, keepdims=True)
    return stack * lax.rsqrt(power + eps)


def solution(mesh):
    in_specs = (
        P(("grp", "chan", "tmpl"), None),
        P(("grp", "chan"), "tmpl", None),
        P(("grp", "chan"), "tmpl"),
        P(("grp", "chan"), "tmpl"),
        P(("grp", "chan"), None),
    )
    out_specs = P(("grp", "chan", "tmpl"), None)
    return jax.shard_map(shards, mesh=mesh, in_specs=in_specs, out_specs=out_specs, check_vma=False)
```

```python
import functools

import jax
import jax.numpy as jnp
from jax import lax
from jax.experimental import pallas as pl
from jax.experimental.pallas import tpu as pltpu
from jax.sharding import PartitionSpec as P

OFF = 128
PHASES = 8


eps = 1e-05


def normalize_rows(values):
    values = values.astype(jnp.float32)
    centred = values - jnp.mean(values, axis=-1, keepdims=True)
    scale = lax.rsqrt(jnp.mean(centred * centred, axis=-1, keepdims=True) + eps)
    return (centred * scale).astype(jnp.bfloat16)


def place_moveout(rows, shifts, padded_len):
    extra = padded_len - rows.shape[-1]
    tail = jnp.zeros(rows.shape[:-1] + (extra,), rows.dtype)
    current = jnp.concatenate([rows, tail], axis=-1)
    for bit_number in range(OFF.bit_length()):
        step_len = 1 << bit_number
        lead = jnp.zeros(rows.shape[:-1] + (step_len,), rows.dtype)
        moved = jnp.concatenate([lead, current[..., : padded_len - step_len]], axis=-1)
        active = shifts >> bit_number & 1 == 1
        current = jnp.where(active[..., None], moved, current)
    return current


def _filter_kernel(grouped_ref, out_ref, *, steps, count, chans, phases):
    width = phases * chans
    first = pl.program_id(0) * steps
    for step in range(steps):
        lo = grouped_ref[first + step].astype(jnp.float32)
        hi = grouped_ref[first + step + 1].astype(jnp.float32)
        joined = jnp.concatenate([lo, hi], axis=-1)
        for e in range(phases):
            cut = (phases - 1 - e) * chans
            moved = pltpu.roll(joined, 2 * width - cut, 1) if cut else joined
            out_ref[step, e * count : (e + 1) * count, :] = moved[:, :width].astype(out_ref.dtype)


def polyphase_filters(placed, phases):
    count, chans, padded_len = placed.shape
    taps = padded_len // phases + 1
    front = phases - 1
    blocks = taps + 1
    padded = jnp.pad(placed, ((0, 0), (0, 0), (front, blocks * phases - padded_len - front)))
    grouped = jnp.transpose(padded, (0, 2, 1)).reshape(count, blocks, phases * chans)
    grouped = jnp.transpose(grouped, (1, 0, 2))
    steps = next(d for d in (9, 3, 1) if taps % d == 0)
    width = phases * chans
    kernel = functools.partial(
        _filter_kernel, steps=steps, count=count, chans=chans, phases=phases
    )
    return pl.pallas_call(
        kernel,
        grid=(taps // steps,),
        in_specs=[pl.BlockSpec((blocks, count, width), lambda q: (0, 0, 0))],
        out_specs=pl.BlockSpec((steps, phases * count, width), lambda q: (q, 0, 0)),
        out_shape=jax.ShapeDtypeStruct((taps, phases * count, width), placed.dtype),
    )(grouped)


def polyphase_signal(blocks, phases):
    n_blocks, chans, window = blocks.shape
    split = blocks.reshape(n_blocks, chans, window // phases, phases)
    split = jnp.transpose(split, (0, 3, 1, 2))
    return split.reshape(n_blocks, phases * chans, window // phases)


def shards(data, templates, stations, offsets, owner_map):
    n_tmpl = lax.axis_size("tmpl")
    ch_local = data.shape[0]
    window = data.shape[1]
    count = templates.shape[0]
    padded_len = templates.shape[2] + OFF
    lags = window - padded_len
    phases = PHASES
    signal = normalize_rows(data)
    n_chan = lax.axis_size("chan")
    if n_chan <= 8:
        me = lax.axis_index("chan")
        pieces = [signal]
        for shift in range(1, n_chan):
            pairs = [(c, (c + shift) % n_chan) for c in range(n_chan)]
            pieces.append(lax.ppermute(signal, "chan", pairs))
        blocks = jnp.stack(pieces)
    else:
        blocks = lax.all_gather(signal, "chan", axis=0, tiled=False)
    n_blocks = blocks.shape[0]
    shaped = normalize_rows(templates)
    local_chan = stations % ch_local
    target = stations[:, 0] // (ch_local * n_tmpl)
    if n_chan <= 8:
        target = (me - target) % n_chan
    hit = local_chan[:, :, None] == jnp.arange(ch_local, dtype=jnp.int32)[None, None, :]
    ordered = jnp.einsum(
        "jki,jkl->jil", hit.astype(jnp.bfloat16), shaped, preferred_element_type=jnp.float32
    ).astype(jnp.bfloat16)
    ordered_shift = jnp.sum(jnp.where(hit, offsets[:, :, None], 0), axis=1)
    placed = place_moveout(ordered, ordered_shift, padded_len)
    filters = polyphase_filters(placed, phases)
    lhs = polyphase_signal(blocks, phases)
    span = lhs.shape[-1]
    lhs = jnp.transpose(lhs, (1, 0, 2)).reshape(1, lhs.shape[1], n_blocks * span)
    corr = lax.conv_general_dilated(
        lhs,
        filters,
        (1,),
        "VALID",
        dimension_numbers=("NCH", "HOI", "NCH"),
        preferred_element_type=jnp.float32,
    )
    corr = jnp.pad(corr[0], ((0, 0), (0, n_blocks * span - corr.shape[-1])))
    corr = corr.reshape(corr.shape[0], n_blocks, span)[:, :, : lags // phases]
    corr = jnp.transpose(corr, (1, 0, 2)).reshape(n_blocks, phases, count, lags // phases)
    pick = target[None, :] == jnp.arange(n_blocks, dtype=jnp.int32)[:, None]
    chosen = jnp.sum(jnp.where(pick[:, None, :, None], corr, 0.0), axis=0)
    partial_value = jnp.transpose(chosen, (1, 2, 0)).reshape(count, lags)
    partial_value = partial_value.astype(jnp.bfloat16)
    inverse = (
        jnp.zeros((count,), jnp.int32).at[owner_map[0]].set(jnp.arange(count, dtype=jnp.int32))
    )
    arranged = partial_value[inverse].reshape(n_tmpl, count // n_tmpl, lags)
    received = lax.all_to_all(arranged, "tmpl", 0, 0, tiled=True)
    stack = jnp.sum(received.astype(jnp.float32), axis=0)
    power = jnp.mean(stack * stack, axis=1, keepdims=True)
    return stack * lax.rsqrt(power + eps)


def solution(mesh):
    in_specs = (
        P(("grp", "chan", "tmpl"), None),
        P(("grp", "chan"), "tmpl", None),
        P(("grp", "chan"), "tmpl"),
        P(("grp", "chan"), "tmpl"),
        P(("grp", "chan"), None),
    )
    out_specs = P(("grp", "chan", "tmpl"), None)
    return jax.shard_map(shards, mesh=mesh, in_specs=in_specs, out_specs=out_specs, check_vma=False)
```

```python
import functools

import jax
import jax.numpy as jnp
from jax import lax
from jax.experimental import pallas as pl
from jax.experimental.pallas import tpu as pltpu
from jax.sharding import PartitionSpec as P

OFF = 128
PHASES = 8


eps = 1e-05


def normalize_rows(values):
    values = values.astype(jnp.float32)
    centred = values - jnp.mean(values, axis=-1, keepdims=True)
    scale = lax.rsqrt(jnp.mean(centred * centred, axis=-1, keepdims=True) + eps)
    return (centred * scale).astype(jnp.bfloat16)


def place_moveout(rows, shifts, padded_len):
    extra = padded_len - rows.shape[-1]
    tail = jnp.zeros(rows.shape[:-1] + (extra,), rows.dtype)
    current = jnp.concatenate([rows, tail], axis=-1)
    for bit_number in range(OFF.bit_length()):
        step_len = 1 << bit_number
        lead = jnp.zeros(rows.shape[:-1] + (step_len,), rows.dtype)
        moved = jnp.concatenate([lead, current[..., : padded_len - step_len]], axis=-1)
        active = shifts >> bit_number & 1 == 1
        current = jnp.where(active[..., None], moved, current)
    return current


def _filter_kernel(grouped_ref, out_ref, *, steps, count, chans, phases):
    width = phases * chans
    first = pl.program_id(0) * steps
    for step in range(steps):
        lo = grouped_ref[first + step].astype(jnp.float32)
        hi = grouped_ref[first + step + 1].astype(jnp.float32)
        joined = jnp.concatenate([lo, hi], axis=-1)
        for e in range(phases):
            cut = (phases - 1 - e) * chans
            moved = pltpu.roll(joined, 2 * width - cut, 1) if cut else joined
            out_ref[step, e * count : (e + 1) * count, :] = moved[:, :width].astype(out_ref.dtype)


def polyphase_filters(placed, phases):
    count, chans, padded_len = placed.shape
    taps = padded_len // phases + 1
    front = phases - 1
    blocks = taps + 1
    padded = jnp.pad(placed, ((0, 0), (0, 0), (front, blocks * phases - padded_len - front)))
    grouped = jnp.transpose(padded, (0, 2, 1)).reshape(count, blocks, phases * chans)
    grouped = jnp.transpose(grouped, (1, 0, 2))
    steps = next(d for d in (9, 3, 1) if taps % d == 0)
    width = phases * chans
    kernel = functools.partial(
        _filter_kernel, steps=steps, count=count, chans=chans, phases=phases
    )
    return pl.pallas_call(
        kernel,
        grid=(taps // steps,),
        in_specs=[pl.BlockSpec((blocks, count, width), lambda q: (0, 0, 0))],
        out_specs=pl.BlockSpec((steps, phases * count, width), lambda q: (q, 0, 0)),
        out_shape=jax.ShapeDtypeStruct((taps, phases * count, width), placed.dtype),
    )(grouped)


def polyphase_signal(blocks, phases):
    n_blocks, chans, window = blocks.shape
    split = blocks.reshape(n_blocks, chans, window // phases, phases)
    split = jnp.transpose(split, (0, 3, 1, 2))
    return split.reshape(n_blocks, phases * chans, window // phases)


def shards(data, templates, stations, offsets, owner_map):
    n_tmpl = lax.axis_size("tmpl")
    ch_local = data.shape[0]
    window = data.shape[1]
    count = templates.shape[0]
    padded_len = templates.shape[2] + OFF
    lags = window - padded_len
    phases = PHASES
    signal = normalize_rows(data)
    n_chan = lax.axis_size("chan")
    if n_chan <= 8:
        me = lax.axis_index("chan")
        pieces = [signal]
        for shift in range(1, n_chan):
            pairs = [(c, (c + shift) % n_chan) for c in range(n_chan)]
            pieces.append(lax.ppermute(signal, "chan", pairs))
        blocks = jnp.stack(pieces)
    else:
        blocks = lax.all_gather(signal, "chan", axis=0, tiled=False)
    n_blocks = blocks.shape[0]
    shaped = normalize_rows(templates)
    local_chan = stations % ch_local
    target = stations[:, 0] // (ch_local * n_tmpl)
    if n_chan <= 8:
        target = (me - target) % n_chan
    hit = local_chan[:, :, None] == jnp.arange(ch_local, dtype=jnp.int32)[None, None, :]
    ordered = jnp.einsum(
        "jki,jkl->jil", hit.astype(jnp.bfloat16), shaped, preferred_element_type=jnp.float32
    ).astype(jnp.bfloat16)
    ordered_shift = jnp.sum(jnp.where(hit, offsets[:, :, None], 0), axis=1)
    placed = place_moveout(ordered, ordered_shift, padded_len)
    filters = polyphase_filters(placed, phases)
    lhs = polyphase_signal(blocks, phases)
    corr = lax.conv_general_dilated(
        lhs,
        filters,
        (1,),
        "VALID",
        dimension_numbers=("NCH", "HOI", "NCH"),
        preferred_element_type=jnp.float32,
    )
    corr = corr[:, :, : lags // phases].reshape(n_blocks, phases, count, lags // phases)
    pick = target[None, :] == jnp.arange(n_blocks, dtype=jnp.int32)[:, None]
    chosen = jnp.sum(jnp.where(pick[:, None, :, None], corr, 0.0), axis=0)
    partial_value = jnp.transpose(chosen, (1, 2, 0)).reshape(count, lags)
    partial_value = partial_value.astype(jnp.bfloat16)
    inverse = (
        jnp.zeros((count,), jnp.int32).at[owner_map[0]].set(jnp.arange(count, dtype=jnp.int32))
    )
    arranged = partial_value[inverse].reshape(n_tmpl, count // n_tmpl, lags)
    if n_tmpl <= 8:
        mine = lax.axis_index("tmpl")
        stack = jnp.take(arranged, mine, axis=0).astype(jnp.float32)
        for shift in range(1, n_tmpl):
            pairs = [(t, (t + shift) % n_tmpl) for t in range(n_tmpl)]
            outgoing = jnp.take(arranged, (mine + shift) % n_tmpl, axis=0)
            stack = stack + lax.ppermute(outgoing, "tmpl", pairs).astype(jnp.float32)
    else:
        received = lax.all_to_all(arranged, "tmpl", 0, 0, tiled=True)
        stack = jnp.sum(received.astype(jnp.float32), axis=0)
    power = jnp.mean(stack * stack, axis=1, keepdims=True)
    return stack * lax.rsqrt(power + eps)


def solution(mesh):
    in_specs = (
        P(("grp", "chan", "tmpl"), None),
        P(("grp", "chan"), "tmpl", None),
        P(("grp", "chan"), "tmpl"),
        P(("grp", "chan"), "tmpl"),
        P(("grp", "chan"), None),
    )
    out_specs = P(("grp", "chan", "tmpl"), None)
    return jax.shard_map(shards, mesh=mesh, in_specs=in_specs, out_specs=out_specs, check_vma=False)
```

```python
import functools

import jax
import jax.numpy as jnp
from jax import lax
from jax.experimental import pallas as pl
from jax.experimental.pallas import tpu as pltpu
from jax.sharding import PartitionSpec as P

OFF = 128
PHASES = 8


eps = 1e-05


def normalize_rows(values):
    values = values.astype(jnp.float32)
    centred = values - jnp.mean(values, axis=-1, keepdims=True)
    scale = lax.rsqrt(jnp.mean(centred * centred, axis=-1, keepdims=True) + eps)
    return (centred * scale).astype(jnp.bfloat16)


def place_moveout(rows, shifts, padded_len):
    extra = padded_len - rows.shape[-1]
    tail = jnp.zeros(rows.shape[:-1] + (extra,), rows.dtype)
    current = jnp.concatenate([rows, tail], axis=-1)
    for bit_number in range(OFF.bit_length()):
        step_len = 1 << bit_number
        lead = jnp.zeros(rows.shape[:-1] + (step_len,), rows.dtype)
        moved = jnp.concatenate([lead, current[..., : padded_len - step_len]], axis=-1)
        active = shifts >> bit_number & 1 == 1
        current = jnp.where(active[..., None], moved, current)
    return current


def _filter_kernel(grouped_ref, out_ref, *, steps, count, chans, phases):
    width = phases * chans
    first = pl.program_id(0) * steps
    for step in range(steps):
        lo = grouped_ref[first + step]
        hi = grouped_ref[first + step + 1]
        joined = jnp.concatenate([lo, hi], axis=-1)
        for e in range(phases):
            cut = (phases - 1 - e) * chans
            moved = pltpu.roll(joined, 2 * width - cut, 1) if cut else joined
            out_ref[step, e * count : (e + 1) * count, :] = moved[:, :width]


def polyphase_filters(placed, phases):
    count, chans, padded_len = placed.shape
    taps = padded_len // phases + 1
    front = phases - 1
    blocks = taps + 1
    padded = jnp.pad(placed, ((0, 0), (0, 0), (front, blocks * phases - padded_len - front)))
    grouped = jnp.transpose(padded, (0, 2, 1)).reshape(count, blocks, phases * chans)
    grouped = jnp.transpose(grouped, (1, 0, 2))
    steps = next(d for d in (9, 3, 1) if taps % d == 0)
    width = phases * chans
    kernel = functools.partial(
        _filter_kernel, steps=steps, count=count, chans=chans, phases=phases
    )
    return pl.pallas_call(
        kernel,
        grid=(taps // steps,),
        in_specs=[pl.BlockSpec((blocks, count, width), lambda q: (0, 0, 0))],
        out_specs=pl.BlockSpec((steps, phases * count, width), lambda q: (q, 0, 0)),
        out_shape=jax.ShapeDtypeStruct((taps, phases * count, width), placed.dtype),
    )(grouped)


def polyphase_signal(blocks, phases):
    n_blocks, chans, window = blocks.shape
    split = blocks.reshape(n_blocks, chans, window // phases, phases)
    split = jnp.transpose(split, (0, 3, 1, 2))
    return split.reshape(n_blocks, phases * chans, window // phases)


def shards(data, templates, stations, offsets, owner_map):
    n_tmpl = lax.axis_size("tmpl")
    ch_local = data.shape[0]
    window = data.shape[1]
    count = templates.shape[0]
    padded_len = templates.shape[2] + OFF
    lags = window - padded_len
    phases = PHASES
    signal = normalize_rows(data)
    n_chan = lax.axis_size("chan")
    me = lax.axis_index("chan")
    shaped = normalize_rows(templates)
    local_chan = stations % ch_local
    target = stations[:, 0] // (ch_local * n_tmpl)
    if n_chan <= 8:
        target = (me - target) % n_chan
    hit = local_chan[:, :, None] == jnp.arange(ch_local, dtype=jnp.int32)[None, None, :]
    ordered = jnp.einsum(
        "jki,jkl->jil", hit.astype(jnp.bfloat16), shaped, preferred_element_type=jnp.float32
    ).astype(jnp.bfloat16)
    ordered_shift = jnp.sum(jnp.where(hit, offsets[:, :, None], 0), axis=1)
    placed = place_moveout(ordered, ordered_shift, padded_len)
    signal, placed = lax.optimization_barrier((signal, placed))
    if n_chan <= 8:
        pieces = [signal]
        for shift in range(1, n_chan):
            pairs = [(c, (c + shift) % n_chan) for c in range(n_chan)]
            pieces.append(lax.ppermute(signal, "chan", pairs))
        blocks = jnp.stack(pieces)
    else:
        blocks = lax.all_gather(signal, "chan", axis=0, tiled=False)
    n_blocks = blocks.shape[0]
    filters = polyphase_filters(placed, phases)
    lhs = polyphase_signal(blocks, phases)
    corr = lax.conv_general_dilated(
        lhs,
        filters,
        (1,),
        "VALID",
        dimension_numbers=("NCH", "HOI", "NCH"),
        preferred_element_type=jnp.float32,
    )
    corr = corr[:, :, : lags // phases].reshape(n_blocks, phases, count, lags // phases)
    pick = target[None, :] == jnp.arange(n_blocks, dtype=jnp.int32)[:, None]
    chosen = jnp.sum(jnp.where(pick[:, None, :, None], corr, 0.0), axis=0)
    partial_value = jnp.transpose(chosen, (1, 2, 0)).reshape(count, lags)
    partial_value = partial_value.astype(jnp.bfloat16)
    inverse = (
        jnp.zeros((count,), jnp.int32).at[owner_map[0]].set(jnp.arange(count, dtype=jnp.int32))
    )
    arranged = partial_value[inverse].reshape(n_tmpl, count // n_tmpl, lags)
    if n_tmpl <= 8:
        mine = lax.axis_index("tmpl")
        stack = jnp.take(arranged, mine, axis=0).astype(jnp.float32)
        for shift in range(1, n_tmpl):
            pairs = [(t, (t + shift) % n_tmpl) for t in range(n_tmpl)]
            outgoing = jnp.take(arranged, (mine + shift) % n_tmpl, axis=0)
            stack = stack + lax.ppermute(outgoing, "tmpl", pairs).astype(jnp.float32)
    else:
        received = lax.all_to_all(arranged, "tmpl", 0, 0, tiled=True)
        stack = jnp.sum(received.astype(jnp.float32), axis=0)
    power = jnp.mean(stack * stack, axis=1, keepdims=True)
    return stack * lax.rsqrt(power + eps)


def solution(mesh):
    in_specs = (
        P(("grp", "chan", "tmpl"), None),
        P(("grp", "chan"), "tmpl", None),
        P(("grp", "chan"), "tmpl"),
        P(("grp", "chan"), "tmpl"),
        P(("grp", "chan"), None),
    )
    out_specs = P(("grp", "chan", "tmpl"), None)
    return jax.shard_map(shards, mesh=mesh, in_specs=in_specs, out_specs=out_specs, check_vma=False)
```

```python
import functools

import jax
import jax.numpy as jnp
from jax import lax
from jax.experimental import pallas as pl
from jax.experimental.pallas import tpu as pltpu
from jax.sharding import PartitionSpec as P

OFF = 128
PHASES = 8


eps = 1e-05


def normalize_rows(values):
    values = values.astype(jnp.float32)
    centred = values - jnp.mean(values, axis=-1, keepdims=True)
    scale = lax.rsqrt(jnp.mean(centred * centred, axis=-1, keepdims=True) + eps)
    return (centred * scale).astype(jnp.bfloat16)


def place_moveout(rows, shifts, padded_len):
    extra = padded_len - rows.shape[-1]
    tail = jnp.zeros(rows.shape[:-1] + (extra,), rows.dtype)
    current = jnp.concatenate([rows, tail], axis=-1)
    for bit_number in range(OFF.bit_length()):
        step_len = 1 << bit_number
        lead = jnp.zeros(rows.shape[:-1] + (step_len,), rows.dtype)
        moved = jnp.concatenate([lead, current[..., : padded_len - step_len]], axis=-1)
        active = shifts >> bit_number & 1 == 1
        current = jnp.where(active[..., None], moved, current)
    return current


def _filter_kernel(grouped_ref, out_ref, *, steps, count, chans, phases):
    width = phases * chans
    first = pl.program_id(0) * steps
    for step in range(steps):
        lo = grouped_ref[first + step]
        hi = grouped_ref[first + step + 1]
        joined = jnp.concatenate([lo, hi], axis=-1)
        for e in range(phases):
            cut = (phases - 1 - e) * chans
            moved = pltpu.roll(joined, 2 * width - cut, 1) if cut else joined
            out_ref[step, e * count : (e + 1) * count, :] = moved[:, :width]


def polyphase_filters(placed, phases):
    count, chans, padded_len = placed.shape
    taps = padded_len // phases + 1
    front = phases - 1
    blocks = taps + 1
    padded = jnp.pad(placed, ((0, 0), (0, 0), (front, blocks * phases - padded_len - front)))
    grouped = jnp.transpose(padded, (0, 2, 1)).reshape(count, blocks, phases * chans)
    grouped = jnp.transpose(grouped, (1, 0, 2))
    steps = next(d for d in (9, 3, 1) if taps % d == 0)
    width = phases * chans
    kernel = functools.partial(
        _filter_kernel, steps=steps, count=count, chans=chans, phases=phases
    )
    return pl.pallas_call(
        kernel,
        grid=(taps // steps,),
        in_specs=[pl.BlockSpec((blocks, count, width), lambda q: (0, 0, 0))],
        out_specs=pl.BlockSpec((steps, phases * count, width), lambda q: (q, 0, 0)),
        out_shape=jax.ShapeDtypeStruct((taps, phases * count, width), placed.dtype),
    )(grouped)


def _corr_kernel(grouped_ref, signal_ref, out_ref, acc_ref, filt_ref, *, steps, count, chans, phases, rows):
    width = phases * chans
    pid = pl.program_id(0)

    @pl.when(pid == 0)
    def _():
        acc_ref[...] = jnp.zeros_like(acc_ref)

    base = pl.multiple_of(pid * steps, steps)
    for step in range(steps):
        joined = jnp.concatenate([grouped_ref[base + step], grouped_ref[base + step + 1]], axis=-1)
        for e in range(phases):
            cut = (phases - 1 - e) * chans
            moved = pltpu.roll(joined, 2 * width - cut, 1) if cut else joined
            filt_ref[step, e * count : (e + 1) * count, :] = moved[:, :width]

    def accumulate(g, carry):
        band = signal_ref[g, pl.ds(base, rows + steps), :]
        total = acc_ref[g]
        for step in range(steps):
            window = band[step : step + rows].astype(filt_ref.dtype)
            total += lax.dot_general(
                window, filt_ref[step], (((1,), (1,)), ((), ())),
                preferred_element_type=jnp.float32,
            )
        acc_ref[g] = total
        return carry

    lax.fori_loop(0, signal_ref.shape[0], accumulate, 0)

    @pl.when(pid == pl.num_programs(0) - 1)
    def _():
        out_ref[...] = acc_ref[...]


def correlate(placed, blocks, phases, lags):
    count, chans, padded_len = placed.shape
    n_blocks, _, window = blocks.shape
    steps = 8
    taps = -(-(padded_len // phases + 1) // steps) * steps
    front = phases - 1
    n_groups = taps + 1
    rows = lags // phases
    width = phases * chans
    padded = jnp.pad(placed, ((0, 0), (0, 0), (front, n_groups * phases - padded_len - front)))
    grouped = jnp.transpose(padded, (0, 2, 1)).reshape(count, n_groups, width)
    grouped = jnp.transpose(grouped, (1, 0, 2))
    signal = jnp.transpose(blocks, (0, 2, 1)).reshape(n_blocks, window // phases, width)
    signal = jnp.pad(signal.astype(jnp.float32), ((0, 0), (0, taps + rows - window // phases), (0, 0)))
    kernel = functools.partial(
        _corr_kernel, steps=steps, count=count, chans=chans, phases=phases, rows=rows
    )
    return pl.pallas_call(
        kernel,
        grid=(taps // steps,),
        in_specs=[
            pl.BlockSpec(grouped.shape, lambda q: (0, 0, 0)),
            pl.BlockSpec(signal.shape, lambda q: (0, 0, 0)),
        ],
        out_specs=pl.BlockSpec((n_blocks, rows, phases * count), lambda q: (0, 0, 0)),
        out_shape=jax.ShapeDtypeStruct((n_blocks, rows, phases * count), jnp.float32),
        scratch_shapes=[
            pltpu.VMEM((n_blocks, rows, phases * count), jnp.float32),
            pltpu.VMEM((steps, phases * count, width), placed.dtype),
        ],
    )(grouped, signal)


def shards(data, templates, stations, offsets, owner_map):
    n_tmpl = lax.axis_size("tmpl")
    ch_local = data.shape[0]
    window = data.shape[1]
    count = templates.shape[0]
    padded_len = templates.shape[2] + OFF
    lags = window - padded_len
    phases = PHASES
    signal = normalize_rows(data)
    n_chan = lax.axis_size("chan")
    me = lax.axis_index("chan")
    shaped = normalize_rows(templates)
    local_chan = stations % ch_local
    target = stations[:, 0] // (ch_local * n_tmpl)
    if n_chan <= 8:
        target = (me - target) % n_chan
    hit = local_chan[:, :, None] == jnp.arange(ch_local, dtype=jnp.int32)[None, None, :]
    ordered = jnp.einsum(
        "jki,jkl->jil", hit.astype(jnp.bfloat16), shaped, preferred_element_type=jnp.float32
    ).astype(jnp.bfloat16)
    ordered_shift = jnp.sum(jnp.where(hit, offsets[:, :, None], 0), axis=1)
    placed = place_moveout(ordered, ordered_shift, padded_len)
    signal, placed = lax.optimization_barrier((signal, placed))
    if n_chan <= 8:
        pieces = [signal]
        for shift in range(1, n_chan):
            pairs = [(c, (c + shift) % n_chan) for c in range(n_chan)]
            pieces.append(lax.ppermute(signal, "chan", pairs))
        blocks = jnp.stack(pieces)
    else:
        blocks = lax.all_gather(signal, "chan", axis=0, tiled=False)
    n_blocks = blocks.shape[0]
    corr = correlate(placed, blocks, phases, lags)
    corr = corr.reshape(n_blocks, lags // phases, phases, count)
    pick = target[None, :] == jnp.arange(n_blocks, dtype=jnp.int32)[:, None]
    chosen = jnp.sum(jnp.where(pick[:, None, None, :], corr, 0.0), axis=0)
    partial_value = jnp.transpose(chosen, (2, 0, 1)).reshape(count, lags)
    partial_value = partial_value.astype(jnp.bfloat16)
    inverse = (
        jnp.zeros((count,), jnp.int32).at[owner_map[0]].set(jnp.arange(count, dtype=jnp.int32))
    )
    arranged = partial_value[inverse].reshape(n_tmpl, count // n_tmpl, lags)
    if n_tmpl <= 8:
        mine = lax.axis_index("tmpl")
        stack = jnp.take(arranged, mine, axis=0).astype(jnp.float32)
        for shift in range(1, n_tmpl):
            pairs = [(t, (t + shift) % n_tmpl) for t in range(n_tmpl)]
            outgoing = jnp.take(arranged, (mine + shift) % n_tmpl, axis=0)
            stack = stack + lax.ppermute(outgoing, "tmpl", pairs).astype(jnp.float32)
    else:
        received = lax.all_to_all(arranged, "tmpl", 0, 0, tiled=True)
        stack = jnp.sum(received.astype(jnp.float32), axis=0)
    power = jnp.mean(stack * stack, axis=1, keepdims=True)
    return stack * lax.rsqrt(power + eps)


def solution(mesh):
    in_specs = (
        P(("grp", "chan", "tmpl"), None),
        P(("grp", "chan"), "tmpl", None),
        P(("grp", "chan"), "tmpl"),
        P(("grp", "chan"), "tmpl"),
        P(("grp", "chan"), None),
    )
    out_specs = P(("grp", "chan", "tmpl"), None)
    return jax.shard_map(shards, mesh=mesh, in_specs=in_specs, out_specs=out_specs, check_vma=False)
```

```python
import functools

import jax
import jax.numpy as jnp
from jax import lax
from jax.experimental import pallas as pl
from jax.experimental.pallas import tpu as pltpu
from jax.sharding import PartitionSpec as P

OFF = 128
PHASES = 8


eps = 1e-05


def normalize_rows(values):
    values = values.astype(jnp.float32)
    centred = values - jnp.mean(values, axis=-1, keepdims=True)
    scale = lax.rsqrt(jnp.mean(centred * centred, axis=-1, keepdims=True) + eps)
    return (centred * scale).astype(jnp.bfloat16)


def place_moveout(rows, shifts, padded_len):
    extra = padded_len - rows.shape[-1]
    tail = jnp.zeros(rows.shape[:-1] + (extra,), rows.dtype)
    current = jnp.concatenate([rows, tail], axis=-1)
    for bit_number in range(OFF.bit_length()):
        step_len = 1 << bit_number
        lead = jnp.zeros(rows.shape[:-1] + (step_len,), rows.dtype)
        moved = jnp.concatenate([lead, current[..., : padded_len - step_len]], axis=-1)
        active = shifts >> bit_number & 1 == 1
        current = jnp.where(active[..., None], moved, current)
    return current


def _filter_kernel(grouped_ref, out_ref, *, steps, count, chans, phases):
    width = phases * chans
    first = pl.program_id(0) * steps
    for step in range(steps):
        lo = grouped_ref[first + step]
        hi = grouped_ref[first + step + 1]
        joined = jnp.concatenate([lo, hi], axis=-1)
        for e in range(phases):
            cut = (phases - 1 - e) * chans
            moved = pltpu.roll(joined, 2 * width - cut, 1) if cut else joined
            out_ref[step, e * count : (e + 1) * count, :] = moved[:, :width]


def polyphase_filters(placed, phases):
    count, chans, padded_len = placed.shape
    taps = padded_len // phases + 1
    front = phases - 1
    blocks = taps + 1
    padded = jnp.pad(placed, ((0, 0), (0, 0), (front, blocks * phases - padded_len - front)))
    grouped = jnp.transpose(padded, (0, 2, 1)).reshape(count, blocks, phases * chans)
    grouped = jnp.transpose(grouped, (1, 0, 2))
    steps = next(d for d in (9, 3, 1) if taps % d == 0)
    width = phases * chans
    kernel = functools.partial(
        _filter_kernel, steps=steps, count=count, chans=chans, phases=phases
    )
    return pl.pallas_call(
        kernel,
        grid=(taps // steps,),
        in_specs=[pl.BlockSpec((blocks, count, width), lambda q: (0, 0, 0))],
        out_specs=pl.BlockSpec((steps, phases * count, width), lambda q: (q, 0, 0)),
        out_shape=jax.ShapeDtypeStruct((taps, phases * count, width), placed.dtype),
    )(grouped)


def _corr_kernel(grouped_ref, signal_ref, out_ref, acc_ref, filt_ref, *, steps, count, chans, phases, rows):
    width = phases * chans
    pid = pl.program_id(0)

    @pl.when(pid == 0)
    def _():
        acc_ref[...] = jnp.zeros_like(acc_ref)

    base = pl.multiple_of(pid * steps, steps)
    for step in range(steps):
        joined = jnp.concatenate([grouped_ref[base + step], grouped_ref[base + step + 1]], axis=-1)
        joined = joined.astype(jnp.float32)
        parts = []
        for e in range(phases):
            cut = (phases - 1 - e) * chans
            moved = pltpu.roll(joined, 2 * width - cut, 1) if cut else joined
            parts.append(moved[:, :width])
        filt_ref[step] = jnp.transpose(jnp.concatenate(parts, axis=0)).astype(filt_ref.dtype)

    def accumulate(g, carry):
        band = signal_ref[g, pl.ds(base, rows + steps), :]
        total = acc_ref[g]
        for step in range(steps):
            window = band[step : step + rows].astype(filt_ref.dtype)
            total += jnp.dot(window, filt_ref[step], preferred_element_type=jnp.float32)
        acc_ref[g] = total
        return carry

    lax.fori_loop(0, signal_ref.shape[0], accumulate, 0)

    @pl.when(pid == pl.num_programs(0) - 1)
    def _():
        out_ref[...] = acc_ref[...]


def correlate(placed, blocks, phases, lags):
    count, chans, padded_len = placed.shape
    n_blocks, _, window = blocks.shape
    steps = 8
    taps = -(-(padded_len // phases + 1) // steps) * steps
    front = phases - 1
    n_groups = taps + 1
    rows = lags // phases
    width = phases * chans
    padded = jnp.pad(placed, ((0, 0), (0, 0), (front, n_groups * phases - padded_len - front)))
    grouped = jnp.transpose(padded, (0, 2, 1)).reshape(count, n_groups, width)
    grouped = jnp.transpose(grouped, (1, 0, 2))
    signal = jnp.transpose(blocks, (0, 2, 1)).reshape(n_blocks, window // phases, width)
    signal = jnp.pad(signal.astype(jnp.float32), ((0, 0), (0, taps + rows - window // phases), (0, 0)))
    kernel = functools.partial(
        _corr_kernel, steps=steps, count=count, chans=chans, phases=phases, rows=rows
    )
    return pl.pallas_call(
        kernel,
        grid=(taps // steps,),
        in_specs=[
            pl.BlockSpec(grouped.shape, lambda q: (0, 0, 0)),
            pl.BlockSpec(signal.shape, lambda q: (0, 0, 0)),
        ],
        out_specs=pl.BlockSpec((n_blocks, rows, phases * count), lambda q: (0, 0, 0)),
        out_shape=jax.ShapeDtypeStruct((n_blocks, rows, phases * count), jnp.float32),
        scratch_shapes=[
            pltpu.VMEM((n_blocks, rows, phases * count), jnp.float32),
            pltpu.VMEM((steps, phases * count, width), placed.dtype),
        ],
    )(grouped, signal)


def shards(data, templates, stations, offsets, owner_map):
    n_tmpl = lax.axis_size("tmpl")
    ch_local = data.shape[0]
    window = data.shape[1]
    count = templates.shape[0]
    padded_len = templates.shape[2] + OFF
    lags = window - padded_len
    phases = PHASES
    signal = normalize_rows(data)
    n_chan = lax.axis_size("chan")
    me = lax.axis_index("chan")
    shaped = normalize_rows(templates)
    local_chan = stations % ch_local
    target = stations[:, 0] // (ch_local * n_tmpl)
    if n_chan <= 8:
        target = (me - target) % n_chan
    hit = local_chan[:, :, None] == jnp.arange(ch_local, dtype=jnp.int32)[None, None, :]
    ordered = jnp.einsum(
        "jki,jkl->jil", hit.astype(jnp.bfloat16), shaped, preferred_element_type=jnp.float32
    ).astype(jnp.bfloat16)
    ordered_shift = jnp.sum(jnp.where(hit, offsets[:, :, None], 0), axis=1)
    placed = place_moveout(ordered, ordered_shift, padded_len)
    signal, placed = lax.optimization_barrier((signal, placed))
    if n_chan <= 8:
        pieces = [signal]
        for shift in range(1, n_chan):
            pairs = [(c, (c + shift) % n_chan) for c in range(n_chan)]
            pieces.append(lax.ppermute(signal, "chan", pairs))
        blocks = jnp.stack(pieces)
    else:
        blocks = lax.all_gather(signal, "chan", axis=0, tiled=False)
    n_blocks = blocks.shape[0]
    corr = correlate(placed, blocks, phases, lags)
    corr = corr.reshape(n_blocks, lags // phases, phases, count)
    pick = target[None, :] == jnp.arange(n_blocks, dtype=jnp.int32)[:, None]
    chosen = jnp.sum(jnp.where(pick[:, None, None, :], corr, 0.0), axis=0)
    partial_value = jnp.transpose(chosen, (2, 0, 1)).reshape(count, lags)
    partial_value = partial_value.astype(jnp.bfloat16)
    inverse = (
        jnp.zeros((count,), jnp.int32).at[owner_map[0]].set(jnp.arange(count, dtype=jnp.int32))
    )
    arranged = partial_value[inverse].reshape(n_tmpl, count // n_tmpl, lags)
    if n_tmpl <= 8:
        mine = lax.axis_index("tmpl")
        stack = jnp.take(arranged, mine, axis=0).astype(jnp.float32)
        for shift in range(1, n_tmpl):
            pairs = [(t, (t + shift) % n_tmpl) for t in range(n_tmpl)]
            outgoing = jnp.take(arranged, (mine + shift) % n_tmpl, axis=0)
            stack = stack + lax.ppermute(outgoing, "tmpl", pairs).astype(jnp.float32)
    else:
        received = lax.all_to_all(arranged, "tmpl", 0, 0, tiled=True)
        stack = jnp.sum(received.astype(jnp.float32), axis=0)
    power = jnp.mean(stack * stack, axis=1, keepdims=True)
    return stack * lax.rsqrt(power + eps)


def solution(mesh):
    in_specs = (
        P(("grp", "chan", "tmpl"), None),
        P(("grp", "chan"), "tmpl", None),
        P(("grp", "chan"), "tmpl"),
        P(("grp", "chan"), "tmpl"),
        P(("grp", "chan"), None),
    )
    out_specs = P(("grp", "chan", "tmpl"), None)
    return jax.shard_map(shards, mesh=mesh, in_specs=in_specs, out_specs=out_specs, check_vma=False)
```

```python
import functools

import jax
import jax.numpy as jnp
from jax import lax
from jax.experimental import pallas as pl
from jax.experimental.pallas import tpu as pltpu
from jax.sharding import PartitionSpec as P

OFF = 128
PHASES = 8


eps = 1e-05


def normalize_rows(values):
    values = values.astype(jnp.float32)
    centred = values - jnp.mean(values, axis=-1, keepdims=True)
    scale = lax.rsqrt(jnp.mean(centred * centred, axis=-1, keepdims=True) + eps)
    return (centred * scale).astype(jnp.bfloat16)


def place_moveout(rows, shifts, padded_len):
    extra = padded_len - rows.shape[-1]
    tail = jnp.zeros(rows.shape[:-1] + (extra,), rows.dtype)
    current = jnp.concatenate([rows, tail], axis=-1)
    for bit_number in range(OFF.bit_length()):
        step_len = 1 << bit_number
        lead = jnp.zeros(rows.shape[:-1] + (step_len,), rows.dtype)
        moved = jnp.concatenate([lead, current[..., : padded_len - step_len]], axis=-1)
        active = shifts >> bit_number & 1 == 1
        current = jnp.where(active[..., None], moved, current)
    return current


def _filter_kernel(grouped_ref, out_ref, *, steps, count, chans, phases):
    width = phases * chans
    first = pl.program_id(0) * steps
    for step in range(steps):
        lo = grouped_ref[first + step]
        hi = grouped_ref[first + step + 1]
        joined = jnp.concatenate([lo, hi], axis=-1)
        for e in range(phases):
            cut = (phases - 1 - e) * chans
            moved = pltpu.roll(joined, 2 * width - cut, 1) if cut else joined
            out_ref[step, e * count : (e + 1) * count, :] = moved[:, :width]


def polyphase_filters(placed, phases):
    count, chans, padded_len = placed.shape
    taps = padded_len // phases + 1
    front = phases - 1
    blocks = taps + 1
    padded = jnp.pad(placed, ((0, 0), (0, 0), (front, blocks * phases - padded_len - front)))
    grouped = jnp.transpose(padded, (0, 2, 1)).reshape(count, blocks, phases * chans)
    grouped = jnp.transpose(grouped, (1, 0, 2))
    steps = next(d for d in (9, 3, 1) if taps % d == 0)
    width = phases * chans
    kernel = functools.partial(
        _filter_kernel, steps=steps, count=count, chans=chans, phases=phases
    )
    return pl.pallas_call(
        kernel,
        grid=(taps // steps,),
        in_specs=[pl.BlockSpec((blocks, count, width), lambda q: (0, 0, 0))],
        out_specs=pl.BlockSpec((steps, phases * count, width), lambda q: (q, 0, 0)),
        out_shape=jax.ShapeDtypeStruct((taps, phases * count, width), placed.dtype),
    )(grouped)


def _corr_kernel(grouped_ref, signal_ref, out_ref, acc_ref, filt_ref, *, steps, count, chans, phases, rows):
    width = phases * chans
    pid = pl.program_id(0)

    @pl.when(pid == 0)
    def _():
        acc_ref[...] = jnp.zeros_like(acc_ref)

    base = pl.multiple_of(pid * steps, steps)
    for step in range(steps):
        joined = jnp.concatenate([grouped_ref[base + step], grouped_ref[base + step + 1]], axis=-1)
        joined = joined.astype(jnp.float32)
        parts = []
        for e in range(phases):
            cut = (phases - 1 - e) * chans
            moved = pltpu.roll(joined, 2 * width - cut, 1) if cut else joined
            parts.append(moved[:, :width])
        filt_ref[step] = jnp.transpose(jnp.concatenate(parts, axis=0)).astype(filt_ref.dtype)

    n_blocks = signal_ref.shape[0]
    if n_blocks <= 8:
        band = signal_ref[:, pl.ds(base, rows + steps), :]
        total = acc_ref[...]
        for step in range(steps):
            window = band[:, step : step + rows].astype(filt_ref.dtype)
            window = window.reshape(n_blocks * rows, width)
            total += jnp.dot(window, filt_ref[step], preferred_element_type=jnp.float32)
        acc_ref[...] = total
    else:

        def accumulate(g, carry):
            band = signal_ref[g, pl.ds(base, rows + steps), :]
            start = pl.multiple_of(g * rows, rows)
            total = acc_ref[pl.ds(start, rows), :]
            for step in range(steps):
                window = band[step : step + rows].astype(filt_ref.dtype)
                total += jnp.dot(window, filt_ref[step], preferred_element_type=jnp.float32)
            acc_ref[pl.ds(start, rows), :] = total
            return carry

        lax.fori_loop(0, n_blocks, accumulate, 0)

    @pl.when(pid == pl.num_programs(0) - 1)
    def _():
        out_ref[...] = acc_ref[...].reshape(out_ref.shape)


def correlate(placed, blocks, phases, lags):
    count, chans, padded_len = placed.shape
    n_blocks, _, window = blocks.shape
    steps = 8
    taps = -(-(padded_len // phases + 1) // steps) * steps
    front = phases - 1
    n_groups = taps + 1
    rows = lags // phases
    width = phases * chans
    padded = jnp.pad(placed, ((0, 0), (0, 0), (front, n_groups * phases - padded_len - front)))
    grouped = jnp.transpose(padded, (0, 2, 1)).reshape(count, n_groups, width)
    grouped = jnp.transpose(grouped, (1, 0, 2))
    signal = jnp.transpose(blocks, (0, 2, 1)).reshape(n_blocks, window // phases, width)
    signal = jnp.pad(signal.astype(jnp.float32), ((0, 0), (0, taps + rows - window // phases), (0, 0)))
    kernel = functools.partial(
        _corr_kernel, steps=steps, count=count, chans=chans, phases=phases, rows=rows
    )
    return pl.pallas_call(
        kernel,
        grid=(taps // steps,),
        in_specs=[
            pl.BlockSpec(grouped.shape, lambda q: (0, 0, 0)),
            pl.BlockSpec(signal.shape, lambda q: (0, 0, 0)),
        ],
        out_specs=pl.BlockSpec((n_blocks, rows, phases * count), lambda q: (0, 0, 0)),
        out_shape=jax.ShapeDtypeStruct((n_blocks, rows, phases * count), jnp.float32),
        scratch_shapes=[
            pltpu.VMEM((n_blocks * rows, phases * count), jnp.float32),
            pltpu.VMEM((steps, phases * count, width), placed.dtype),
        ],
    )(grouped, signal)


def shards(data, templates, stations, offsets, owner_map):
    n_tmpl = lax.axis_size("tmpl")
    ch_local = data.shape[0]
    window = data.shape[1]
    count = templates.shape[0]
    padded_len = templates.shape[2] + OFF
    lags = window - padded_len
    phases = PHASES
    signal = normalize_rows(data)
    n_chan = lax.axis_size("chan")
    me = lax.axis_index("chan")
    shaped = normalize_rows(templates)
    local_chan = stations % ch_local
    target = stations[:, 0] // (ch_local * n_tmpl)
    if n_chan <= 8:
        target = (me - target) % n_chan
    hit = local_chan[:, :, None] == jnp.arange(ch_local, dtype=jnp.int32)[None, None, :]
    ordered = jnp.einsum(
        "jki,jkl->jil", hit.astype(jnp.bfloat16), shaped, preferred_element_type=jnp.float32
    ).astype(jnp.bfloat16)
    ordered_shift = jnp.sum(jnp.where(hit, offsets[:, :, None], 0), axis=1)
    placed = place_moveout(ordered, ordered_shift, padded_len)
    signal, placed = lax.optimization_barrier((signal, placed))
    if n_chan <= 8:
        pieces = [signal]
        for shift in range(1, n_chan):
            pairs = [(c, (c + shift) % n_chan) for c in range(n_chan)]
            pieces.append(lax.ppermute(signal, "chan", pairs))
        blocks = jnp.stack(pieces)
    else:
        blocks = lax.all_gather(signal, "chan", axis=0, tiled=False)
    n_blocks = blocks.shape[0]
    corr = correlate(placed, blocks, phases, lags)
    corr = corr.reshape(n_blocks, lags // phases, phases, count)
    pick = target[None, :] == jnp.arange(n_blocks, dtype=jnp.int32)[:, None]
    chosen = jnp.sum(jnp.where(pick[:, None, None, :], corr, 0.0), axis=0)
    partial_value = jnp.transpose(chosen, (2, 0, 1)).reshape(count, lags)
    partial_value = partial_value.astype(jnp.bfloat16)
    inverse = (
        jnp.zeros((count,), jnp.int32).at[owner_map[0]].set(jnp.arange(count, dtype=jnp.int32))
    )
    arranged = partial_value[inverse].reshape(n_tmpl, count // n_tmpl, lags)
    if n_tmpl <= 8:
        mine = lax.axis_index("tmpl")
        stack = jnp.take(arranged, mine, axis=0).astype(jnp.float32)
        for shift in range(1, n_tmpl):
            pairs = [(t, (t + shift) % n_tmpl) for t in range(n_tmpl)]
            outgoing = jnp.take(arranged, (mine + shift) % n_tmpl, axis=0)
            stack = stack + lax.ppermute(outgoing, "tmpl", pairs).astype(jnp.float32)
    else:
        received = lax.all_to_all(arranged, "tmpl", 0, 0, tiled=True)
        stack = jnp.sum(received.astype(jnp.float32), axis=0)
    power = jnp.mean(stack * stack, axis=1, keepdims=True)
    return stack * lax.rsqrt(power + eps)


def solution(mesh):
    in_specs = (
        P(("grp", "chan", "tmpl"), None),
        P(("grp", "chan"), "tmpl", None),
        P(("grp", "chan"), "tmpl"),
        P(("grp", "chan"), "tmpl"),
        P(("grp", "chan"), None),
    )
    out_specs = P(("grp", "chan", "tmpl"), None)
    return jax.shard_map(shards, mesh=mesh, in_specs=in_specs, out_specs=out_specs, check_vma=False)
```

```python
import functools

import jax
import jax.numpy as jnp
from jax import lax
from jax.experimental import pallas as pl
from jax.experimental.pallas import tpu as pltpu
from jax.sharding import PartitionSpec as P

OFF = 128
PHASES = 8


eps = 1e-05


def normalize_rows(values):
    values = values.astype(jnp.float32)
    centred = values - jnp.mean(values, axis=-1, keepdims=True)
    scale = lax.rsqrt(jnp.mean(centred * centred, axis=-1, keepdims=True) + eps)
    return (centred * scale).astype(jnp.bfloat16)


def place_moveout(rows, shifts, padded_len):
    extra = padded_len - rows.shape[-1]
    tail = jnp.zeros(rows.shape[:-1] + (extra,), rows.dtype)
    current = jnp.concatenate([rows, tail], axis=-1)
    for bit_number in range(OFF.bit_length()):
        step_len = 1 << bit_number
        lead = jnp.zeros(rows.shape[:-1] + (step_len,), rows.dtype)
        moved = jnp.concatenate([lead, current[..., : padded_len - step_len]], axis=-1)
        active = shifts >> bit_number & 1 == 1
        current = jnp.where(active[..., None], moved, current)
    return current


def _filter_kernel(grouped_ref, out_ref, *, steps, count, chans, phases):
    width = phases * chans
    first = pl.program_id(0) * steps
    for step in range(steps):
        lo = grouped_ref[first + step]
        hi = grouped_ref[first + step + 1]
        joined = jnp.concatenate([lo, hi], axis=-1)
        for e in range(phases):
            cut = (phases - 1 - e) * chans
            moved = pltpu.roll(joined, 2 * width - cut, 1) if cut else joined
            out_ref[step, e * count : (e + 1) * count, :] = moved[:, :width]


def polyphase_filters(placed, phases):
    count, chans, padded_len = placed.shape
    taps = padded_len // phases + 1
    front = phases - 1
    blocks = taps + 1
    padded = jnp.pad(placed, ((0, 0), (0, 0), (front, blocks * phases - padded_len - front)))
    grouped = jnp.transpose(padded, (0, 2, 1)).reshape(count, blocks, phases * chans)
    grouped = jnp.transpose(grouped, (1, 0, 2))
    steps = next(d for d in (9, 3, 1) if taps % d == 0)
    width = phases * chans
    kernel = functools.partial(
        _filter_kernel, steps=steps, count=count, chans=chans, phases=phases
    )
    return pl.pallas_call(
        kernel,
        grid=(taps // steps,),
        in_specs=[pl.BlockSpec((blocks, count, width), lambda q: (0, 0, 0))],
        out_specs=pl.BlockSpec((steps, phases * count, width), lambda q: (q, 0, 0)),
        out_shape=jax.ShapeDtypeStruct((taps, phases * count, width), placed.dtype),
    )(grouped)


def _corr_kernel(grouped_ref, signal_ref, out_ref, acc_ref, filt_ref, *, steps, count, chans, phases, rows):
    width = phases * chans
    pid = pl.program_id(0)

    @pl.when(pid == 0)
    def _():
        acc_ref[...] = jnp.zeros_like(acc_ref)

    base = pl.multiple_of(pid * steps, steps)
    for step in range(steps):
        joined = jnp.concatenate(
            [grouped_ref[:, base + step, :], grouped_ref[:, base + step + 1, :]], axis=-1
        )
        joined = joined.astype(jnp.float32)
        parts = []
        for e in range(phases):
            cut = (phases - 1 - e) * chans
            moved = pltpu.roll(joined, 2 * width - cut, 1) if cut else joined
            parts.append(moved[:, :width])
        filt_ref[step] = jnp.transpose(jnp.concatenate(parts, axis=0)).astype(filt_ref.dtype)

    n_blocks = signal_ref.shape[0]
    if n_blocks <= 8:
        band = signal_ref[:, pl.ds(base, rows + steps), :]
        total = acc_ref[...]
        for step in range(steps):
            window = band[:, step : step + rows].astype(filt_ref.dtype)
            window = window.reshape(n_blocks * rows, width)
            total += jnp.dot(window, filt_ref[step], preferred_element_type=jnp.float32)
        acc_ref[...] = total
    else:

        def accumulate(g, carry):
            band = signal_ref[g, pl.ds(base, rows + steps), :]
            start = pl.multiple_of(g * rows, rows)
            total = acc_ref[pl.ds(start, rows), :]
            for step in range(steps):
                window = band[step : step + rows].astype(filt_ref.dtype)
                total += jnp.dot(window, filt_ref[step], preferred_element_type=jnp.float32)
            acc_ref[pl.ds(start, rows), :] = total
            return carry

        lax.fori_loop(0, n_blocks, accumulate, 0)

    @pl.when(pid == pl.num_programs(0) - 1)
    def _():
        out_ref[...] = acc_ref[...].reshape(out_ref.shape)


def correlate(placed, blocks, phases, lags):
    count, chans, padded_len = placed.shape
    n_blocks, _, window = blocks.shape
    steps = 8
    taps = -(-(padded_len // phases + 1) // steps) * steps
    front = phases - 1
    n_groups = taps + 1
    rows = lags // phases
    width = phases * chans
    padded = jnp.pad(placed, ((0, 0), (0, 0), (front, n_groups * phases - padded_len - front)))
    grouped = jnp.transpose(padded, (0, 2, 1)).reshape(count, n_groups, width)
    grouped = grouped.astype(jnp.float32)
    signal = jnp.transpose(blocks, (0, 2, 1)).reshape(n_blocks, window // phases, width)
    signal = jnp.pad(signal.astype(jnp.float32), ((0, 0), (0, taps + rows - window // phases), (0, 0)))
    kernel = functools.partial(
        _corr_kernel, steps=steps, count=count, chans=chans, phases=phases, rows=rows
    )
    return pl.pallas_call(
        kernel,
        grid=(taps // steps,),
        in_specs=[
            pl.BlockSpec(grouped.shape, lambda q: (0, 0, 0)),
            pl.BlockSpec(signal.shape, lambda q: (0, 0, 0)),
        ],
        out_specs=pl.BlockSpec((n_blocks, rows, phases * count), lambda q: (0, 0, 0)),
        out_shape=jax.ShapeDtypeStruct((n_blocks, rows, phases * count), jnp.float32),
        scratch_shapes=[
            pltpu.VMEM((n_blocks * rows, phases * count), jnp.float32),
            pltpu.VMEM((steps, phases * count, width), placed.dtype),
        ],
    )(grouped, signal)


def shards(data, templates, stations, offsets, owner_map):
    n_tmpl = lax.axis_size("tmpl")
    ch_local = data.shape[0]
    window = data.shape[1]
    count = templates.shape[0]
    padded_len = templates.shape[2] + OFF
    lags = window - padded_len
    phases = PHASES
    signal = normalize_rows(data)
    n_chan = lax.axis_size("chan")
    me = lax.axis_index("chan")
    shaped = normalize_rows(templates)
    local_chan = stations % ch_local
    target = stations[:, 0] // (ch_local * n_tmpl)
    if n_chan <= 8:
        target = (me - target) % n_chan
    hit = local_chan[:, :, None] == jnp.arange(ch_local, dtype=jnp.int32)[None, None, :]
    ordered = jnp.einsum(
        "jki,jkl->jil", hit.astype(jnp.bfloat16), shaped, preferred_element_type=jnp.float32
    ).astype(jnp.bfloat16)
    ordered_shift = jnp.sum(jnp.where(hit, offsets[:, :, None], 0), axis=1)
    placed = place_moveout(ordered, ordered_shift, padded_len)
    signal, placed = lax.optimization_barrier((signal, placed))
    if n_chan <= 8:
        pieces = [signal]
        for shift in range(1, n_chan):
            pairs = [(c, (c + shift) % n_chan) for c in range(n_chan)]
            pieces.append(lax.ppermute(signal, "chan", pairs))
        blocks = jnp.stack(pieces)
    else:
        blocks = lax.all_gather(signal, "chan", axis=0, tiled=False)
    n_blocks = blocks.shape[0]
    corr = correlate(placed, blocks, phases, lags)
    corr = corr.reshape(n_blocks, lags // phases, phases, count)
    pick = target[None, :] == jnp.arange(n_blocks, dtype=jnp.int32)[:, None]
    chosen = jnp.sum(jnp.where(pick[:, None, None, :], corr, 0.0), axis=0)
    partial_value = jnp.transpose(chosen, (2, 0, 1)).reshape(count, lags)
    partial_value = partial_value.astype(jnp.bfloat16)
    inverse = (
        jnp.zeros((count,), jnp.int32).at[owner_map[0]].set(jnp.arange(count, dtype=jnp.int32))
    )
    arranged = partial_value[inverse].reshape(n_tmpl, count // n_tmpl, lags)
    if n_tmpl <= 8:
        mine = lax.axis_index("tmpl")
        stack = jnp.take(arranged, mine, axis=0).astype(jnp.float32)
        for shift in range(1, n_tmpl):
            pairs = [(t, (t + shift) % n_tmpl) for t in range(n_tmpl)]
            outgoing = jnp.take(arranged, (mine + shift) % n_tmpl, axis=0)
            stack = stack + lax.ppermute(outgoing, "tmpl", pairs).astype(jnp.float32)
    else:
        received = lax.all_to_all(arranged, "tmpl", 0, 0, tiled=True)
        stack = jnp.sum(received.astype(jnp.float32), axis=0)
    power = jnp.mean(stack * stack, axis=1, keepdims=True)
    return stack * lax.rsqrt(power + eps)


def solution(mesh):
    in_specs = (
        P(("grp", "chan", "tmpl"), None),
        P(("grp", "chan"), "tmpl", None),
        P(("grp", "chan"), "tmpl"),
        P(("grp", "chan"), "tmpl"),
        P(("grp", "chan"), None),
    )
    out_specs = P(("grp", "chan", "tmpl"), None)
    return jax.shard_map(shards, mesh=mesh, in_specs=in_specs, out_specs=out_specs, check_vma=False)
```

```python
import functools

import jax
import jax.numpy as jnp
from jax import lax
from jax.experimental import pallas as pl
from jax.experimental.pallas import tpu as pltpu
from jax.sharding import PartitionSpec as P

OFF = 128
PHASES = 8


eps = 1e-05


def normalize_rows(values):
    values = values.astype(jnp.float32)
    centred = values - jnp.mean(values, axis=-1, keepdims=True)
    scale = lax.rsqrt(jnp.mean(centred * centred, axis=-1, keepdims=True) + eps)
    return (centred * scale).astype(jnp.bfloat16)


def place_moveout(rows, shifts, padded_len):
    extra = padded_len - rows.shape[-1]
    tail = jnp.zeros(rows.shape[:-1] + (extra,), rows.dtype)
    current = jnp.concatenate([rows, tail], axis=-1)
    for bit_number in range(OFF.bit_length()):
        step_len = 1 << bit_number
        lead = jnp.zeros(rows.shape[:-1] + (step_len,), rows.dtype)
        moved = jnp.concatenate([lead, current[..., : padded_len - step_len]], axis=-1)
        active = shifts >> bit_number & 1 == 1
        current = jnp.where(active[..., None], moved, current)
    return current


def _filter_kernel(grouped_ref, out_ref, *, steps, count, chans, phases):
    width = phases * chans
    first = pl.program_id(0) * steps
    for step in range(steps):
        lo = grouped_ref[first + step]
        hi = grouped_ref[first + step + 1]
        joined = jnp.concatenate([lo, hi], axis=-1)
        for e in range(phases):
            cut = (phases - 1 - e) * chans
            moved = pltpu.roll(joined, 2 * width - cut, 1) if cut else joined
            out_ref[step, e * count : (e + 1) * count, :] = moved[:, :width]


def polyphase_filters(placed, phases):
    count, chans, padded_len = placed.shape
    taps = padded_len // phases + 1
    front = phases - 1
    blocks = taps + 1
    padded = jnp.pad(placed, ((0, 0), (0, 0), (front, blocks * phases - padded_len - front)))
    grouped = jnp.transpose(padded, (0, 2, 1)).reshape(count, blocks, phases * chans)
    grouped = jnp.transpose(grouped, (1, 0, 2))
    steps = next(d for d in (9, 3, 1) if taps % d == 0)
    width = phases * chans
    kernel = functools.partial(
        _filter_kernel, steps=steps, count=count, chans=chans, phases=phases
    )
    return pl.pallas_call(
        kernel,
        grid=(taps // steps,),
        in_specs=[pl.BlockSpec((blocks, count, width), lambda q: (0, 0, 0))],
        out_specs=pl.BlockSpec((steps, phases * count, width), lambda q: (q, 0, 0)),
        out_shape=jax.ShapeDtypeStruct((taps, phases * count, width), placed.dtype),
    )(grouped)


def _build_filters(grouped_ref, filt_ref, base, steps_range, *, count, chans, phases):
    width = phases * chans
    for step in steps_range:
        joined = jnp.concatenate([grouped_ref[base + step], grouped_ref[base + step + 1]], axis=-1)
        joined = joined.astype(jnp.float32)
        parts = []
        for e in range(phases):
            cut = (phases - 1 - e) * chans
            moved = pltpu.roll(joined, 2 * width - cut, 1) if cut else joined
            parts.append(moved[:, :width])
        filt_ref[step] = jnp.transpose(jnp.concatenate(parts, axis=0)).astype(filt_ref.dtype)


def _accumulate(signal_ref, filt_ref, acc_ref, base, steps_range, *, steps, rows, width):
    n_blocks = signal_ref.shape[0]
    if n_blocks <= 8:
        band = signal_ref[:, pl.ds(base, rows + steps), :]
        total = acc_ref[...]
        for step in steps_range:
            window = band[:, step : step + rows].astype(filt_ref.dtype)
            window = window.reshape(n_blocks * rows, width)
            total += jnp.dot(window, filt_ref[step], preferred_element_type=jnp.float32)
        acc_ref[...] = total
    else:

        def body(g, carry):
            band = signal_ref[g, pl.ds(base, rows + steps), :]
            start = pl.multiple_of(g * rows, rows)
            total = acc_ref[pl.ds(start, rows), :]
            for step in steps_range:
                window = band[step : step + rows].astype(filt_ref.dtype)
                total += jnp.dot(window, filt_ref[step], preferred_element_type=jnp.float32)
            acc_ref[pl.ds(start, rows), :] = total
            return carry

        lax.fori_loop(0, n_blocks, body, 0)


def _corr_kernel(grouped_ref, signal_ref, out_ref, acc_ref, filt_ref, *, steps, last_steps, count, chans, phases, rows):
    width = phases * chans
    pid = pl.program_id(0)
    last = pl.num_programs(0) - 1
    base = pl.multiple_of(pid * steps, steps)
    build = functools.partial(_build_filters, count=count, chans=chans, phases=phases)
    accumulate = functools.partial(_accumulate, steps=steps, rows=rows, width=width)

    @pl.when(pid == 0)
    def _():
        acc_ref[...] = jnp.zeros_like(acc_ref)

    build(grouped_ref, filt_ref, base, range(last_steps))
    accumulate(signal_ref, filt_ref, acc_ref, base, range(last_steps))
    if last_steps < steps:

        @pl.when(pid < last)
        def _():
            build(grouped_ref, filt_ref, base, range(last_steps, steps))
            accumulate(signal_ref, filt_ref, acc_ref, base, range(last_steps, steps))

    @pl.when(pid == last)
    def _():
        out_ref[...] = acc_ref[...].reshape(out_ref.shape)


CORR_STEPS = 8


def corr_taps(padded_len, phases):
    taps = padded_len // phases + 1
    return taps, -(-taps // CORR_STEPS) * CORR_STEPS


def polyphase_rows(signal, phases, total_rows):
    chans, window = signal.shape
    rows = jnp.transpose(signal, (1, 0)).reshape(window // phases, phases * chans)
    return jnp.pad(rows, ((0, total_rows - window // phases), (0, 0)))


def correlate(placed, signal_rows, phases, lags):
    count, chans, padded_len = placed.shape
    n_blocks = signal_rows.shape[0]
    steps = CORR_STEPS
    real_taps, taps = corr_taps(padded_len, phases)
    last_steps = real_taps - (taps - steps)
    front = phases - 1
    n_groups = taps + 1
    rows = lags // phases
    width = phases * chans
    padded = jnp.pad(placed, ((0, 0), (0, 0), (front, n_groups * phases - padded_len - front)))
    grouped = jnp.transpose(padded, (0, 2, 1)).reshape(count, n_groups, width)
    grouped = jnp.transpose(grouped, (1, 0, 2))
    signal = signal_rows.astype(jnp.float32)
    kernel = functools.partial(
        _corr_kernel, steps=steps, last_steps=last_steps, count=count, chans=chans,
        phases=phases, rows=rows,
    )
    return pl.pallas_call(
        kernel,
        grid=(taps // steps,),
        in_specs=[
            pl.BlockSpec(grouped.shape, lambda q: (0, 0, 0)),
            pl.BlockSpec(signal.shape, lambda q: (0, 0, 0)),
        ],
        out_specs=pl.BlockSpec((n_blocks, rows, phases * count), lambda q: (0, 0, 0)),
        out_shape=jax.ShapeDtypeStruct((n_blocks, rows, phases * count), jnp.float32),
        scratch_shapes=[
            pltpu.VMEM((n_blocks * rows, phases * count), jnp.float32),
            pltpu.VMEM((steps, phases * count, width), placed.dtype),
        ],
    )(grouped, signal)


def shards(data, templates, stations, offsets, owner_map):
    n_tmpl = lax.axis_size("tmpl")
    ch_local = data.shape[0]
    window = data.shape[1]
    count = templates.shape[0]
    padded_len = templates.shape[2] + OFF
    lags = window - padded_len
    phases = PHASES
    signal = normalize_rows(data)
    n_chan = lax.axis_size("chan")
    me = lax.axis_index("chan")
    shaped = normalize_rows(templates)
    local_chan = stations % ch_local
    target = stations[:, 0] // (ch_local * n_tmpl)
    if n_chan <= 8:
        target = (me - target) % n_chan
    hit = local_chan[:, :, None] == jnp.arange(ch_local, dtype=jnp.int32)[None, None, :]
    ordered = jnp.einsum(
        "jki,jkl->jil", hit.astype(jnp.bfloat16), shaped, preferred_element_type=jnp.float32
    ).astype(jnp.bfloat16)
    ordered_shift = jnp.sum(jnp.where(hit, offsets[:, :, None], 0), axis=1)
    placed = place_moveout(ordered, ordered_shift, padded_len)
    _, taps = corr_taps(padded_len, phases)
    signal = polyphase_rows(signal, phases, taps + lags // phases)
    signal, placed = lax.optimization_barrier((signal, placed))
    if n_chan <= 8:
        pieces = [signal]
        for shift in range(1, n_chan):
            pairs = [(c, (c + shift) % n_chan) for c in range(n_chan)]
            pieces.append(lax.ppermute(signal, "chan", pairs))
        blocks = jnp.stack(pieces)
    else:
        blocks = lax.all_gather(signal, "chan", axis=0, tiled=False)
    n_blocks = blocks.shape[0]
    corr = correlate(placed, blocks, phases, lags)
    corr = corr.reshape(n_blocks, lags // phases, phases, count)
    pick = target[None, :] == jnp.arange(n_blocks, dtype=jnp.int32)[:, None]
    chosen = jnp.sum(jnp.where(pick[:, None, None, :], corr, 0.0), axis=0)
    partial_value = jnp.transpose(chosen, (2, 0, 1)).reshape(count, lags)
    partial_value = partial_value.astype(jnp.bfloat16)
    inverse = (
        jnp.zeros((count,), jnp.int32).at[owner_map[0]].set(jnp.arange(count, dtype=jnp.int32))
    )
    arranged = partial_value[inverse].reshape(n_tmpl, count // n_tmpl, lags)
    if n_tmpl <= 8:
        mine = lax.axis_index("tmpl")
        stack = jnp.take(arranged, mine, axis=0).astype(jnp.float32)
        for shift in range(1, n_tmpl):
            pairs = [(t, (t + shift) % n_tmpl) for t in range(n_tmpl)]
            outgoing = jnp.take(arranged, (mine + shift) % n_tmpl, axis=0)
            stack = stack + lax.ppermute(outgoing, "tmpl", pairs).astype(jnp.float32)
    else:
        received = lax.all_to_all(arranged, "tmpl", 0, 0, tiled=True)
        stack = jnp.sum(received.astype(jnp.float32), axis=0)
    power = jnp.mean(stack * stack, axis=1, keepdims=True)
    return stack * lax.rsqrt(power + eps)


def solution(mesh):
    in_specs = (
        P(("grp", "chan", "tmpl"), None),
        P(("grp", "chan"), "tmpl", None),
        P(("grp", "chan"), "tmpl"),
        P(("grp", "chan"), "tmpl"),
        P(("grp", "chan"), None),
    )
    out_specs = P(("grp", "chan", "tmpl"), None)
    return jax.shard_map(shards, mesh=mesh, in_specs=in_specs, out_specs=out_specs, check_vma=False)
```

```python
import functools

import jax
import jax.numpy as jnp
from jax import lax
from jax.experimental import pallas as pl
from jax.experimental.pallas import tpu as pltpu
from jax.sharding import PartitionSpec as P

OFF = 128
PHASES = 8


eps = 1e-05


def normalize_rows(values):
    values = values.astype(jnp.float32)
    centred = values - jnp.mean(values, axis=-1, keepdims=True)
    scale = lax.rsqrt(jnp.mean(centred * centred, axis=-1, keepdims=True) + eps)
    return (centred * scale).astype(jnp.bfloat16)


def place_moveout(rows, shifts, padded_len):
    extra = padded_len - rows.shape[-1]
    tail = jnp.zeros(rows.shape[:-1] + (extra,), rows.dtype)
    current = jnp.concatenate([rows, tail], axis=-1)
    for bit_number in range(OFF.bit_length()):
        step_len = 1 << bit_number
        lead = jnp.zeros(rows.shape[:-1] + (step_len,), rows.dtype)
        moved = jnp.concatenate([lead, current[..., : padded_len - step_len]], axis=-1)
        active = shifts >> bit_number & 1 == 1
        current = jnp.where(active[..., None], moved, current)
    return current


def _filter_kernel(grouped_ref, out_ref, *, steps, count, chans, phases):
    width = phases * chans
    first = pl.program_id(0) * steps
    for step in range(steps):
        lo = grouped_ref[first + step]
        hi = grouped_ref[first + step + 1]
        joined = jnp.concatenate([lo, hi], axis=-1)
        for e in range(phases):
            cut = (phases - 1 - e) * chans
            moved = pltpu.roll(joined, 2 * width - cut, 1) if cut else joined
            out_ref[step, e * count : (e + 1) * count, :] = moved[:, :width]


def polyphase_filters(placed, phases):
    count, chans, padded_len = placed.shape
    taps = padded_len // phases + 1
    front = phases - 1
    blocks = taps + 1
    padded = jnp.pad(placed, ((0, 0), (0, 0), (front, blocks * phases - padded_len - front)))
    grouped = jnp.transpose(padded, (0, 2, 1)).reshape(count, blocks, phases * chans)
    grouped = jnp.transpose(grouped, (1, 0, 2))
    steps = next(d for d in (9, 3, 1) if taps % d == 0)
    width = phases * chans
    kernel = functools.partial(
        _filter_kernel, steps=steps, count=count, chans=chans, phases=phases
    )
    return pl.pallas_call(
        kernel,
        grid=(taps // steps,),
        in_specs=[pl.BlockSpec((blocks, count, width), lambda q: (0, 0, 0))],
        out_specs=pl.BlockSpec((steps, phases * count, width), lambda q: (q, 0, 0)),
        out_shape=jax.ShapeDtypeStruct((taps, phases * count, width), placed.dtype),
    )(grouped)


def _corr_kernel(grouped_ref, signal_ref, out_ref, acc_ref, filt_ref, *, steps, count, chans, phases, rows):
    width = phases * chans
    pid = pl.program_id(0)

    @pl.when(pid == 0)
    def _():
        acc_ref[...] = jnp.zeros_like(acc_ref)

    base = pl.multiple_of(pid * steps, steps)
    for step in range(steps):
        joined = jnp.concatenate([grouped_ref[base + step], grouped_ref[base + step + 1]], axis=-1)
        joined = joined.astype(jnp.float32)
        parts = []
        for e in range(phases):
            cut = (phases - 1 - e) * chans
            moved = pltpu.roll(joined, 2 * width - cut, 1) if cut else joined
            parts.append(moved[:, :width])
        filt_ref[step] = jnp.transpose(jnp.concatenate(parts, axis=0)).astype(filt_ref.dtype)

    n_blocks = signal_ref.shape[0]
    if n_blocks <= 8:
        band = signal_ref[:, pl.ds(base, rows + steps), :]
        total = acc_ref[...]
        for step in range(steps):
            window = band[:, step : step + rows].astype(filt_ref.dtype)
            window = window.reshape(n_blocks * rows, width)
            total += jnp.dot(window, filt_ref[step], preferred_element_type=jnp.float32)
        acc_ref[...] = total
    else:

        def accumulate(g, carry):
            band = signal_ref[g, pl.ds(base, rows + steps), :]
            start = pl.multiple_of(g * rows, rows)
            total = acc_ref[pl.ds(start, rows), :]
            for step in range(steps):
                window = band[step : step + rows].astype(filt_ref.dtype)
                total += jnp.dot(window, filt_ref[step], preferred_element_type=jnp.float32)
            acc_ref[pl.ds(start, rows), :] = total
            return carry

        lax.fori_loop(0, n_blocks, accumulate, 0)

    @pl.when(pid == pl.num_programs(0) - 1)
    def _():
        out_ref[...] = acc_ref[...].reshape(out_ref.shape)


CORR_STEPS = 8


def corr_taps(padded_len, phases):
    taps = padded_len // phases + 1
    return taps, -(-taps // CORR_STEPS) * CORR_STEPS


def polyphase_rows(signal, phases, total_rows):
    chans, window = signal.shape
    rows = jnp.transpose(signal, (1, 0)).reshape(window // phases, phases * chans)
    return jnp.pad(rows, ((0, total_rows - window // phases), (0, 0)))


def correlate(placed, signal_rows, phases, lags):
    count, chans, padded_len = placed.shape
    n_blocks = signal_rows.shape[0]
    steps = CORR_STEPS
    _, taps = corr_taps(padded_len, phases)
    front = phases - 1
    n_groups = taps + 1
    rows = lags // phases
    width = phases * chans
    padded = jnp.pad(placed, ((0, 0), (0, 0), (front, n_groups * phases - padded_len - front)))
    grouped = jnp.transpose(padded, (0, 2, 1)).reshape(count, n_groups, width)
    grouped = jnp.transpose(grouped, (1, 0, 2))
    signal = signal_rows.astype(jnp.float32)
    kernel = functools.partial(
        _corr_kernel, steps=steps, count=count, chans=chans, phases=phases, rows=rows
    )
    return pl.pallas_call(
        kernel,
        grid=(taps // steps,),
        in_specs=[
            pl.BlockSpec(grouped.shape, lambda q: (0, 0, 0)),
            pl.BlockSpec(signal.shape, lambda q: (0, 0, 0)),
        ],
        out_specs=pl.BlockSpec((n_blocks, rows, phases * count), lambda q: (0, 0, 0)),
        out_shape=jax.ShapeDtypeStruct((n_blocks, rows, phases * count), jnp.float32),
        scratch_shapes=[
            pltpu.VMEM((n_blocks * rows, phases * count), jnp.float32),
            pltpu.VMEM((steps, phases * count, width), placed.dtype),
        ],
    )(grouped, signal)


def shards(data, templates, stations, offsets, owner_map):
    n_tmpl = lax.axis_size("tmpl")
    ch_local = data.shape[0]
    window = data.shape[1]
    count = templates.shape[0]
    padded_len = templates.shape[2] + OFF
    lags = window - padded_len
    phases = PHASES
    signal = normalize_rows(data)
    n_chan = lax.axis_size("chan")
    me = lax.axis_index("chan")
    shaped = normalize_rows(templates)
    local_chan = stations % ch_local
    target = stations[:, 0] // (ch_local * n_tmpl)
    if n_chan <= 8:
        target = (me - target) % n_chan
    hit = local_chan[:, :, None] == jnp.arange(ch_local, dtype=jnp.int32)[None, None, :]
    ordered = jnp.einsum(
        "jki,jkl->jil", hit.astype(jnp.bfloat16), shaped, preferred_element_type=jnp.float32
    ).astype(jnp.bfloat16)
    ordered_shift = jnp.sum(jnp.where(hit, offsets[:, :, None], 0), axis=1)
    placed = place_moveout(ordered, ordered_shift, padded_len)
    _, taps = corr_taps(padded_len, phases)
    signal = polyphase_rows(signal, phases, taps + lags // phases)
    signal, placed = lax.optimization_barrier((signal, placed))
    if n_chan <= 8:
        pieces = [signal]
        for shift in range(1, n_chan):
            pairs = [(c, (c + shift) % n_chan) for c in range(n_chan)]
            pieces.append(lax.ppermute(signal, "chan", pairs))
        blocks = jnp.stack(pieces)
    else:
        blocks = lax.all_gather(signal, "chan", axis=0, tiled=False)
    n_blocks = blocks.shape[0]
    corr = correlate(placed, blocks, phases, lags)
    corr = corr.reshape(n_blocks, lags // phases, phases, count)
    pick = target[None, :] == jnp.arange(n_blocks, dtype=jnp.int32)[:, None]
    chosen = jnp.sum(jnp.where(pick[:, None, None, :], corr, 0.0), axis=0)
    partial_value = jnp.transpose(chosen, (2, 0, 1)).reshape(count, lags)
    partial_value = partial_value.astype(jnp.bfloat16)
    inverse = (
        jnp.zeros((count,), jnp.int32).at[owner_map[0]].set(jnp.arange(count, dtype=jnp.int32))
    )
    arranged = partial_value[inverse].reshape(n_tmpl, count // n_tmpl, lags)
    if n_tmpl <= 8:
        mine = lax.axis_index("tmpl")
        stack = jnp.take(arranged, mine, axis=0).astype(jnp.float32)
        for shift in range(1, n_tmpl):
            pairs = [(t, (t + shift) % n_tmpl) for t in range(n_tmpl)]
            outgoing = jnp.take(arranged, (mine + shift) % n_tmpl, axis=0)
            stack = stack + lax.ppermute(outgoing, "tmpl", pairs).astype(jnp.float32)
    else:
        received = lax.all_to_all(arranged, "tmpl", 0, 0, tiled=True)
        stack = jnp.sum(received.astype(jnp.float32), axis=0)
    power = jnp.mean(stack * stack, axis=1, keepdims=True)
    return stack * lax.rsqrt(power + eps)


def solution(mesh):
    in_specs = (
        P(("grp", "chan", "tmpl"), None),
        P(("grp", "chan"), "tmpl", None),
        P(("grp", "chan"), "tmpl"),
        P(("grp", "chan"), "tmpl"),
        P(("grp", "chan"), None),
    )
    out_specs = P(("grp", "chan", "tmpl"), None)
    return jax.shard_map(shards, mesh=mesh, in_specs=in_specs, out_specs=out_specs, check_vma=False)
```

```python
import functools

import jax
import jax.numpy as jnp
from jax import lax
from jax.experimental import pallas as pl
from jax.experimental.pallas import tpu as pltpu
from jax.sharding import PartitionSpec as P

OFF = 128
PHASES = 8


eps = 1e-05


def normalize_rows(values):
    values = values.astype(jnp.float32)
    centred = values - jnp.mean(values, axis=-1, keepdims=True)
    scale = lax.rsqrt(jnp.mean(centred * centred, axis=-1, keepdims=True) + eps)
    return (centred * scale).astype(jnp.bfloat16)


def place_moveout(rows, shifts, padded_len):
    extra = padded_len - rows.shape[-1]
    tail = jnp.zeros(rows.shape[:-1] + (extra,), rows.dtype)
    current = jnp.concatenate([rows, tail], axis=-1)
    for bit_number in range(OFF.bit_length()):
        step_len = 1 << bit_number
        lead = jnp.zeros(rows.shape[:-1] + (step_len,), rows.dtype)
        moved = jnp.concatenate([lead, current[..., : padded_len - step_len]], axis=-1)
        active = shifts >> bit_number & 1 == 1
        current = jnp.where(active[..., None], moved, current)
    return current


def _filter_kernel(grouped_ref, out_ref, *, steps, count, chans, phases):
    width = phases * chans
    first = pl.program_id(0) * steps
    for step in range(steps):
        lo = grouped_ref[first + step]
        hi = grouped_ref[first + step + 1]
        joined = jnp.concatenate([lo, hi], axis=-1)
        for e in range(phases):
            cut = (phases - 1 - e) * chans
            moved = pltpu.roll(joined, 2 * width - cut, 1) if cut else joined
            out_ref[step, e * count : (e + 1) * count, :] = moved[:, :width]


def polyphase_filters(placed, phases):
    count, chans, padded_len = placed.shape
    taps = padded_len // phases + 1
    front = phases - 1
    blocks = taps + 1
    padded = jnp.pad(placed, ((0, 0), (0, 0), (front, blocks * phases - padded_len - front)))
    grouped = jnp.transpose(padded, (0, 2, 1)).reshape(count, blocks, phases * chans)
    grouped = jnp.transpose(grouped, (1, 0, 2))
    steps = next(d for d in (9, 3, 1) if taps % d == 0)
    width = phases * chans
    kernel = functools.partial(
        _filter_kernel, steps=steps, count=count, chans=chans, phases=phases
    )
    return pl.pallas_call(
        kernel,
        grid=(taps // steps,),
        in_specs=[pl.BlockSpec((blocks, count, width), lambda q: (0, 0, 0))],
        out_specs=pl.BlockSpec((steps, phases * count, width), lambda q: (q, 0, 0)),
        out_shape=jax.ShapeDtypeStruct((taps, phases * count, width), placed.dtype),
    )(grouped)


def _corr_kernel(grouped_ref, signal_ref, mask_ref, out_ref, acc_ref, filt_ref, *, steps, count, chans, phases, rows):
    width = phases * chans
    pid = pl.program_id(0)

    @pl.when(pid == 0)
    def _():
        acc_ref[...] = jnp.zeros_like(acc_ref)

    base = pl.multiple_of(pid * steps, steps)
    for step in range(steps):
        joined = jnp.concatenate([grouped_ref[base + step], grouped_ref[base + step + 1]], axis=-1)
        joined = joined.astype(jnp.float32)
        parts = []
        for e in range(phases):
            cut = (phases - 1 - e) * chans
            moved = pltpu.roll(joined, 2 * width - cut, 1) if cut else joined
            parts.append(moved[:, :width])
        filt_ref[step] = jnp.transpose(jnp.concatenate(parts, axis=0)).astype(filt_ref.dtype)

    n_blocks = signal_ref.shape[0]
    if n_blocks <= 8:
        band = signal_ref[:, pl.ds(base, rows + steps), :]
        total = acc_ref[...]
        for step in range(steps):
            window = band[:, step : step + rows].astype(filt_ref.dtype)
            window = window.reshape(n_blocks * rows, width)
            total += jnp.dot(window, filt_ref[step], preferred_element_type=jnp.float32)
        acc_ref[...] = total
    else:

        def accumulate(g, carry):
            band = signal_ref[g, pl.ds(base, rows + steps), :]
            start = pl.multiple_of(g * rows, rows)
            total = acc_ref[pl.ds(start, rows), :]
            for step in range(steps):
                window = band[step : step + rows].astype(filt_ref.dtype)
                total += jnp.dot(window, filt_ref[step], preferred_element_type=jnp.float32)
            acc_ref[pl.ds(start, rows), :] = total
            return carry

        lax.fori_loop(0, n_blocks, accumulate, 0)

    @pl.when(pid == pl.num_programs(0) - 1)
    def _():
        def pick(g, carry):
            start = pl.multiple_of(g * rows, rows)
            return carry + acc_ref[pl.ds(start, rows), :] * mask_ref[g]

        out_ref[...] = lax.fori_loop(0, n_blocks, pick, jnp.zeros(out_ref.shape, jnp.float32))


CORR_STEPS = 8


def corr_taps(padded_len, phases):
    taps = padded_len // phases + 1
    return taps, -(-taps // CORR_STEPS) * CORR_STEPS


def polyphase_rows(signal, phases, total_rows):
    chans, window = signal.shape
    rows = jnp.transpose(signal, (1, 0)).reshape(window // phases, phases * chans)
    return jnp.pad(rows, ((0, total_rows - window // phases), (0, 0)))


def correlate(placed, signal_rows, target, phases, lags):
    count, chans, padded_len = placed.shape
    n_blocks = signal_rows.shape[0]
    steps = CORR_STEPS
    _, taps = corr_taps(padded_len, phases)
    front = phases - 1
    n_groups = taps + 1
    rows = lags // phases
    width = phases * chans
    padded = jnp.pad(placed, ((0, 0), (0, 0), (front, n_groups * phases - padded_len - front)))
    grouped = jnp.transpose(padded, (0, 2, 1)).reshape(count, n_groups, width)
    grouped = jnp.transpose(grouped, (1, 0, 2))
    signal = signal_rows.astype(jnp.float32)
    hit = target[None, :] == jnp.arange(n_blocks, dtype=jnp.int32)[:, None]
    mask = jnp.tile(hit.astype(jnp.float32), (1, phases))[:, None, :]
    kernel = functools.partial(
        _corr_kernel, steps=steps, count=count, chans=chans, phases=phases, rows=rows
    )
    return pl.pallas_call(
        kernel,
        grid=(taps // steps,),
        in_specs=[
            pl.BlockSpec(grouped.shape, lambda q: (0, 0, 0)),
            pl.BlockSpec(signal.shape, lambda q: (0, 0, 0)),
            pl.BlockSpec(mask.shape, lambda q: (0, 0, 0)),
        ],
        out_specs=pl.BlockSpec((rows, phases * count), lambda q: (0, 0)),
        out_shape=jax.ShapeDtypeStruct((rows, phases * count), jnp.float32),
        scratch_shapes=[
            pltpu.VMEM((n_blocks * rows, phases * count), jnp.float32),
            pltpu.VMEM((steps, phases * count, width), placed.dtype),
        ],
    )(grouped, signal, mask)


def shards(data, templates, stations, offsets, owner_map):
    n_tmpl = lax.axis_size("tmpl")
    ch_local = data.shape[0]
    window = data.shape[1]
    count = templates.shape[0]
    padded_len = templates.shape[2] + OFF
    lags = window - padded_len
    phases = PHASES
    signal = normalize_rows(data)
    n_chan = lax.axis_size("chan")
    me = lax.axis_index("chan")
    shaped = normalize_rows(templates)
    local_chan = stations % ch_local
    target = stations[:, 0] // (ch_local * n_tmpl)
    if n_chan <= 8:
        target = (me - target) % n_chan
    hit = local_chan[:, :, None] == jnp.arange(ch_local, dtype=jnp.int32)[None, None, :]
    ordered = jnp.einsum(
        "jki,jkl->jil", hit.astype(jnp.bfloat16), shaped, preferred_element_type=jnp.float32
    ).astype(jnp.bfloat16)
    ordered_shift = jnp.sum(jnp.where(hit, offsets[:, :, None], 0), axis=1)
    placed = place_moveout(ordered, ordered_shift, padded_len)
    _, taps = corr_taps(padded_len, phases)
    signal = polyphase_rows(signal, phases, taps + lags // phases)
    signal, placed = lax.optimization_barrier((signal, placed))
    if n_chan <= 8:
        pieces = [signal]
        for shift in range(1, n_chan):
            pairs = [(c, (c + shift) % n_chan) for c in range(n_chan)]
            pieces.append(lax.ppermute(signal, "chan", pairs))
        blocks = jnp.stack(pieces)
    else:
        blocks = lax.all_gather(signal, "chan", axis=0, tiled=False)
    n_blocks = blocks.shape[0]
    corr = correlate(placed, blocks, target, phases, lags)
    chosen = corr.reshape(lags // phases, phases, count)
    partial_value = jnp.transpose(chosen, (2, 0, 1)).reshape(count, lags)
    partial_value = partial_value.astype(jnp.bfloat16)
    inverse = (
        jnp.zeros((count,), jnp.int32).at[owner_map[0]].set(jnp.arange(count, dtype=jnp.int32))
    )
    arranged = partial_value[inverse].reshape(n_tmpl, count // n_tmpl, lags)
    if n_tmpl <= 8:
        mine = lax.axis_index("tmpl")
        stack = jnp.take(arranged, mine, axis=0).astype(jnp.float32)
        for shift in range(1, n_tmpl):
            pairs = [(t, (t + shift) % n_tmpl) for t in range(n_tmpl)]
            outgoing = jnp.take(arranged, (mine + shift) % n_tmpl, axis=0)
            stack = stack + lax.ppermute(outgoing, "tmpl", pairs).astype(jnp.float32)
    else:
        received = lax.all_to_all(arranged, "tmpl", 0, 0, tiled=True)
        stack = jnp.sum(received.astype(jnp.float32), axis=0)
    power = jnp.mean(stack * stack, axis=1, keepdims=True)
    return stack * lax.rsqrt(power + eps)


def solution(mesh):
    in_specs = (
        P(("grp", "chan", "tmpl"), None),
        P(("grp", "chan"), "tmpl", None),
        P(("grp", "chan"), "tmpl"),
        P(("grp", "chan"), "tmpl"),
        P(("grp", "chan"), None),
    )
    out_specs = P(("grp", "chan", "tmpl"), None)
    return jax.shard_map(shards, mesh=mesh, in_specs=in_specs, out_specs=out_specs, check_vma=False)
```

```python
import functools

import jax
import jax.numpy as jnp
from jax import lax
from jax.experimental import pallas as pl
from jax.experimental.pallas import tpu as pltpu
from jax.sharding import PartitionSpec as P

OFF = 128
PHASES = 8


eps = 1e-05


def normalize_rows(values):
    values = values.astype(jnp.float32)
    centred = values - jnp.mean(values, axis=-1, keepdims=True)
    scale = lax.rsqrt(jnp.mean(centred * centred, axis=-1, keepdims=True) + eps)
    return (centred * scale).astype(jnp.bfloat16)


def place_moveout(rows, shifts, padded_len):
    extra = padded_len - rows.shape[-1]
    tail = jnp.zeros(rows.shape[:-1] + (extra,), rows.dtype)
    current = jnp.concatenate([rows, tail], axis=-1)
    for bit_number in range(OFF.bit_length()):
        step_len = 1 << bit_number
        lead = jnp.zeros(rows.shape[:-1] + (step_len,), rows.dtype)
        moved = jnp.concatenate([lead, current[..., : padded_len - step_len]], axis=-1)
        active = shifts >> bit_number & 1 == 1
        current = jnp.where(active[..., None], moved, current)
    return current


def _filter_kernel(grouped_ref, out_ref, *, steps, count, chans, phases):
    width = phases * chans
    first = pl.program_id(0) * steps
    for step in range(steps):
        lo = grouped_ref[first + step]
        hi = grouped_ref[first + step + 1]
        joined = jnp.concatenate([lo, hi], axis=-1)
        for e in range(phases):
            cut = (phases - 1 - e) * chans
            moved = pltpu.roll(joined, 2 * width - cut, 1) if cut else joined
            out_ref[step, e * count : (e + 1) * count, :] = moved[:, :width]


def polyphase_filters(placed, phases):
    count, chans, padded_len = placed.shape
    taps = padded_len // phases + 1
    front = phases - 1
    blocks = taps + 1
    padded = jnp.pad(placed, ((0, 0), (0, 0), (front, blocks * phases - padded_len - front)))
    grouped = jnp.transpose(padded, (0, 2, 1)).reshape(count, blocks, phases * chans)
    grouped = jnp.transpose(grouped, (1, 0, 2))
    steps = next(d for d in (9, 3, 1) if taps % d == 0)
    width = phases * chans
    kernel = functools.partial(
        _filter_kernel, steps=steps, count=count, chans=chans, phases=phases
    )
    return pl.pallas_call(
        kernel,
        grid=(taps // steps,),
        in_specs=[pl.BlockSpec((blocks, count, width), lambda q: (0, 0, 0))],
        out_specs=pl.BlockSpec((steps, phases * count, width), lambda q: (q, 0, 0)),
        out_shape=jax.ShapeDtypeStruct((taps, phases * count, width), placed.dtype),
    )(grouped)


def _corr_kernel(grouped_ref, signal_ref, out_ref, acc_ref, filt_ref, *, steps, extra_taps, count, chans, phases, rows):
    width = phases * chans
    pid = pl.program_id(0)

    @pl.when(pid == 0)
    def _():
        acc_ref[...] = jnp.zeros_like(acc_ref)

    base = pl.multiple_of(pid * steps, steps)
    for step in range(steps):
        joined = jnp.concatenate([grouped_ref[base + step], grouped_ref[base + step + 1]], axis=-1)
        joined = joined.astype(jnp.float32)
        parts = []
        for e in range(phases):
            cut = (phases - 1 - e) * chans
            moved = pltpu.roll(joined, 2 * width - cut, 1) if cut else joined
            parts.append(moved[:, :width])
        filt_ref[step] = jnp.transpose(jnp.concatenate(parts, axis=0)).astype(filt_ref.dtype)

    n_blocks = signal_ref.shape[0]
    if n_blocks <= 8:
        band = signal_ref[:, pl.ds(base, rows + steps), :]
        total = acc_ref[...]
        for step in range(steps):
            window = band[:, step : step + rows].astype(filt_ref.dtype)
            window = window.reshape(n_blocks * rows, width)
            total += jnp.dot(window, filt_ref[step], preferred_element_type=jnp.float32)
        acc_ref[...] = total
    else:

        def accumulate(g, carry):
            band = signal_ref[g, pl.ds(base, rows + steps), :]
            start = pl.multiple_of(g * rows, rows)
            total = acc_ref[pl.ds(start, rows), :]
            for step in range(steps):
                window = band[step : step + rows].astype(filt_ref.dtype)
                total += jnp.dot(window, filt_ref[step], preferred_element_type=jnp.float32)
            acc_ref[pl.ds(start, rows), :] = total
            return carry

        lax.fori_loop(0, n_blocks, accumulate, 0)

    @pl.when(pid == pl.num_programs(0) - 1)
    def _():
        for extra in range(extra_taps):
            q = (pid + 1) * steps + extra
            joined = jnp.concatenate([grouped_ref[q], grouped_ref[q + 1]], axis=-1)
            joined = joined.astype(jnp.float32)
            parts = []
            for e in range(phases):
                cut = (phases - 1 - e) * chans
                moved = pltpu.roll(joined, 2 * width - cut, 1) if cut else joined
                parts.append(moved[:, :width])
            filt = jnp.transpose(jnp.concatenate(parts, axis=0)).astype(filt_ref.dtype)
            start = pl.multiple_of((pid + 1) * steps, steps)

            def tail(g, carry):
                window = signal_ref[g, pl.ds(start, rows + steps), :][extra : extra + rows]
                lo = pl.multiple_of(g * rows, rows)
                acc_ref[pl.ds(lo, rows), :] += jnp.dot(
                    window.astype(filt.dtype), filt, preferred_element_type=jnp.float32
                )
                return carry

            lax.fori_loop(0, n_blocks, tail, 0)
        out_ref[...] = acc_ref[...].reshape(out_ref.shape)


CORR_STEPS = 8


def corr_taps(padded_len, phases):
    taps = padded_len // phases + 1
    main = taps // CORR_STEPS * CORR_STEPS
    return taps - main, main + CORR_STEPS


def polyphase_rows(signal, phases, total_rows):
    chans, window = signal.shape
    rows = jnp.transpose(signal, (1, 0)).reshape(window // phases, phases * chans)
    return jnp.pad(rows, ((0, total_rows - window // phases), (0, 0)))


def correlate(placed, signal_rows, phases, lags):
    count, chans, padded_len = placed.shape
    n_blocks = signal_rows.shape[0]
    steps = CORR_STEPS
    extra_taps, span = corr_taps(padded_len, phases)
    taps = span - steps
    front = phases - 1
    n_groups = taps + extra_taps + 1
    rows = lags // phases
    width = phases * chans
    padded = jnp.pad(placed, ((0, 0), (0, 0), (front, n_groups * phases - padded_len - front)))
    grouped = jnp.transpose(padded, (0, 2, 1)).reshape(count, n_groups, width)
    grouped = jnp.transpose(grouped, (1, 0, 2))
    signal = signal_rows.astype(jnp.float32)
    kernel = functools.partial(
        _corr_kernel, steps=steps, extra_taps=extra_taps, count=count, chans=chans,
        phases=phases, rows=rows,
    )
    return pl.pallas_call(
        kernel,
        grid=(taps // steps,),
        in_specs=[
            pl.BlockSpec(grouped.shape, lambda q: (0, 0, 0)),
            pl.BlockSpec(signal.shape, lambda q: (0, 0, 0)),
        ],
        out_specs=pl.BlockSpec((n_blocks, rows, phases * count), lambda q: (0, 0, 0)),
        out_shape=jax.ShapeDtypeStruct((n_blocks, rows, phases * count), jnp.float32),
        scratch_shapes=[
            pltpu.VMEM((n_blocks * rows, phases * count), jnp.float32),
            pltpu.VMEM((steps, phases * count, width), placed.dtype),
        ],
    )(grouped, signal)


def shards(data, templates, stations, offsets, owner_map):
    n_tmpl = lax.axis_size("tmpl")
    ch_local = data.shape[0]
    window = data.shape[1]
    count = templates.shape[0]
    padded_len = templates.shape[2] + OFF
    lags = window - padded_len
    phases = PHASES
    signal = normalize_rows(data)
    n_chan = lax.axis_size("chan")
    me = lax.axis_index("chan")
    shaped = normalize_rows(templates)
    local_chan = stations % ch_local
    target = stations[:, 0] // (ch_local * n_tmpl)
    if n_chan <= 8:
        target = (me - target) % n_chan
    hit = local_chan[:, :, None] == jnp.arange(ch_local, dtype=jnp.int32)[None, None, :]
    ordered = jnp.einsum(
        "jki,jkl->jil", hit.astype(jnp.bfloat16), shaped, preferred_element_type=jnp.float32
    ).astype(jnp.bfloat16)
    ordered_shift = jnp.sum(jnp.where(hit, offsets[:, :, None], 0), axis=1)
    placed = place_moveout(ordered, ordered_shift, padded_len)
    _, span = corr_taps(padded_len, phases)
    signal = polyphase_rows(signal, phases, span + lags // phases)
    signal, placed = lax.optimization_barrier((signal, placed))
    if n_chan <= 8:
        pieces = [signal]
        for shift in range(1, n_chan):
            pairs = [(c, (c + shift) % n_chan) for c in range(n_chan)]
            pieces.append(lax.ppermute(signal, "chan", pairs))
        blocks = jnp.stack(pieces)
    else:
        blocks = lax.all_gather(signal, "chan", axis=0, tiled=False)
    n_blocks = blocks.shape[0]
    corr = correlate(placed, blocks, phases, lags)
    corr = corr.reshape(n_blocks, lags // phases, phases, count)
    pick = target[None, :] == jnp.arange(n_blocks, dtype=jnp.int32)[:, None]
    chosen = jnp.sum(jnp.where(pick[:, None, None, :], corr, 0.0), axis=0)
    partial_value = jnp.transpose(chosen, (2, 0, 1)).reshape(count, lags)
    partial_value = partial_value.astype(jnp.bfloat16)
    inverse = (
        jnp.zeros((count,), jnp.int32).at[owner_map[0]].set(jnp.arange(count, dtype=jnp.int32))
    )
    arranged = partial_value[inverse].reshape(n_tmpl, count // n_tmpl, lags)
    if n_tmpl <= 8:
        mine = lax.axis_index("tmpl")
        stack = jnp.take(arranged, mine, axis=0).astype(jnp.float32)
        for shift in range(1, n_tmpl):
            pairs = [(t, (t + shift) % n_tmpl) for t in range(n_tmpl)]
            outgoing = jnp.take(arranged, (mine + shift) % n_tmpl, axis=0)
            stack = stack + lax.ppermute(outgoing, "tmpl", pairs).astype(jnp.float32)
    else:
        received = lax.all_to_all(arranged, "tmpl", 0, 0, tiled=True)
        stack = jnp.sum(received.astype(jnp.float32), axis=0)
    power = jnp.mean(stack * stack, axis=1, keepdims=True)
    return stack * lax.rsqrt(power + eps)


def solution(mesh):
    in_specs = (
        P(("grp", "chan", "tmpl"), None),
        P(("grp", "chan"), "tmpl", None),
        P(("grp", "chan"), "tmpl"),
        P(("grp", "chan"), "tmpl"),
        P(("grp", "chan"), None),
    )
    out_specs = P(("grp", "chan", "tmpl"), None)
    return jax.shard_map(shards, mesh=mesh, in_specs=in_specs, out_specs=out_specs, check_vma=False)
```

```python
import functools

import jax
import jax.numpy as jnp
from jax import lax
from jax.experimental import pallas as pl
from jax.experimental.pallas import tpu as pltpu
from jax.sharding import PartitionSpec as P

OFF = 128
PHASES = 8


eps = 1e-05


def normalize_rows(values):
    values = values.astype(jnp.float32)
    centred = values - jnp.mean(values, axis=-1, keepdims=True)
    scale = lax.rsqrt(jnp.mean(centred * centred, axis=-1, keepdims=True) + eps)
    return (centred * scale).astype(jnp.bfloat16)


def place_moveout(rows, shifts, padded_len):
    extra = padded_len - rows.shape[-1]
    tail = jnp.zeros(rows.shape[:-1] + (extra,), rows.dtype)
    current = jnp.concatenate([rows, tail], axis=-1)
    for bit_number in range(OFF.bit_length()):
        step_len = 1 << bit_number
        lead = jnp.zeros(rows.shape[:-1] + (step_len,), rows.dtype)
        moved = jnp.concatenate([lead, current[..., : padded_len - step_len]], axis=-1)
        active = shifts >> bit_number & 1 == 1
        current = jnp.where(active[..., None], moved, current)
    return current


def _filter_kernel(grouped_ref, out_ref, *, steps, count, chans, phases):
    width = phases * chans
    first = pl.program_id(0) * steps
    for step in range(steps):
        lo = grouped_ref[first + step]
        hi = grouped_ref[first + step + 1]
        joined = jnp.concatenate([lo, hi], axis=-1)
        for e in range(phases):
            cut = (phases - 1 - e) * chans
            moved = pltpu.roll(joined, 2 * width - cut, 1) if cut else joined
            out_ref[step, e * count : (e + 1) * count, :] = moved[:, :width]


def polyphase_filters(placed, phases):
    count, chans, padded_len = placed.shape
    taps = padded_len // phases + 1
    front = phases - 1
    blocks = taps + 1
    padded = jnp.pad(placed, ((0, 0), (0, 0), (front, blocks * phases - padded_len - front)))
    grouped = jnp.transpose(padded, (0, 2, 1)).reshape(count, blocks, phases * chans)
    grouped = jnp.transpose(grouped, (1, 0, 2))
    steps = next(d for d in (9, 3, 1) if taps % d == 0)
    width = phases * chans
    kernel = functools.partial(
        _filter_kernel, steps=steps, count=count, chans=chans, phases=phases
    )
    return pl.pallas_call(
        kernel,
        grid=(taps // steps,),
        in_specs=[pl.BlockSpec((blocks, count, width), lambda q: (0, 0, 0))],
        out_specs=pl.BlockSpec((steps, phases * count, width), lambda q: (q, 0, 0)),
        out_shape=jax.ShapeDtypeStruct((taps, phases * count, width), placed.dtype),
    )(grouped)


def _corr_kernel(grouped_ref, signal_ref, out_ref, acc_ref, filt_ref, *, steps, extra_taps, count, chans, phases, rows):
    width = phases * chans
    pid = pl.program_id(0)

    @pl.when(pid == 0)
    def _():
        acc_ref[...] = jnp.zeros_like(acc_ref)

    base = pl.multiple_of(pid * steps, steps)
    for step in range(steps):
        joined = jnp.concatenate([grouped_ref[base + step], grouped_ref[base + step + 1]], axis=-1)
        joined = joined.astype(jnp.float32)
        parts = []
        for e in range(phases):
            cut = (phases - 1 - e) * chans
            moved = pltpu.roll(joined, 2 * width - cut, 1) if cut else joined
            parts.append(moved[:, :width])
        filt_ref[step] = jnp.transpose(jnp.concatenate(parts, axis=0)).astype(filt_ref.dtype)

    n_blocks = signal_ref.shape[0]
    if n_blocks <= 8:
        band = signal_ref[:, pl.ds(base, rows + steps), :]
        total = acc_ref[...]
        for step in range(steps):
            window = band[:, step : step + rows].astype(filt_ref.dtype)
            window = window.reshape(n_blocks * rows, width)
            total += jnp.dot(window, filt_ref[step], preferred_element_type=jnp.float32)
        acc_ref[...] = total
    else:

        def accumulate(g, carry):
            band = signal_ref[g, pl.ds(base, rows + steps), :]
            start = pl.multiple_of(g * rows, rows)
            total = acc_ref[pl.ds(start, rows), :]
            for step in range(steps):
                window = band[step : step + rows].astype(filt_ref.dtype)
                total += jnp.dot(window, filt_ref[step], preferred_element_type=jnp.float32)
            acc_ref[pl.ds(start, rows), :] = total
            return carry

        lax.fori_loop(0, n_blocks, accumulate, 0)

    @pl.when(pid == pl.num_programs(0) - 1)
    def _():
        for extra in range(extra_taps):
            q = (pid + 1) * steps + extra
            joined = jnp.concatenate([grouped_ref[q], grouped_ref[q + 1]], axis=-1)
            joined = joined.astype(jnp.float32)
            parts = []
            for e in range(phases):
                cut = (phases - 1 - e) * chans
                moved = pltpu.roll(joined, 2 * width - cut, 1) if cut else joined
                parts.append(moved[:, :width])
            filt = jnp.transpose(jnp.concatenate(parts, axis=0)).astype(filt_ref.dtype)
            start = pl.multiple_of((pid + 1) * steps, steps)

            def tail(g, carry):
                window = signal_ref[g, pl.ds(start, rows + steps), :][extra : extra + rows]
                lo = pl.multiple_of(g * rows, rows)
                acc_ref[pl.ds(lo, rows), :] += jnp.dot(
                    window.astype(filt.dtype), filt, preferred_element_type=jnp.float32
                )
                return carry

            lax.fori_loop(0, n_blocks, tail, 0)
        out_ref[...] = acc_ref[...].reshape(out_ref.shape)


CORR_STEPS = 16


def corr_taps(padded_len, phases):
    taps = padded_len // phases + 1
    main = taps // CORR_STEPS * CORR_STEPS
    return taps - main, main + CORR_STEPS


def polyphase_rows(signal, phases, total_rows):
    chans, window = signal.shape
    rows = jnp.transpose(signal, (1, 0)).reshape(window // phases, phases * chans)
    return jnp.pad(rows, ((0, total_rows - window // phases), (0, 0)))


def correlate(placed, signal_rows, phases, lags):
    count, chans, padded_len = placed.shape
    n_blocks = signal_rows.shape[0]
    steps = CORR_STEPS
    extra_taps, span = corr_taps(padded_len, phases)
    taps = span - steps
    front = phases - 1
    n_groups = taps + extra_taps + 1
    rows = lags // phases
    width = phases * chans
    padded = jnp.pad(placed, ((0, 0), (0, 0), (front, n_groups * phases - padded_len - front)))
    grouped = jnp.transpose(padded, (0, 2, 1)).reshape(count, n_groups, width)
    grouped = jnp.transpose(grouped, (1, 0, 2))
    signal = signal_rows.astype(jnp.float32)
    kernel = functools.partial(
        _corr_kernel, steps=steps, extra_taps=extra_taps, count=count, chans=chans,
        phases=phases, rows=rows,
    )
    return pl.pallas_call(
        kernel,
        grid=(taps // steps,),
        in_specs=[
            pl.BlockSpec(grouped.shape, lambda q: (0, 0, 0)),
            pl.BlockSpec(signal.shape, lambda q: (0, 0, 0)),
        ],
        out_specs=pl.BlockSpec((n_blocks, rows, phases * count), lambda q: (0, 0, 0)),
        out_shape=jax.ShapeDtypeStruct((n_blocks, rows, phases * count), jnp.float32),
        scratch_shapes=[
            pltpu.VMEM((n_blocks * rows, phases * count), jnp.float32),
            pltpu.VMEM((steps, phases * count, width), placed.dtype),
        ],
    )(grouped, signal)


def shards(data, templates, stations, offsets, owner_map):
    n_tmpl = lax.axis_size("tmpl")
    ch_local = data.shape[0]
    window = data.shape[1]
    count = templates.shape[0]
    padded_len = templates.shape[2] + OFF
    lags = window - padded_len
    phases = PHASES
    signal = normalize_rows(data)
    n_chan = lax.axis_size("chan")
    me = lax.axis_index("chan")
    shaped = normalize_rows(templates)
    local_chan = stations % ch_local
    target = stations[:, 0] // (ch_local * n_tmpl)
    if n_chan <= 8:
        target = (me - target) % n_chan
    hit = local_chan[:, :, None] == jnp.arange(ch_local, dtype=jnp.int32)[None, None, :]
    ordered = jnp.einsum(
        "jki,jkl->jil", hit.astype(jnp.bfloat16), shaped, preferred_element_type=jnp.float32
    ).astype(jnp.bfloat16)
    ordered_shift = jnp.sum(jnp.where(hit, offsets[:, :, None], 0), axis=1)
    placed = place_moveout(ordered, ordered_shift, padded_len)
    _, span = corr_taps(padded_len, phases)
    signal = polyphase_rows(signal, phases, span + lags // phases)
    signal, placed = lax.optimization_barrier((signal, placed))
    if n_chan <= 8:
        pieces = [signal]
        for shift in range(1, n_chan):
            pairs = [(c, (c + shift) % n_chan) for c in range(n_chan)]
            pieces.append(lax.ppermute(signal, "chan", pairs))
        blocks = jnp.stack(pieces)
    else:
        blocks = lax.all_gather(signal, "chan", axis=0, tiled=False)
    n_blocks = blocks.shape[0]
    corr = correlate(placed, blocks, phases, lags)
    corr = corr.reshape(n_blocks, lags // phases, phases, count)
    pick = target[None, :] == jnp.arange(n_blocks, dtype=jnp.int32)[:, None]
    chosen = jnp.sum(jnp.where(pick[:, None, None, :], corr, 0.0), axis=0)
    partial_value = jnp.transpose(chosen, (2, 0, 1)).reshape(count, lags)
    partial_value = partial_value.astype(jnp.bfloat16)
    inverse = (
        jnp.zeros((count,), jnp.int32).at[owner_map[0]].set(jnp.arange(count, dtype=jnp.int32))
    )
    arranged = partial_value[inverse].reshape(n_tmpl, count // n_tmpl, lags)
    if n_tmpl <= 8:
        mine = lax.axis_index("tmpl")
        stack = jnp.take(arranged, mine, axis=0).astype(jnp.float32)
        for shift in range(1, n_tmpl):
            pairs = [(t, (t + shift) % n_tmpl) for t in range(n_tmpl)]
            outgoing = jnp.take(arranged, (mine + shift) % n_tmpl, axis=0)
            stack = stack + lax.ppermute(outgoing, "tmpl", pairs).astype(jnp.float32)
    else:
        received = lax.all_to_all(arranged, "tmpl", 0, 0, tiled=True)
        stack = jnp.sum(received.astype(jnp.float32), axis=0)
    power = jnp.mean(stack * stack, axis=1, keepdims=True)
    return stack * lax.rsqrt(power + eps)


def solution(mesh):
    in_specs = (
        P(("grp", "chan", "tmpl"), None),
        P(("grp", "chan"), "tmpl", None),
        P(("grp", "chan"), "tmpl"),
        P(("grp", "chan"), "tmpl"),
        P(("grp", "chan"), None),
    )
    out_specs = P(("grp", "chan", "tmpl"), None)
    return jax.shard_map(shards, mesh=mesh, in_specs=in_specs, out_specs=out_specs, check_vma=False)
```

```python
import functools

import jax
import jax.numpy as jnp
from jax import lax
from jax.experimental import pallas as pl
from jax.experimental.pallas import tpu as pltpu
from jax.sharding import PartitionSpec as P

OFF = 128
PHASES = 8


eps = 1e-05


def normalize_rows(values):
    values = values.astype(jnp.float32)
    centred = values - jnp.mean(values, axis=-1, keepdims=True)
    scale = lax.rsqrt(jnp.mean(centred * centred, axis=-1, keepdims=True) + eps)
    return (centred * scale).astype(jnp.bfloat16)


def place_moveout(rows, shifts, padded_len):
    extra = padded_len - rows.shape[-1]
    tail = jnp.zeros(rows.shape[:-1] + (extra,), rows.dtype)
    current = jnp.concatenate([rows, tail], axis=-1)
    for bit_number in range(OFF.bit_length()):
        step_len = 1 << bit_number
        lead = jnp.zeros(rows.shape[:-1] + (step_len,), rows.dtype)
        moved = jnp.concatenate([lead, current[..., : padded_len - step_len]], axis=-1)
        active = shifts >> bit_number & 1 == 1
        current = jnp.where(active[..., None], moved, current)
    return current


def _filter_kernel(grouped_ref, out_ref, *, steps, count, chans, phases):
    width = phases * chans
    first = pl.program_id(0) * steps
    for step in range(steps):
        lo = grouped_ref[first + step]
        hi = grouped_ref[first + step + 1]
        joined = jnp.concatenate([lo, hi], axis=-1)
        for e in range(phases):
            cut = (phases - 1 - e) * chans
            moved = pltpu.roll(joined, 2 * width - cut, 1) if cut else joined
            out_ref[step, e * count : (e + 1) * count, :] = moved[:, :width]


def polyphase_filters(placed, phases):
    count, chans, padded_len = placed.shape
    taps = padded_len // phases + 1
    front = phases - 1
    blocks = taps + 1
    padded = jnp.pad(placed, ((0, 0), (0, 0), (front, blocks * phases - padded_len - front)))
    grouped = jnp.transpose(padded, (0, 2, 1)).reshape(count, blocks, phases * chans)
    grouped = jnp.transpose(grouped, (1, 0, 2))
    steps = next(d for d in (9, 3, 1) if taps % d == 0)
    width = phases * chans
    kernel = functools.partial(
        _filter_kernel, steps=steps, count=count, chans=chans, phases=phases
    )
    return pl.pallas_call(
        kernel,
        grid=(taps // steps,),
        in_specs=[pl.BlockSpec((blocks, count, width), lambda q: (0, 0, 0))],
        out_specs=pl.BlockSpec((steps, phases * count, width), lambda q: (q, 0, 0)),
        out_shape=jax.ShapeDtypeStruct((taps, phases * count, width), placed.dtype),
    )(grouped)


def _corr_kernel(grouped_ref, signal_ref, out_ref, acc_ref, filt_ref, *, steps, extra_taps, count, chans, phases, rows):
    width = phases * chans
    pid = pl.program_id(0)

    @pl.when(pid == 0)
    def _():
        acc_ref[...] = jnp.zeros_like(acc_ref)

    base = pl.multiple_of(pid * steps, steps)
    for step in range(steps):
        joined = jnp.concatenate([grouped_ref[base + step], grouped_ref[base + step + 1]], axis=-1)
        joined = joined.astype(jnp.float32)
        parts = []
        for e in range(phases):
            cut = (phases - 1 - e) * chans
            moved = pltpu.roll(joined, 2 * width - cut, 1) if cut else joined
            parts.append(moved[:, :width])
        filt_ref[step] = jnp.transpose(jnp.concatenate(parts, axis=0)).astype(filt_ref.dtype)

    n_blocks = signal_ref.shape[0]
    if n_blocks <= 8:
        band = signal_ref[:, pl.ds(base, rows + steps), :]
        total = acc_ref[...]
        for step in range(steps):
            window = band[:, step : step + rows].astype(filt_ref.dtype)
            window = window.reshape(n_blocks * rows, width)
            total += jnp.dot(window, filt_ref[step], preferred_element_type=jnp.float32)
        acc_ref[...] = total
    else:

        def accumulate(g, carry):
            band = signal_ref[g, pl.ds(base, rows + steps), :]
            start = pl.multiple_of(g * rows, rows)
            total = acc_ref[pl.ds(start, rows), :]
            for step in range(steps):
                window = band[step : step + rows].astype(filt_ref.dtype)
                total += jnp.dot(window, filt_ref[step], preferred_element_type=jnp.float32)
            acc_ref[pl.ds(start, rows), :] = total
            return carry

        lax.fori_loop(0, n_blocks, accumulate, 0)

    @pl.when(pid == pl.num_programs(0) - 1)
    def _():
        for extra in range(extra_taps):
            q = (pid + 1) * steps + extra
            joined = jnp.concatenate([grouped_ref[q], grouped_ref[q + 1]], axis=-1)
            joined = joined.astype(jnp.float32)
            parts = []
            for e in range(phases):
                cut = (phases - 1 - e) * chans
                moved = pltpu.roll(joined, 2 * width - cut, 1) if cut else joined
                parts.append(moved[:, :width])
            filt = jnp.transpose(jnp.concatenate(parts, axis=0)).astype(filt_ref.dtype)
            start = pl.multiple_of((pid + 1) * steps, steps)

            def tail(g, carry):
                window = signal_ref[g, pl.ds(start, rows + steps), :][extra : extra + rows]
                lo = pl.multiple_of(g * rows, rows)
                acc_ref[pl.ds(lo, rows), :] += jnp.dot(
                    window.astype(filt.dtype), filt, preferred_element_type=jnp.float32
                )
                return carry

            lax.fori_loop(0, n_blocks, tail, 0)
        out_ref[...] = acc_ref[...].reshape(out_ref.shape)


CORR_STEPS = 40


def corr_taps(padded_len, phases):
    taps = padded_len // phases + 1
    main = taps // CORR_STEPS * CORR_STEPS
    return taps - main, main + CORR_STEPS


def polyphase_rows(signal, phases, total_rows):
    chans, window = signal.shape
    rows = jnp.transpose(signal, (1, 0)).reshape(window // phases, phases * chans)
    return jnp.pad(rows, ((0, total_rows - window // phases), (0, 0)))


def correlate(placed, signal_rows, phases, lags):
    count, chans, padded_len = placed.shape
    n_blocks = signal_rows.shape[0]
    steps = CORR_STEPS
    extra_taps, span = corr_taps(padded_len, phases)
    taps = span - steps
    front = phases - 1
    n_groups = taps + extra_taps + 1
    rows = lags // phases
    width = phases * chans
    padded = jnp.pad(placed, ((0, 0), (0, 0), (front, n_groups * phases - padded_len - front)))
    grouped = jnp.transpose(padded, (0, 2, 1)).reshape(count, n_groups, width)
    grouped = jnp.transpose(grouped, (1, 0, 2))
    signal = signal_rows.astype(jnp.float32)
    kernel = functools.partial(
        _corr_kernel, steps=steps, extra_taps=extra_taps, count=count, chans=chans,
        phases=phases, rows=rows,
    )
    return pl.pallas_call(
        kernel,
        grid=(taps // steps,),
        in_specs=[
            pl.BlockSpec(grouped.shape, lambda q: (0, 0, 0)),
            pl.BlockSpec(signal.shape, lambda q: (0, 0, 0)),
        ],
        out_specs=pl.BlockSpec((n_blocks, rows, phases * count), lambda q: (0, 0, 0)),
        out_shape=jax.ShapeDtypeStruct((n_blocks, rows, phases * count), jnp.float32),
        scratch_shapes=[
            pltpu.VMEM((n_blocks * rows, phases * count), jnp.float32),
            pltpu.VMEM((steps, phases * count, width), placed.dtype),
        ],
    )(grouped, signal)


def shards(data, templates, stations, offsets, owner_map):
    n_tmpl = lax.axis_size("tmpl")
    ch_local = data.shape[0]
    window = data.shape[1]
    count = templates.shape[0]
    padded_len = templates.shape[2] + OFF
    lags = window - padded_len
    phases = PHASES
    signal = normalize_rows(data)
    n_chan = lax.axis_size("chan")
    me = lax.axis_index("chan")
    shaped = normalize_rows(templates)
    local_chan = stations % ch_local
    target = stations[:, 0] // (ch_local * n_tmpl)
    if n_chan <= 8:
        target = (me - target) % n_chan
    hit = local_chan[:, :, None] == jnp.arange(ch_local, dtype=jnp.int32)[None, None, :]
    ordered = jnp.einsum(
        "jki,jkl->jil", hit.astype(jnp.bfloat16), shaped, preferred_element_type=jnp.float32
    ).astype(jnp.bfloat16)
    ordered_shift = jnp.sum(jnp.where(hit, offsets[:, :, None], 0), axis=1)
    placed = place_moveout(ordered, ordered_shift, padded_len)
    _, span = corr_taps(padded_len, phases)
    signal = polyphase_rows(signal, phases, span + lags // phases)
    signal, placed = lax.optimization_barrier((signal, placed))
    if n_chan <= 8:
        pieces = [signal]
        for shift in range(1, n_chan):
            pairs = [(c, (c + shift) % n_chan) for c in range(n_chan)]
            pieces.append(lax.ppermute(signal, "chan", pairs))
        blocks = jnp.stack(pieces)
    else:
        blocks = lax.all_gather(signal, "chan", axis=0, tiled=False)
    n_blocks = blocks.shape[0]
    corr = correlate(placed, blocks, phases, lags)
    corr = corr.reshape(n_blocks, lags // phases, phases, count)
    pick = target[None, :] == jnp.arange(n_blocks, dtype=jnp.int32)[:, None]
    chosen = jnp.sum(jnp.where(pick[:, None, None, :], corr, 0.0), axis=0)
    partial_value = jnp.transpose(chosen, (2, 0, 1)).reshape(count, lags)
    partial_value = partial_value.astype(jnp.bfloat16)
    inverse = (
        jnp.zeros((count,), jnp.int32).at[owner_map[0]].set(jnp.arange(count, dtype=jnp.int32))
    )
    arranged = partial_value[inverse].reshape(n_tmpl, count // n_tmpl, lags)
    if n_tmpl <= 8:
        mine = lax.axis_index("tmpl")
        stack = jnp.take(arranged, mine, axis=0).astype(jnp.float32)
        for shift in range(1, n_tmpl):
            pairs = [(t, (t + shift) % n_tmpl) for t in range(n_tmpl)]
            outgoing = jnp.take(arranged, (mine + shift) % n_tmpl, axis=0)
            stack = stack + lax.ppermute(outgoing, "tmpl", pairs).astype(jnp.float32)
    else:
        received = lax.all_to_all(arranged, "tmpl", 0, 0, tiled=True)
        stack = jnp.sum(received.astype(jnp.float32), axis=0)
    power = jnp.mean(stack * stack, axis=1, keepdims=True)
    return stack * lax.rsqrt(power + eps)


def solution(mesh):
    in_specs = (
        P(("grp", "chan", "tmpl"), None),
        P(("grp", "chan"), "tmpl", None),
        P(("grp", "chan"), "tmpl"),
        P(("grp", "chan"), "tmpl"),
        P(("grp", "chan"), None),
    )
    out_specs = P(("grp", "chan", "tmpl"), None)
    return jax.shard_map(shards, mesh=mesh, in_specs=in_specs, out_specs=out_specs, check_vma=False)
```

```python
import functools

import jax
import jax.numpy as jnp
from jax import lax
from jax.experimental import pallas as pl
from jax.experimental.pallas import tpu as pltpu
from jax.sharding import PartitionSpec as P

OFF = 128
PHASES = 8


eps = 1e-05


def normalize_rows(values):
    values = values.astype(jnp.float32)
    centred = values - jnp.mean(values, axis=-1, keepdims=True)
    scale = lax.rsqrt(jnp.mean(centred * centred, axis=-1, keepdims=True) + eps)
    return (centred * scale).astype(jnp.bfloat16)


def place_moveout(rows, shifts, padded_len):
    extra = padded_len - rows.shape[-1]
    tail = jnp.zeros(rows.shape[:-1] + (extra,), rows.dtype)
    current = jnp.concatenate([rows, tail], axis=-1)
    for bit_number in range(OFF.bit_length()):
        step_len = 1 << bit_number
        lead = jnp.zeros(rows.shape[:-1] + (step_len,), rows.dtype)
        moved = jnp.concatenate([lead, current[..., : padded_len - step_len]], axis=-1)
        active = shifts >> bit_number & 1 == 1
        current = jnp.where(active[..., None], moved, current)
    return current


def _filter_kernel(grouped_ref, out_ref, *, steps, count, chans, phases):
    width = phases * chans
    first = pl.program_id(0) * steps
    for step in range(steps):
        lo = grouped_ref[first + step]
        hi = grouped_ref[first + step + 1]
        joined = jnp.concatenate([lo, hi], axis=-1)
        for e in range(phases):
            cut = (phases - 1 - e) * chans
            moved = pltpu.roll(joined, 2 * width - cut, 1) if cut else joined
            out_ref[step, e * count : (e + 1) * count, :] = moved[:, :width]


def polyphase_filters(placed, phases):
    count, chans, padded_len = placed.shape
    taps = padded_len // phases + 1
    front = phases - 1
    blocks = taps + 1
    padded = jnp.pad(placed, ((0, 0), (0, 0), (front, blocks * phases - padded_len - front)))
    grouped = jnp.transpose(padded, (0, 2, 1)).reshape(count, blocks, phases * chans)
    grouped = jnp.transpose(grouped, (1, 0, 2))
    steps = next(d for d in (9, 3, 1) if taps % d == 0)
    width = phases * chans
    kernel = functools.partial(
        _filter_kernel, steps=steps, count=count, chans=chans, phases=phases
    )
    return pl.pallas_call(
        kernel,
        grid=(taps // steps,),
        in_specs=[pl.BlockSpec((blocks, count, width), lambda q: (0, 0, 0))],
        out_specs=pl.BlockSpec((steps, phases * count, width), lambda q: (q, 0, 0)),
        out_shape=jax.ShapeDtypeStruct((taps, phases * count, width), placed.dtype),
    )(grouped)


def _corr_kernel(grouped_ref, signal_ref, out_ref, acc_ref, filt_ref, *, steps, extra_taps, count, chans, phases, rows):
    width = phases * chans
    pid = pl.program_id(0)

    @pl.when(pid == 0)
    def _():
        acc_ref[...] = jnp.zeros_like(acc_ref)

    base = pl.multiple_of(pid * steps, steps)
    for step in range(steps):
        joined = jnp.concatenate([grouped_ref[base + step], grouped_ref[base + step + 1]], axis=-1)
        joined = joined.astype(jnp.float32)
        parts = []
        for e in range(phases):
            cut = (phases - 1 - e) * chans
            moved = pltpu.roll(joined, 2 * width - cut, 1) if cut else joined
            parts.append(moved[:, :width])
        filt_ref[step] = jnp.transpose(jnp.concatenate(parts, axis=0)).astype(filt_ref.dtype)

    n_blocks = signal_ref.shape[0]
    if n_blocks <= 8:
        band = signal_ref[:, pl.ds(base, rows + steps), :]
        total = acc_ref[...]
        for step in range(steps):
            window = band[:, step : step + rows].astype(filt_ref.dtype)
            window = window.reshape(n_blocks * rows, width)
            total += jnp.dot(window, filt_ref[step], preferred_element_type=jnp.float32)
        acc_ref[...] = total
    else:

        def accumulate(g, carry):
            band = signal_ref[g, pl.ds(base, rows + steps), :]
            start = pl.multiple_of(g * rows, rows)
            total = acc_ref[pl.ds(start, rows), :]
            for step in range(steps):
                window = band[step : step + rows].astype(filt_ref.dtype)
                total += jnp.dot(window, filt_ref[step], preferred_element_type=jnp.float32)
            acc_ref[pl.ds(start, rows), :] = total
            return carry

        lax.fori_loop(0, n_blocks, accumulate, 0)

    @pl.when(pid == pl.num_programs(0) - 1)
    def _():
        for extra in range(extra_taps):
            q = (pid + 1) * steps + extra
            joined = jnp.concatenate([grouped_ref[q], grouped_ref[q + 1]], axis=-1)
            joined = joined.astype(jnp.float32)
            parts = []
            for e in range(phases):
                cut = (phases - 1 - e) * chans
                moved = pltpu.roll(joined, 2 * width - cut, 1) if cut else joined
                parts.append(moved[:, :width])
            filt = jnp.transpose(jnp.concatenate(parts, axis=0)).astype(filt_ref.dtype)
            start = pl.multiple_of((pid + 1) * steps, steps)

            def tail(g, carry):
                window = signal_ref[g, pl.ds(start, rows + steps), :][extra : extra + rows]
                lo = pl.multiple_of(g * rows, rows)
                acc_ref[pl.ds(lo, rows), :] += jnp.dot(
                    window.astype(filt.dtype), filt, preferred_element_type=jnp.float32
                )
                return carry

            lax.fori_loop(0, n_blocks, tail, 0)
        out_ref[...] = acc_ref[...].reshape(out_ref.shape)


CORR_STEPS = 40


def corr_steps(padded_len, phases, n_blocks):
    taps = padded_len // phases + 1
    if n_blocks <= 8:
        return max(8, taps // 8 * 8)
    return CORR_STEPS


def corr_taps(padded_len, phases, steps):
    taps = padded_len // phases + 1
    main = taps // steps * steps
    return taps - main, main + steps


def polyphase_rows(signal, phases, total_rows):
    chans, window = signal.shape
    rows = jnp.transpose(signal, (1, 0)).reshape(window // phases, phases * chans)
    return jnp.pad(rows, ((0, total_rows - window // phases), (0, 0)))


def correlate(placed, signal_rows, phases, lags):
    count, chans, padded_len = placed.shape
    n_blocks = signal_rows.shape[0]
    steps = corr_steps(padded_len, phases, n_blocks)
    extra_taps, span = corr_taps(padded_len, phases, steps)
    taps = span - steps
    front = phases - 1
    n_groups = taps + extra_taps + 1
    rows = lags // phases
    width = phases * chans
    padded = jnp.pad(placed, ((0, 0), (0, 0), (front, n_groups * phases - padded_len - front)))
    grouped = jnp.transpose(padded, (0, 2, 1)).reshape(count, n_groups, width)
    grouped = jnp.transpose(grouped, (1, 0, 2))
    signal = signal_rows.astype(jnp.float32)
    kernel = functools.partial(
        _corr_kernel, steps=steps, extra_taps=extra_taps, count=count, chans=chans,
        phases=phases, rows=rows,
    )
    return pl.pallas_call(
        kernel,
        grid=(taps // steps,),
        in_specs=[
            pl.BlockSpec(grouped.shape, lambda q: (0, 0, 0)),
            pl.BlockSpec(signal.shape, lambda q: (0, 0, 0)),
        ],
        out_specs=pl.BlockSpec((n_blocks, rows, phases * count), lambda q: (0, 0, 0)),
        out_shape=jax.ShapeDtypeStruct((n_blocks, rows, phases * count), jnp.float32),
        scratch_shapes=[
            pltpu.VMEM((n_blocks * rows, phases * count), jnp.float32),
            pltpu.VMEM((steps, phases * count, width), placed.dtype),
        ],
    )(grouped, signal)


def shards(data, templates, stations, offsets, owner_map):
    n_tmpl = lax.axis_size("tmpl")
    ch_local = data.shape[0]
    window = data.shape[1]
    count = templates.shape[0]
    padded_len = templates.shape[2] + OFF
    lags = window - padded_len
    phases = PHASES
    signal = normalize_rows(data)
    n_chan = lax.axis_size("chan")
    me = lax.axis_index("chan")
    shaped = normalize_rows(templates)
    local_chan = stations % ch_local
    target = stations[:, 0] // (ch_local * n_tmpl)
    if n_chan <= 8:
        target = (me - target) % n_chan
    hit = local_chan[:, :, None] == jnp.arange(ch_local, dtype=jnp.int32)[None, None, :]
    ordered = jnp.einsum(
        "jki,jkl->jil", hit.astype(jnp.bfloat16), shaped, preferred_element_type=jnp.float32
    ).astype(jnp.bfloat16)
    ordered_shift = jnp.sum(jnp.where(hit, offsets[:, :, None], 0), axis=1)
    placed = place_moveout(ordered, ordered_shift, padded_len)
    _, span = corr_taps(padded_len, phases, corr_steps(padded_len, phases, n_chan))
    signal = polyphase_rows(signal, phases, span + lags // phases)
    signal, placed = lax.optimization_barrier((signal, placed))
    if n_chan <= 8:
        pieces = [signal]
        for shift in range(1, n_chan):
            pairs = [(c, (c + shift) % n_chan) for c in range(n_chan)]
            pieces.append(lax.ppermute(signal, "chan", pairs))
        blocks = jnp.stack(pieces)
    else:
        blocks = lax.all_gather(signal, "chan", axis=0, tiled=False)
    n_blocks = blocks.shape[0]
    corr = correlate(placed, blocks, phases, lags)
    corr = corr.reshape(n_blocks, lags // phases, phases, count)
    pick = target[None, :] == jnp.arange(n_blocks, dtype=jnp.int32)[:, None]
    chosen = jnp.sum(jnp.where(pick[:, None, None, :], corr, 0.0), axis=0)
    partial_value = jnp.transpose(chosen, (2, 0, 1)).reshape(count, lags)
    partial_value = partial_value.astype(jnp.bfloat16)
    inverse = (
        jnp.zeros((count,), jnp.int32).at[owner_map[0]].set(jnp.arange(count, dtype=jnp.int32))
    )
    arranged = partial_value[inverse].reshape(n_tmpl, count // n_tmpl, lags)
    if n_tmpl <= 8:
        mine = lax.axis_index("tmpl")
        stack = jnp.take(arranged, mine, axis=0).astype(jnp.float32)
        for shift in range(1, n_tmpl):
            pairs = [(t, (t + shift) % n_tmpl) for t in range(n_tmpl)]
            outgoing = jnp.take(arranged, (mine + shift) % n_tmpl, axis=0)
            stack = stack + lax.ppermute(outgoing, "tmpl", pairs).astype(jnp.float32)
    else:
        received = lax.all_to_all(arranged, "tmpl", 0, 0, tiled=True)
        stack = jnp.sum(received.astype(jnp.float32), axis=0)
    power = jnp.mean(stack * stack, axis=1, keepdims=True)
    return stack * lax.rsqrt(power + eps)


def solution(mesh):
    in_specs = (
        P(("grp", "chan", "tmpl"), None),
        P(("grp", "chan"), "tmpl", None),
        P(("grp", "chan"), "tmpl"),
        P(("grp", "chan"), "tmpl"),
        P(("grp", "chan"), None),
    )
    out_specs = P(("grp", "chan", "tmpl"), None)
    return jax.shard_map(shards, mesh=mesh, in_specs=in_specs, out_specs=out_specs, check_vma=False)
```

```python
import functools

import jax
import jax.numpy as jnp
from jax import lax
from jax.experimental import pallas as pl
from jax.experimental.pallas import tpu as pltpu
from jax.sharding import PartitionSpec as P

OFF = 128
PHASES = 8


eps = 1e-05


def normalize_rows(values):
    values = values.astype(jnp.float32)
    centred = values - jnp.mean(values, axis=-1, keepdims=True)
    scale = lax.rsqrt(jnp.mean(centred * centred, axis=-1, keepdims=True) + eps)
    return (centred * scale).astype(jnp.bfloat16)


def place_moveout(rows, shifts, padded_len):
    extra = padded_len - rows.shape[-1]
    tail = jnp.zeros(rows.shape[:-1] + (extra,), rows.dtype)
    current = jnp.concatenate([rows, tail], axis=-1)
    for bit_number in range(OFF.bit_length()):
        step_len = 1 << bit_number
        lead = jnp.zeros(rows.shape[:-1] + (step_len,), rows.dtype)
        moved = jnp.concatenate([lead, current[..., : padded_len - step_len]], axis=-1)
        active = shifts >> bit_number & 1 == 1
        current = jnp.where(active[..., None], moved, current)
    return current


def _filter_kernel(grouped_ref, out_ref, *, steps, count, chans, phases):
    width = phases * chans
    first = pl.program_id(0) * steps
    for step in range(steps):
        lo = grouped_ref[first + step]
        hi = grouped_ref[first + step + 1]
        joined = jnp.concatenate([lo, hi], axis=-1)
        for e in range(phases):
            cut = (phases - 1 - e) * chans
            moved = pltpu.roll(joined, 2 * width - cut, 1) if cut else joined
            out_ref[step, e * count : (e + 1) * count, :] = moved[:, :width]


def polyphase_filters(placed, phases):
    count, chans, padded_len = placed.shape
    taps = padded_len // phases + 1
    front = phases - 1
    blocks = taps + 1
    padded = jnp.pad(placed, ((0, 0), (0, 0), (front, blocks * phases - padded_len - front)))
    grouped = jnp.transpose(padded, (0, 2, 1)).reshape(count, blocks, phases * chans)
    grouped = jnp.transpose(grouped, (1, 0, 2))
    steps = next(d for d in (9, 3, 1) if taps % d == 0)
    width = phases * chans
    kernel = functools.partial(
        _filter_kernel, steps=steps, count=count, chans=chans, phases=phases
    )
    return pl.pallas_call(
        kernel,
        grid=(taps // steps,),
        in_specs=[pl.BlockSpec((blocks, count, width), lambda q: (0, 0, 0))],
        out_specs=pl.BlockSpec((steps, phases * count, width), lambda q: (q, 0, 0)),
        out_shape=jax.ShapeDtypeStruct((taps, phases * count, width), placed.dtype),
    )(grouped)


def _corr_kernel(grouped_ref, signal_ref, out_ref, acc_ref, filt_ref, *, steps, extra_taps, count, chans, phases, rows):
    width = phases * chans
    pid = pl.program_id(0)

    @pl.when(pid == 0)
    def _():
        acc_ref[...] = jnp.zeros_like(acc_ref)

    base = pl.multiple_of(pid * steps, steps)
    for step in range(steps):
        joined = jnp.concatenate([grouped_ref[base + step], grouped_ref[base + step + 1]], axis=-1)
        joined = joined.astype(jnp.float32)
        parts = []
        for e in range(phases):
            cut = (phases - 1 - e) * chans
            moved = pltpu.roll(joined, 2 * width - cut, 1) if cut else joined
            parts.append(moved[:, :width])
        filt_ref[step] = jnp.transpose(jnp.concatenate(parts, axis=0)).astype(filt_ref.dtype)

    n_blocks = signal_ref.shape[0]
    if n_blocks <= 8:
        band = signal_ref[:, pl.ds(base, rows + steps), :]
        total = acc_ref[...]
        for step in range(steps):
            window = band[:, step : step + rows].astype(filt_ref.dtype)
            window = window.reshape(n_blocks * rows, width)
            total += jnp.dot(window, filt_ref[step], preferred_element_type=jnp.float32)
        acc_ref[...] = total
    else:

        def accumulate(g, carry):
            band = signal_ref[g, pl.ds(base, rows + steps), :]
            start = pl.multiple_of(g * rows, rows)
            total = acc_ref[pl.ds(start, rows), :]
            for step in range(steps):
                window = band[step : step + rows].astype(filt_ref.dtype)
                total += jnp.dot(window, filt_ref[step], preferred_element_type=jnp.float32)
            acc_ref[pl.ds(start, rows), :] = total
            return carry

        lax.fori_loop(0, n_blocks, accumulate, 0)

    @pl.when(pid == pl.num_programs(0) - 1)
    def _():
        for extra in range(extra_taps):
            q = (pid + 1) * steps + extra
            joined = jnp.concatenate([grouped_ref[q], grouped_ref[q + 1]], axis=-1)
            joined = joined.astype(jnp.float32)
            parts = []
            for e in range(phases):
                cut = (phases - 1 - e) * chans
                moved = pltpu.roll(joined, 2 * width - cut, 1) if cut else joined
                parts.append(moved[:, :width])
            filt = jnp.transpose(jnp.concatenate(parts, axis=0)).astype(filt_ref.dtype)
            start = pl.multiple_of((pid + 1) * steps, steps)

            def tail(g, carry):
                window = signal_ref[g, pl.ds(start, rows + steps), :][extra : extra + rows]
                lo = pl.multiple_of(g * rows, rows)
                acc_ref[pl.ds(lo, rows), :] += jnp.dot(
                    window.astype(filt.dtype), filt, preferred_element_type=jnp.float32
                )
                return carry

            lax.fori_loop(0, n_blocks, tail, 0)
        out_ref[...] = acc_ref[...].reshape(out_ref.shape)


CORR_STEPS = 40


def corr_steps(padded_len, phases, n_blocks):
    taps = padded_len // phases + 1
    if n_blocks <= 8:
        return max(8, taps // 8 * 8)
    return CORR_STEPS


def corr_taps(padded_len, phases, steps):
    taps = padded_len // phases + 1
    main = taps // steps * steps
    return taps - main, main + steps


def polyphase_rows(signal, phases, total_rows):
    chans, window = signal.shape
    rows = jnp.transpose(signal, (1, 0)).reshape(window // phases, phases * chans)
    return jnp.pad(rows, ((0, total_rows - window // phases), (0, 0)))


def correlate(placed, signal_rows, phases, lags):
    count, chans, padded_len = placed.shape
    n_blocks = signal_rows.shape[0]
    steps = corr_steps(padded_len, phases, n_blocks)
    extra_taps, span = corr_taps(padded_len, phases, steps)
    taps = span - steps
    front = phases - 1
    n_groups = taps + extra_taps + 1
    rows = lags // phases
    width = phases * chans
    padded = jnp.pad(placed, ((0, 0), (0, 0), (front, n_groups * phases - padded_len - front)))
    grouped = jnp.transpose(padded, (0, 2, 1)).reshape(count, n_groups, width)
    grouped = jnp.transpose(grouped, (1, 0, 2))
    signal = signal_rows.astype(jnp.float32)
    kernel = functools.partial(
        _corr_kernel, steps=steps, extra_taps=extra_taps, count=count, chans=chans,
        phases=phases, rows=rows,
    )
    return pl.pallas_call(
        kernel,
        grid=(taps // steps,),
        in_specs=[
            pl.BlockSpec(grouped.shape, lambda q: (0, 0, 0)),
            pl.BlockSpec(signal.shape, lambda q: (0, 0, 0)),
        ],
        out_specs=pl.BlockSpec((n_blocks, rows, phases * count), lambda q: (0, 0, 0)),
        out_shape=jax.ShapeDtypeStruct((n_blocks, rows, phases * count), jnp.float32),
        scratch_shapes=[
            pltpu.VMEM((n_blocks * rows, phases * count), jnp.float32),
            pltpu.VMEM((steps, phases * count, width), placed.dtype),
        ],
    )(grouped, signal)


def shards(data, templates, stations, offsets, owner_map):
    n_tmpl = lax.axis_size("tmpl")
    ch_local = data.shape[0]
    window = data.shape[1]
    count = templates.shape[0]
    padded_len = templates.shape[2] + OFF
    lags = window - padded_len
    phases = PHASES
    signal = normalize_rows(data)
    n_chan = lax.axis_size("chan")
    me = lax.axis_index("chan")
    shaped = normalize_rows(templates)
    local_chan = stations % ch_local
    target = stations[:, 0] // (ch_local * n_tmpl)
    if n_chan <= 8:
        target = (me - target) % n_chan
    hit = local_chan[:, :, None] == jnp.arange(ch_local, dtype=jnp.int32)[None, None, :]
    ordered = jnp.einsum(
        "jki,jkl->jil", hit.astype(jnp.bfloat16), shaped, preferred_element_type=jnp.float32
    ).astype(jnp.bfloat16)
    ordered_shift = jnp.sum(jnp.where(hit, offsets[:, :, None], 0), axis=1)
    placed = place_moveout(ordered, ordered_shift, padded_len)
    _, span = corr_taps(padded_len, phases, corr_steps(padded_len, phases, n_chan))
    signal = polyphase_rows(signal, phases, span + lags // phases).astype(jnp.float32)
    signal, placed = lax.optimization_barrier((signal, placed))
    if n_chan <= 8:
        pieces = [signal]
        for shift in range(1, n_chan):
            pairs = [(c, (c + shift) % n_chan) for c in range(n_chan)]
            pieces.append(lax.ppermute(signal, "chan", pairs))
        blocks = jnp.stack(pieces)
    else:
        blocks = lax.all_gather(signal, "chan", axis=0, tiled=False)
    n_blocks = blocks.shape[0]
    corr = correlate(placed, blocks, phases, lags)
    corr = corr.reshape(n_blocks, lags // phases, phases, count)
    pick = target[None, :] == jnp.arange(n_blocks, dtype=jnp.int32)[:, None]
    chosen = jnp.sum(jnp.where(pick[:, None, None, :], corr, 0.0), axis=0)
    partial_value = jnp.transpose(chosen, (2, 0, 1)).reshape(count, lags)
    partial_value = partial_value.astype(jnp.bfloat16)
    inverse = (
        jnp.zeros((count,), jnp.int32).at[owner_map[0]].set(jnp.arange(count, dtype=jnp.int32))
    )
    arranged = partial_value[inverse].reshape(n_tmpl, count // n_tmpl, lags)
    if n_tmpl <= 8:
        mine = lax.axis_index("tmpl")
        stack = jnp.take(arranged, mine, axis=0).astype(jnp.float32)
        for shift in range(1, n_tmpl):
            pairs = [(t, (t + shift) % n_tmpl) for t in range(n_tmpl)]
            outgoing = jnp.take(arranged, (mine + shift) % n_tmpl, axis=0)
            stack = stack + lax.ppermute(outgoing, "tmpl", pairs).astype(jnp.float32)
    else:
        received = lax.all_to_all(arranged, "tmpl", 0, 0, tiled=True)
        stack = jnp.sum(received.astype(jnp.float32), axis=0)
    power = jnp.mean(stack * stack, axis=1, keepdims=True)
    return stack * lax.rsqrt(power + eps)


def solution(mesh):
    in_specs = (
        P(("grp", "chan", "tmpl"), None),
        P(("grp", "chan"), "tmpl", None),
        P(("grp", "chan"), "tmpl"),
        P(("grp", "chan"), "tmpl"),
        P(("grp", "chan"), None),
    )
    out_specs = P(("grp", "chan", "tmpl"), None)
    return jax.shard_map(shards, mesh=mesh, in_specs=in_specs, out_specs=out_specs, check_vma=False)
```

```python
import functools

import jax
import jax.numpy as jnp
from jax import lax
from jax.experimental import pallas as pl
from jax.experimental.pallas import tpu as pltpu
from jax.sharding import PartitionSpec as P

OFF = 128
PHASES = 8


eps = 1e-05


def normalize_rows(values):
    values = values.astype(jnp.float32)
    centred = values - jnp.mean(values, axis=-1, keepdims=True)
    scale = lax.rsqrt(jnp.mean(centred * centred, axis=-1, keepdims=True) + eps)
    return (centred * scale).astype(jnp.bfloat16)


def place_moveout(rows, shifts, padded_len):
    extra = padded_len - rows.shape[-1]
    tail = jnp.zeros(rows.shape[:-1] + (extra,), rows.dtype)
    current = jnp.concatenate([rows, tail], axis=-1)
    for bit_number in range(OFF.bit_length()):
        step_len = 1 << bit_number
        lead = jnp.zeros(rows.shape[:-1] + (step_len,), rows.dtype)
        moved = jnp.concatenate([lead, current[..., : padded_len - step_len]], axis=-1)
        active = shifts >> bit_number & 1 == 1
        current = jnp.where(active[..., None], moved, current)
    return current


def _filter_kernel(grouped_ref, out_ref, *, steps, count, chans, phases):
    width = phases * chans
    first = pl.program_id(0) * steps
    for step in range(steps):
        lo = grouped_ref[first + step]
        hi = grouped_ref[first + step + 1]
        joined = jnp.concatenate([lo, hi], axis=-1)
        for e in range(phases):
            cut = (phases - 1 - e) * chans
            moved = pltpu.roll(joined, 2 * width - cut, 1) if cut else joined
            out_ref[step, e * count : (e + 1) * count, :] = moved[:, :width]


def polyphase_filters(placed, phases):
    count, chans, padded_len = placed.shape
    taps = padded_len // phases + 1
    front = phases - 1
    blocks = taps + 1
    padded = jnp.pad(placed, ((0, 0), (0, 0), (front, blocks * phases - padded_len - front)))
    grouped = jnp.transpose(padded, (0, 2, 1)).reshape(count, blocks, phases * chans)
    grouped = jnp.transpose(grouped, (1, 0, 2))
    steps = next(d for d in (9, 3, 1) if taps % d == 0)
    width = phases * chans
    kernel = functools.partial(
        _filter_kernel, steps=steps, count=count, chans=chans, phases=phases
    )
    return pl.pallas_call(
        kernel,
        grid=(taps // steps,),
        in_specs=[pl.BlockSpec((blocks, count, width), lambda q: (0, 0, 0))],
        out_specs=pl.BlockSpec((steps, phases * count, width), lambda q: (q, 0, 0)),
        out_shape=jax.ShapeDtypeStruct((taps, phases * count, width), placed.dtype),
    )(grouped)


def _corr_kernel(grouped_ref, signal_ref, out_ref, acc_ref, filt_ref, *, steps, extra_taps, count, chans, phases, rows):
    width = phases * chans
    pid = pl.program_id(0)

    @pl.when(pid == 0)
    def _():
        acc_ref[...] = jnp.zeros_like(acc_ref)

    base = pl.multiple_of(pid * steps, steps)
    for step in range(steps):
        joined = jnp.concatenate([grouped_ref[base + step], grouped_ref[base + step + 1]], axis=-1)
        joined = joined.astype(jnp.float32)
        parts = []
        for e in range(phases):
            cut = (phases - 1 - e) * chans
            moved = pltpu.roll(joined, 2 * width - cut, 1) if cut else joined
            parts.append(moved[:, :width])
        filt_ref[step] = jnp.transpose(jnp.concatenate(parts, axis=0)).astype(filt_ref.dtype)

    n_blocks = signal_ref.shape[0]
    if n_blocks <= 8:
        band = signal_ref[:, pl.ds(base, rows + steps), :]
        total = acc_ref[...]
        for step in range(steps):
            window = band[:, step : step + rows].astype(filt_ref.dtype)
            window = window.reshape(n_blocks * rows, width)
            total += jnp.dot(window, filt_ref[step], preferred_element_type=jnp.float32)
        acc_ref[...] = total
    else:

        def accumulate(g, carry):
            band = signal_ref[g, pl.ds(base, rows + steps), :]
            start = pl.multiple_of(g * rows, rows)
            total = acc_ref[pl.ds(start, rows), :]
            for step in range(steps):
                window = band[step : step + rows].astype(filt_ref.dtype)
                total += jnp.dot(window, filt_ref[step], preferred_element_type=jnp.float32)
            acc_ref[pl.ds(start, rows), :] = total
            return carry

        lax.fori_loop(0, n_blocks, accumulate, 0)

    @pl.when(pid == pl.num_programs(0) - 1)
    def _():
        tail_rows = -(-extra_taps // 8) * 8
        for extra in range(extra_taps):
            q = (pid + 1) * steps + extra
            joined = jnp.concatenate([grouped_ref[q], grouped_ref[q + 1]], axis=-1)
            joined = joined.astype(jnp.float32)
            parts = []
            for e in range(phases):
                cut = (phases - 1 - e) * chans
                moved = pltpu.roll(joined, 2 * width - cut, 1) if cut else joined
                parts.append(moved[:, :width])
            filt = jnp.transpose(jnp.concatenate(parts, axis=0)).astype(filt_ref.dtype)
            start = pl.multiple_of((pid + 1) * steps, steps)

            def tail(g, carry):
                window = signal_ref[g, pl.ds(start, rows + tail_rows), :][extra : extra + rows]
                lo = pl.multiple_of(g * rows, rows)
                acc_ref[pl.ds(lo, rows), :] += jnp.dot(
                    window.astype(filt.dtype), filt, preferred_element_type=jnp.float32
                )
                return carry

            lax.fori_loop(0, n_blocks, tail, 0)
        out_ref[...] = acc_ref[...].reshape(out_ref.shape)


CORR_STEPS = 40


def corr_steps(padded_len, phases, n_blocks):
    taps = padded_len // phases + 1
    if n_blocks <= 8:
        return max(8, taps // 8 * 8)
    return CORR_STEPS


def corr_taps(padded_len, phases, steps):
    taps = padded_len // phases + 1
    main = taps // steps * steps
    return taps - main, main + steps


def polyphase_rows(signal, phases, total_rows):
    chans, window = signal.shape
    rows = jnp.transpose(signal, (1, 0)).reshape(window // phases, phases * chans)
    return jnp.pad(rows, ((0, total_rows - window // phases), (0, 0)))


def correlate(placed, signal_rows, phases, lags):
    count, chans, padded_len = placed.shape
    n_blocks = signal_rows.shape[0]
    steps = corr_steps(padded_len, phases, n_blocks)
    extra_taps, span = corr_taps(padded_len, phases, steps)
    taps = span - steps
    front = phases - 1
    n_groups = taps + extra_taps + 1
    rows = lags // phases
    width = phases * chans
    padded = jnp.pad(placed, ((0, 0), (0, 0), (front, n_groups * phases - padded_len - front)))
    grouped = jnp.transpose(padded, (0, 2, 1)).reshape(count, n_groups, width)
    grouped = jnp.transpose(grouped, (1, 0, 2))
    signal = signal_rows.astype(jnp.float32)
    kernel = functools.partial(
        _corr_kernel, steps=steps, extra_taps=extra_taps, count=count, chans=chans,
        phases=phases, rows=rows,
    )
    return pl.pallas_call(
        kernel,
        grid=(taps // steps,),
        in_specs=[
            pl.BlockSpec(grouped.shape, lambda q: (0, 0, 0)),
            pl.BlockSpec(signal.shape, lambda q: (0, 0, 0)),
        ],
        out_specs=pl.BlockSpec((n_blocks, rows, phases * count), lambda q: (0, 0, 0)),
        out_shape=jax.ShapeDtypeStruct((n_blocks, rows, phases * count), jnp.float32),
        scratch_shapes=[
            pltpu.VMEM((n_blocks * rows, phases * count), jnp.float32),
            pltpu.VMEM((steps, phases * count, width), placed.dtype),
        ],
    )(grouped, signal)


def shards(data, templates, stations, offsets, owner_map):
    n_tmpl = lax.axis_size("tmpl")
    ch_local = data.shape[0]
    window = data.shape[1]
    count = templates.shape[0]
    padded_len = templates.shape[2] + OFF
    lags = window - padded_len
    phases = PHASES
    signal = normalize_rows(data)
    n_chan = lax.axis_size("chan")
    me = lax.axis_index("chan")
    shaped = normalize_rows(templates)
    local_chan = stations % ch_local
    target = stations[:, 0] // (ch_local * n_tmpl)
    if n_chan <= 8:
        target = (me - target) % n_chan
    hit = local_chan[:, :, None] == jnp.arange(ch_local, dtype=jnp.int32)[None, None, :]
    ordered = jnp.einsum(
        "jki,jkl->jil", hit.astype(jnp.bfloat16), shaped, preferred_element_type=jnp.float32
    ).astype(jnp.bfloat16)
    ordered_shift = jnp.sum(jnp.where(hit, offsets[:, :, None], 0), axis=1)
    placed = place_moveout(ordered, ordered_shift, padded_len)
    steps = corr_steps(padded_len, phases, n_chan)
    extra, span = corr_taps(padded_len, phases, steps)
    total_rows = span - steps + lags // phases + -(-extra // 8) * 8
    signal = polyphase_rows(signal, phases, total_rows)
    signal, placed = lax.optimization_barrier((signal, placed))
    if n_chan <= 8:
        pieces = [signal]
        for shift in range(1, n_chan):
            pairs = [(c, (c + shift) % n_chan) for c in range(n_chan)]
            pieces.append(lax.ppermute(signal, "chan", pairs))
        blocks = jnp.stack(pieces)
    else:
        blocks = lax.all_gather(signal, "chan", axis=0, tiled=False)
    n_blocks = blocks.shape[0]
    corr = correlate(placed, blocks, phases, lags)
    corr = corr.reshape(n_blocks, lags // phases, phases, count)
    pick = target[None, :] == jnp.arange(n_blocks, dtype=jnp.int32)[:, None]
    chosen = jnp.sum(jnp.where(pick[:, None, None, :], corr, 0.0), axis=0)
    partial_value = jnp.transpose(chosen, (2, 0, 1)).reshape(count, lags)
    partial_value = partial_value.astype(jnp.bfloat16)
    inverse = (
        jnp.zeros((count,), jnp.int32).at[owner_map[0]].set(jnp.arange(count, dtype=jnp.int32))
    )
    arranged = partial_value[inverse].reshape(n_tmpl, count // n_tmpl, lags)
    if n_tmpl <= 8:
        mine = lax.axis_index("tmpl")
        stack = jnp.take(arranged, mine, axis=0).astype(jnp.float32)
        for shift in range(1, n_tmpl):
            pairs = [(t, (t + shift) % n_tmpl) for t in range(n_tmpl)]
            outgoing = jnp.take(arranged, (mine + shift) % n_tmpl, axis=0)
            stack = stack + lax.ppermute(outgoing, "tmpl", pairs).astype(jnp.float32)
    else:
        received = lax.all_to_all(arranged, "tmpl", 0, 0, tiled=True)
        stack = jnp.sum(received.astype(jnp.float32), axis=0)
    power = jnp.mean(stack * stack, axis=1, keepdims=True)
    return stack * lax.rsqrt(power + eps)


def solution(mesh):
    in_specs = (
        P(("grp", "chan", "tmpl"), None),
        P(("grp", "chan"), "tmpl", None),
        P(("grp", "chan"), "tmpl"),
        P(("grp", "chan"), "tmpl"),
        P(("grp", "chan"), None),
    )
    out_specs = P(("grp", "chan", "tmpl"), None)
    return jax.shard_map(shards, mesh=mesh, in_specs=in_specs, out_specs=out_specs, check_vma=False)
```

```python
import functools

import jax
import jax.numpy as jnp
from jax import lax
from jax.experimental import pallas as pl
from jax.experimental.pallas import tpu as pltpu
from jax.sharding import PartitionSpec as P

OFF = 128
PHASES = 8


eps = 1e-05


def normalize_rows(values):
    values = values.astype(jnp.float32)
    centred = values - jnp.mean(values, axis=-1, keepdims=True)
    scale = lax.rsqrt(jnp.mean(centred * centred, axis=-1, keepdims=True) + eps)
    return (centred * scale).astype(jnp.bfloat16)


def place_moveout(rows, shifts, padded_len):
    extra = padded_len - rows.shape[-1]
    tail = jnp.zeros(rows.shape[:-1] + (extra,), rows.dtype)
    current = jnp.concatenate([rows, tail], axis=-1)
    for bit_number in range(OFF.bit_length()):
        step_len = 1 << bit_number
        lead = jnp.zeros(rows.shape[:-1] + (step_len,), rows.dtype)
        moved = jnp.concatenate([lead, current[..., : padded_len - step_len]], axis=-1)
        active = shifts >> bit_number & 1 == 1
        current = jnp.where(active[..., None], moved, current)
    return current


def _filter_kernel(grouped_ref, out_ref, *, steps, count, chans, phases):
    width = phases * chans
    first = pl.program_id(0) * steps
    for step in range(steps):
        lo = grouped_ref[first + step]
        hi = grouped_ref[first + step + 1]
        joined = jnp.concatenate([lo, hi], axis=-1)
        for e in range(phases):
            cut = (phases - 1 - e) * chans
            moved = pltpu.roll(joined, 2 * width - cut, 1) if cut else joined
            out_ref[step, e * count : (e + 1) * count, :] = moved[:, :width]


def polyphase_filters(placed, phases):
    count, chans, padded_len = placed.shape
    taps = padded_len // phases + 1
    front = phases - 1
    blocks = taps + 1
    padded = jnp.pad(placed, ((0, 0), (0, 0), (front, blocks * phases - padded_len - front)))
    grouped = jnp.transpose(padded, (0, 2, 1)).reshape(count, blocks, phases * chans)
    grouped = jnp.transpose(grouped, (1, 0, 2))
    steps = next(d for d in (9, 3, 1) if taps % d == 0)
    width = phases * chans
    kernel = functools.partial(
        _filter_kernel, steps=steps, count=count, chans=chans, phases=phases
    )
    return pl.pallas_call(
        kernel,
        grid=(taps // steps,),
        in_specs=[pl.BlockSpec((blocks, count, width), lambda q: (0, 0, 0))],
        out_specs=pl.BlockSpec((steps, phases * count, width), lambda q: (q, 0, 0)),
        out_shape=jax.ShapeDtypeStruct((taps, phases * count, width), placed.dtype),
    )(grouped)


def _corr_kernel(grouped_ref, signal_ref, out_ref, acc_ref, filt_ref, *, steps, extra_taps, count, chans, phases, rows):
    width = phases * chans
    pid = pl.program_id(0)

    @pl.when(pid == 0)
    def _():
        acc_ref[...] = jnp.zeros_like(acc_ref)

    base = pl.multiple_of(pid * steps, steps)
    for step in range(steps):
        joined = jnp.concatenate([grouped_ref[base + step], grouped_ref[base + step + 1]], axis=-1)
        joined = joined.astype(jnp.float32)
        parts = []
        for e in range(phases):
            cut = (phases - 1 - e) * chans
            moved = pltpu.roll(joined, 2 * width - cut, 1) if cut else joined
            parts.append(moved[:, :width])
        filt_ref[step] = jnp.transpose(jnp.concatenate(parts, axis=0)).astype(filt_ref.dtype)

    n_blocks = signal_ref.shape[0]
    if n_blocks <= 8:
        band = signal_ref[:, pl.ds(base, rows + steps), :]
        total = acc_ref[...]
        for step in range(steps):
            window = band[:, step : step + rows].astype(filt_ref.dtype)
            window = window.reshape(n_blocks * rows, width)
            total += jnp.dot(window, filt_ref[step], preferred_element_type=jnp.float32)
        acc_ref[...] = total
    else:

        def accumulate(g, carry):
            band = signal_ref[g, pl.ds(base, rows + steps), :]
            start = pl.multiple_of(g * rows, rows)
            total = acc_ref[pl.ds(start, rows), :]
            for step in range(steps):
                window = band[step : step + rows].astype(filt_ref.dtype)
                total += jnp.dot(window, filt_ref[step], preferred_element_type=jnp.float32)
            acc_ref[pl.ds(start, rows), :] = total
            return carry

        lax.fori_loop(0, n_blocks, accumulate, 0)

    @pl.when(pid == pl.num_programs(0) - 1)
    def _():
        tail_rows = -(-extra_taps // 8) * 8
        for extra in range(extra_taps):
            q = (pid + 1) * steps + extra
            joined = jnp.concatenate([grouped_ref[q], grouped_ref[q + 1]], axis=-1)
            joined = joined.astype(jnp.float32)
            parts = []
            for e in range(phases):
                cut = (phases - 1 - e) * chans
                moved = pltpu.roll(joined, 2 * width - cut, 1) if cut else joined
                parts.append(moved[:, :width])
            filt = jnp.transpose(jnp.concatenate(parts, axis=0)).astype(filt_ref.dtype)
            start = pl.multiple_of((pid + 1) * steps, steps)

            def tail(g, carry):
                window = signal_ref[g, pl.ds(start, rows + tail_rows), :][extra : extra + rows]
                lo = pl.multiple_of(g * rows, rows)
                acc_ref[pl.ds(lo, rows), :] += jnp.dot(
                    window.astype(filt.dtype), filt, preferred_element_type=jnp.float32
                )
                return carry

            lax.fori_loop(0, n_blocks, tail, 0)
        out_ref[...] = acc_ref[...].reshape(out_ref.shape)


CORR_STEPS = 40


def corr_steps(padded_len, phases, n_blocks):
    taps = padded_len // phases + 1
    if n_blocks <= 8:
        return max(8, taps // 8 * 8)
    return CORR_STEPS


def corr_taps(padded_len, phases, steps):
    taps = padded_len // phases + 1
    main = taps // steps * steps
    return taps - main, main + steps


def polyphase_rows(signal, phases, total_rows):
    chans, window = signal.shape
    rows = jnp.transpose(signal, (1, 0)).reshape(window // phases, phases * chans)
    return jnp.pad(rows, ((0, total_rows - window // phases), (0, 0)))


def correlate(placed, signal_rows, phases, lags):
    count, chans, padded_len = placed.shape
    n_blocks = signal_rows.shape[0]
    steps = corr_steps(padded_len, phases, n_blocks)
    extra_taps, span = corr_taps(padded_len, phases, steps)
    taps = span - steps
    front = phases - 1
    n_groups = taps + extra_taps + 1
    rows = lags // phases
    width = phases * chans
    padded = jnp.pad(placed, ((0, 0), (0, 0), (front, n_groups * phases - padded_len - front)))
    grouped = jnp.transpose(padded, (0, 2, 1)).reshape(count, n_groups, width)
    grouped = jnp.transpose(grouped, (1, 0, 2))
    signal = signal_rows if n_blocks <= 8 else signal_rows.astype(jnp.float32)
    kernel = functools.partial(
        _corr_kernel, steps=steps, extra_taps=extra_taps, count=count, chans=chans,
        phases=phases, rows=rows,
    )
    return pl.pallas_call(
        kernel,
        grid=(taps // steps,),
        in_specs=[
            pl.BlockSpec(grouped.shape, lambda q: (0, 0, 0)),
            pl.BlockSpec(signal.shape, lambda q: (0, 0, 0)),
        ],
        out_specs=pl.BlockSpec((n_blocks, rows, phases * count), lambda q: (0, 0, 0)),
        out_shape=jax.ShapeDtypeStruct((n_blocks, rows, phases * count), jnp.float32),
        scratch_shapes=[
            pltpu.VMEM((n_blocks * rows, phases * count), jnp.float32),
            pltpu.VMEM((steps, phases * count, width), placed.dtype),
        ],
    )(grouped, signal)


def shards(data, templates, stations, offsets, owner_map):
    n_tmpl = lax.axis_size("tmpl")
    ch_local = data.shape[0]
    window = data.shape[1]
    count = templates.shape[0]
    padded_len = templates.shape[2] + OFF
    lags = window - padded_len
    phases = PHASES
    signal = normalize_rows(data)
    n_chan = lax.axis_size("chan")
    me = lax.axis_index("chan")
    shaped = normalize_rows(templates)
    local_chan = stations % ch_local
    target = stations[:, 0] // (ch_local * n_tmpl)
    if n_chan <= 8:
        target = (me - target) % n_chan
    hit = local_chan[:, :, None] == jnp.arange(ch_local, dtype=jnp.int32)[None, None, :]
    ordered = jnp.einsum(
        "jki,jkl->jil", hit.astype(jnp.bfloat16), shaped, preferred_element_type=jnp.float32
    ).astype(jnp.bfloat16)
    ordered_shift = jnp.sum(jnp.where(hit, offsets[:, :, None], 0), axis=1)
    placed = place_moveout(ordered, ordered_shift, padded_len)
    steps = corr_steps(padded_len, phases, n_chan)
    extra, span = corr_taps(padded_len, phases, steps)
    total_rows = span - steps + lags // phases + -(-extra // 8) * 8
    signal = polyphase_rows(signal, phases, total_rows)
    signal, placed = lax.optimization_barrier((signal, placed))
    if n_chan <= 8:
        pieces = [signal]
        for shift in range(1, n_chan):
            pairs = [(c, (c + shift) % n_chan) for c in range(n_chan)]
            pieces.append(lax.ppermute(signal, "chan", pairs))
        blocks = jnp.stack(pieces)
    else:
        blocks = lax.all_gather(signal, "chan", axis=0, tiled=False)
    n_blocks = blocks.shape[0]
    corr = correlate(placed, blocks, phases, lags)
    corr = corr.reshape(n_blocks, lags // phases, phases, count)
    pick = target[None, :] == jnp.arange(n_blocks, dtype=jnp.int32)[:, None]
    chosen = jnp.sum(jnp.where(pick[:, None, None, :], corr, 0.0), axis=0)
    partial_value = jnp.transpose(chosen, (2, 0, 1)).reshape(count, lags)
    partial_value = partial_value.astype(jnp.bfloat16)
    inverse = (
        jnp.zeros((count,), jnp.int32).at[owner_map[0]].set(jnp.arange(count, dtype=jnp.int32))
    )
    arranged = partial_value[inverse].reshape(n_tmpl, count // n_tmpl, lags)
    if n_tmpl <= 8:
        mine = lax.axis_index("tmpl")
        stack = jnp.take(arranged, mine, axis=0).astype(jnp.float32)
        for shift in range(1, n_tmpl):
            pairs = [(t, (t + shift) % n_tmpl) for t in range(n_tmpl)]
            outgoing = jnp.take(arranged, (mine + shift) % n_tmpl, axis=0)
            stack = stack + lax.ppermute(outgoing, "tmpl", pairs).astype(jnp.float32)
    else:
        received = lax.all_to_all(arranged, "tmpl", 0, 0, tiled=True)
        stack = jnp.sum(received.astype(jnp.float32), axis=0)
    power = jnp.mean(stack * stack, axis=1, keepdims=True)
    return stack * lax.rsqrt(power + eps)


def solution(mesh):
    in_specs = (
        P(("grp", "chan", "tmpl"), None),
        P(("grp", "chan"), "tmpl", None),
        P(("grp", "chan"), "tmpl"),
        P(("grp", "chan"), "tmpl"),
        P(("grp", "chan"), None),
    )
    out_specs = P(("grp", "chan", "tmpl"), None)
    return jax.shard_map(shards, mesh=mesh, in_specs=in_specs, out_specs=out_specs, check_vma=False)
```

```python
import functools

import jax
import jax.numpy as jnp
from jax import lax
from jax.experimental import pallas as pl
from jax.experimental.pallas import tpu as pltpu
from jax.sharding import PartitionSpec as P

OFF = 128
PHASES = 8


eps = 1e-05


def normalize_rows(values):
    values = values.astype(jnp.float32)
    centred = values - jnp.mean(values, axis=-1, keepdims=True)
    scale = lax.rsqrt(jnp.mean(centred * centred, axis=-1, keepdims=True) + eps)
    return (centred * scale).astype(jnp.bfloat16)


def place_moveout(rows, shifts, padded_len):
    extra = padded_len - rows.shape[-1]
    tail = jnp.zeros(rows.shape[:-1] + (extra,), rows.dtype)
    current = jnp.concatenate([rows, tail], axis=-1)
    for bit_number in range(OFF.bit_length()):
        step_len = 1 << bit_number
        lead = jnp.zeros(rows.shape[:-1] + (step_len,), rows.dtype)
        moved = jnp.concatenate([lead, current[..., : padded_len - step_len]], axis=-1)
        active = shifts >> bit_number & 1 == 1
        current = jnp.where(active[..., None], moved, current)
    return current


def _filter_kernel(grouped_ref, out_ref, *, steps, count, chans, phases):
    width = phases * chans
    first = pl.program_id(0) * steps
    for step in range(steps):
        lo = grouped_ref[first + step]
        hi = grouped_ref[first + step + 1]
        joined = jnp.concatenate([lo, hi], axis=-1)
        for e in range(phases):
            cut = (phases - 1 - e) * chans
            moved = pltpu.roll(joined, 2 * width - cut, 1) if cut else joined
            out_ref[step, e * count : (e + 1) * count, :] = moved[:, :width]


def polyphase_filters(placed, phases):
    count, chans, padded_len = placed.shape
    taps = padded_len // phases + 1
    front = phases - 1
    blocks = taps + 1
    padded = jnp.pad(placed, ((0, 0), (0, 0), (front, blocks * phases - padded_len - front)))
    grouped = jnp.transpose(padded, (0, 2, 1)).reshape(count, blocks, phases * chans)
    grouped = jnp.transpose(grouped, (1, 0, 2))
    steps = next(d for d in (9, 3, 1) if taps % d == 0)
    width = phases * chans
    kernel = functools.partial(
        _filter_kernel, steps=steps, count=count, chans=chans, phases=phases
    )
    return pl.pallas_call(
        kernel,
        grid=(taps // steps,),
        in_specs=[pl.BlockSpec((blocks, count, width), lambda q: (0, 0, 0))],
        out_specs=pl.BlockSpec((steps, phases * count, width), lambda q: (q, 0, 0)),
        out_shape=jax.ShapeDtypeStruct((taps, phases * count, width), placed.dtype),
    )(grouped)


def _corr_kernel(grouped_ref, signal_ref, out_ref, acc_ref, filt_ref, *, steps, extra_taps, count, chans, phases, rows):
    width = phases * chans
    pid = pl.program_id(0)

    @pl.when(pid == 0)
    def _():
        acc_ref[...] = jnp.zeros_like(acc_ref)

    base = pl.multiple_of(pid * steps, steps)
    for step in range(steps):
        joined = jnp.concatenate([grouped_ref[base + step], grouped_ref[base + step + 1]], axis=-1)
        parts = []
        for e in range(phases):
            cut = (phases - 1 - e) * chans
            moved = pltpu.roll(joined, 2 * width - cut, 1) if cut else joined
            parts.append(moved[:, :width])
        slab = jnp.concatenate(parts, axis=0).astype(jnp.float32)
        filt_ref[step] = jnp.transpose(slab).astype(filt_ref.dtype)

    n_blocks = signal_ref.shape[0]
    if n_blocks <= 8:
        band = signal_ref[:, pl.ds(base, rows + steps), :]
        total = acc_ref[...]
        for step in range(steps):
            window = band[:, step : step + rows].astype(filt_ref.dtype)
            window = window.reshape(n_blocks * rows, width)
            total += jnp.dot(window, filt_ref[step], preferred_element_type=jnp.float32)
        acc_ref[...] = total
    else:

        def accumulate(g, carry):
            band = signal_ref[g, pl.ds(base, rows + steps), :]
            start = pl.multiple_of(g * rows, rows)
            total = acc_ref[pl.ds(start, rows), :]
            for step in range(steps):
                window = band[step : step + rows].astype(filt_ref.dtype)
                total += jnp.dot(window, filt_ref[step], preferred_element_type=jnp.float32)
            acc_ref[pl.ds(start, rows), :] = total
            return carry

        lax.fori_loop(0, n_blocks, accumulate, 0)

    @pl.when(pid == pl.num_programs(0) - 1)
    def _():
        tail_rows = -(-extra_taps // 8) * 8
        for extra in range(extra_taps):
            q = (pid + 1) * steps + extra
            joined = jnp.concatenate([grouped_ref[q], grouped_ref[q + 1]], axis=-1)
            joined = joined.astype(jnp.float32)
            parts = []
            for e in range(phases):
                cut = (phases - 1 - e) * chans
                moved = pltpu.roll(joined, 2 * width - cut, 1) if cut else joined
                parts.append(moved[:, :width])
            filt = jnp.transpose(jnp.concatenate(parts, axis=0)).astype(filt_ref.dtype)
            start = pl.multiple_of((pid + 1) * steps, steps)

            def tail(g, carry):
                window = signal_ref[g, pl.ds(start, rows + tail_rows), :][extra : extra + rows]
                lo = pl.multiple_of(g * rows, rows)
                acc_ref[pl.ds(lo, rows), :] += jnp.dot(
                    window.astype(filt.dtype), filt, preferred_element_type=jnp.float32
                )
                return carry

            lax.fori_loop(0, n_blocks, tail, 0)
        out_ref[...] = acc_ref[...].reshape(out_ref.shape)


CORR_STEPS = 40


def corr_steps(padded_len, phases, n_blocks):
    taps = padded_len // phases + 1
    if n_blocks <= 8:
        return max(8, taps // 8 * 8)
    return CORR_STEPS


def corr_taps(padded_len, phases, steps):
    taps = padded_len // phases + 1
    main = taps // steps * steps
    return taps - main, main + steps


def polyphase_rows(signal, phases, total_rows):
    chans, window = signal.shape
    rows = jnp.transpose(signal, (1, 0)).reshape(window // phases, phases * chans)
    return jnp.pad(rows, ((0, total_rows - window // phases), (0, 0)))


def correlate(placed, signal_rows, phases, lags):
    count, chans, padded_len = placed.shape
    n_blocks = signal_rows.shape[0]
    steps = corr_steps(padded_len, phases, n_blocks)
    extra_taps, span = corr_taps(padded_len, phases, steps)
    taps = span - steps
    front = phases - 1
    n_groups = taps + extra_taps + 1
    rows = lags // phases
    width = phases * chans
    padded = jnp.pad(placed, ((0, 0), (0, 0), (front, n_groups * phases - padded_len - front)))
    grouped = jnp.transpose(padded, (0, 2, 1)).reshape(count, n_groups, width)
    grouped = jnp.transpose(grouped, (1, 0, 2))
    signal = signal_rows if n_blocks <= 8 else signal_rows.astype(jnp.float32)
    kernel = functools.partial(
        _corr_kernel, steps=steps, extra_taps=extra_taps, count=count, chans=chans,
        phases=phases, rows=rows,
    )
    return pl.pallas_call(
        kernel,
        grid=(taps // steps,),
        in_specs=[
            pl.BlockSpec(grouped.shape, lambda q: (0, 0, 0)),
            pl.BlockSpec(signal.shape, lambda q: (0, 0, 0)),
        ],
        out_specs=pl.BlockSpec((n_blocks, rows, phases * count), lambda q: (0, 0, 0)),
        out_shape=jax.ShapeDtypeStruct((n_blocks, rows, phases * count), jnp.float32),
        scratch_shapes=[
            pltpu.VMEM((n_blocks * rows, phases * count), jnp.float32),
            pltpu.VMEM((steps, phases * count, width), placed.dtype),
        ],
    )(grouped, signal)


def shards(data, templates, stations, offsets, owner_map):
    n_tmpl = lax.axis_size("tmpl")
    ch_local = data.shape[0]
    window = data.shape[1]
    count = templates.shape[0]
    padded_len = templates.shape[2] + OFF
    lags = window - padded_len
    phases = PHASES
    signal = normalize_rows(data)
    n_chan = lax.axis_size("chan")
    me = lax.axis_index("chan")
    shaped = normalize_rows(templates)
    local_chan = stations % ch_local
    target = stations[:, 0] // (ch_local * n_tmpl)
    if n_chan <= 8:
        target = (me - target) % n_chan
    hit = local_chan[:, :, None] == jnp.arange(ch_local, dtype=jnp.int32)[None, None, :]
    ordered = jnp.einsum(
        "jki,jkl->jil", hit.astype(jnp.bfloat16), shaped, preferred_element_type=jnp.float32
    ).astype(jnp.bfloat16)
    ordered_shift = jnp.sum(jnp.where(hit, offsets[:, :, None], 0), axis=1)
    placed = place_moveout(ordered, ordered_shift, padded_len)
    steps = corr_steps(padded_len, phases, n_chan)
    extra, span = corr_taps(padded_len, phases, steps)
    total_rows = span - steps + lags // phases + -(-extra // 8) * 8
    signal = polyphase_rows(signal, phases, total_rows)
    signal, placed = lax.optimization_barrier((signal, placed))
    if n_chan <= 8:
        pieces = [signal]
        for shift in range(1, n_chan):
            pairs = [(c, (c + shift) % n_chan) for c in range(n_chan)]
            pieces.append(lax.ppermute(signal, "chan", pairs))
        blocks = jnp.stack(pieces)
    else:
        blocks = lax.all_gather(signal, "chan", axis=0, tiled=False)
    n_blocks = blocks.shape[0]
    corr = correlate(placed, blocks, phases, lags)
    corr = corr.reshape(n_blocks, lags // phases, phases, count)
    pick = target[None, :] == jnp.arange(n_blocks, dtype=jnp.int32)[:, None]
    chosen = jnp.sum(jnp.where(pick[:, None, None, :], corr, 0.0), axis=0)
    partial_value = jnp.transpose(chosen, (2, 0, 1)).reshape(count, lags)
    partial_value = partial_value.astype(jnp.bfloat16)
    inverse = (
        jnp.zeros((count,), jnp.int32).at[owner_map[0]].set(jnp.arange(count, dtype=jnp.int32))
    )
    arranged = partial_value[inverse].reshape(n_tmpl, count // n_tmpl, lags)
    if n_tmpl <= 8:
        mine = lax.axis_index("tmpl")
        stack = jnp.take(arranged, mine, axis=0).astype(jnp.float32)
        for shift in range(1, n_tmpl):
            pairs = [(t, (t + shift) % n_tmpl) for t in range(n_tmpl)]
            outgoing = jnp.take(arranged, (mine + shift) % n_tmpl, axis=0)
            stack = stack + lax.ppermute(outgoing, "tmpl", pairs).astype(jnp.float32)
    else:
        received = lax.all_to_all(arranged, "tmpl", 0, 0, tiled=True)
        stack = jnp.sum(received.astype(jnp.float32), axis=0)
    power = jnp.mean(stack * stack, axis=1, keepdims=True)
    return stack * lax.rsqrt(power + eps)


def solution(mesh):
    in_specs = (
        P(("grp", "chan", "tmpl"), None),
        P(("grp", "chan"), "tmpl", None),
        P(("grp", "chan"), "tmpl"),
        P(("grp", "chan"), "tmpl"),
        P(("grp", "chan"), None),
    )
    out_specs = P(("grp", "chan", "tmpl"), None)
    return jax.shard_map(shards, mesh=mesh, in_specs=in_specs, out_specs=out_specs, check_vma=False)
```
